256 devices in a mesh: chan: 64 (over x, z, core), tm: 4 (over y).
Axes of the slice: x: 4, y: 4, z: 8, core: 2. Of those that a mesh axis runs over, the one named last changes fastest.
Arguments:
- recorded: bfloat16 [8192, 512], P(('tm', 'chan')), may hold values from -6 to 6
- partners: int32 [64], replicated, may hold values from 0 to 63, as said below
- offsets: int32 [64], P('chan'), may hold values from 3 to 4
- first_weight: bfloat16 [16, 1, 7, 7], replicated, may hold values from -1.25 to 1.25
- first_bias: float32 [16], replicated, may hold values from -3 to 3
- second_weight: bfloat16 [32, 16, 7, 7], replicated, may hold values from -0.3125 to 0.3125
- second_bias: float32 [32], replicated, may hold values from -3 to 3
- loop_weight: bfloat16 [7, 32, 32], replicated, may hold values from -1 to 1
- third_weight: bfloat16 [32, 32, 7, 7], replicated, may hold values from -0.21875 to 0.21875
- third_bias: float32 [32], replicated, may hold values from -3 to 3
- fourth_weight: bfloat16 [64, 32, 7, 7], replicated, may hold values from -0.21875 to 0.21875
- fourth_bias: float32 [64], replicated, may hold values from -3 to 3
Outputs:
- features: bfloat16 [64, 512, 512], P(None, 'chan', 'tm')
The draws below stay inside these ranges and needn't reach their ends.
Inputs may be any that keep to these rules, and one draw needn't show every extreme that they name: partners pairs the 64 blocks: partners[partners[b]] = b and partners[b] != b for every block b.
All inputs are finite; a program needn't handle non-finite values.
Results may differ from the reference program's by a relative error of at most 0.014.
Values may be sent and summed in bfloat16 or wider, within the bound.
No kernel may reach another device: no remote copies, remote signals or barrier semaphores. Data moves between devices by JAX's collectives and lax.ppermute only.
A program may use at most 64 MiB of HBM per device.

```python
import jax
import jax.numpy as jnp
from jax import lax

C_DEV = 8
K = 7
F1 = 16
F2 = 32
F3 = 64
BLOCKS = 64
NC = 512
NT = 8192


def draw_partners(key, part):
    order = jax.random.permutation(key, BLOCKS).astype(jnp.int32)
    mates = order.reshape(BLOCKS // 2, 2)[:, ::-1].reshape(BLOCKS)
    return jnp.zeros((BLOCKS,), jnp.int32).at[order].set(mates)


def with_ends(entries, own_key, low, top_value):
    longest = entries.shape.index(max(entries.shape))
    spots = []
    for shift in (0, 1):
        where = [jax.random.randint(jax.random.fold_in(own_key, axis), (), 0, length) for axis, length in enumerate(entries.shape)]
        where[longest] = (where[longest] + shift) % entries.shape[longest]
        spots.append(tuple(where))
    return entries.at[spots[0]].set(low).at[spots[1]].set(top_value)


def level_of(key, shape, cuts, low, high):
    loudness = 1.0
    for dim, blocks in cuts:
        steps = jax.random.uniform(jax.random.fold_in(jax.random.fold_in(key, 6), dim), (blocks,), jnp.float32, low / len(cuts), high / len(cuts))
        loudness = loudness * jnp.repeat(jnp.exp(steps), shape[dim] // blocks).reshape((-1,) + (1,) * (len(shape) - 1 - dim))
    return loudness


def normal_values(rng, extent, spread, reach, pieces=(), held_as=jnp.bfloat16):
    values = jax.random.normal(rng, extent, jnp.float32) * spread
    if len(pieces) > 0:
        values = level_of(rng, extent, pieces, -0.22, 0.18) * values
    return jnp.clip(values, min=-reach, max=reach).astype(held_as)


def setup_inputs(seed: int = 0) -> dict:
    arg_keys = jax.random.split(jax.random.key(seed), 13)
    recorded = normal_values(arg_keys[0], (NT, NC), 1.0, 6.0, ((0, 256),))
    partners = draw_partners(jax.random.fold_in(arg_keys[12], 71), 0)
    offsets = with_ends(jax.random.randint(arg_keys[2], (BLOCKS,), 3, C_DEV - 3), jax.random.fold_in(arg_keys[2], 1), 3, (C_DEV - 3) - 1).astype(jnp.int32)
    first_weight = normal_values(arg_keys[3], (F1, 1, K, K), (K * K // 2) ** -0.5, 1.25)
    first_bias = normal_values(arg_keys[4], (F1,), 0.5, 3.0, (), jnp.float32)
    second_weight = normal_values(arg_keys[5], (F2, F1, K, K), (F1 * K * K // 2) ** -0.5, 0.3125)
    second_bias = normal_values(arg_keys[6], (F2,), 0.5, 3.0, (), jnp.float32)
    loop_weight = normal_values(arg_keys[7], (K, F2, F2), F2 ** -0.5, 1.0)
    third_weight = normal_values(arg_keys[8], (F2, F2, K, K), (F2 * K * K // 2) ** -0.5, 0.21875)
    third_bias = normal_values(arg_keys[9], (F2,), 0.5, 3.0, (), jnp.float32)
    fourth_weight = normal_values(arg_keys[10], (F3, F2, K, K), (F2 * K * K // 2) ** -0.5, 0.21875)
    fourth_bias = normal_values(arg_keys[11], (F3,), 0.5, 3.0, (), jnp.float32)
    return {"recorded": recorded, "partners": partners, "offsets": offsets, "first_weight": first_weight, "first_bias": first_bias, "second_weight": second_weight, "second_bias": second_bias, "loop_weight": loop_weight, "third_weight": third_weight, "third_bias": third_bias, "fourth_weight": fourth_weight, "fourth_bias": fourth_bias}


def conv_layer(values, weight, stride, finish):
    fin, total_rows, length = values.shape
    if stride == 1:
        low_pad, high_pad = 3, 3
    else:
        low_pad, high_pad = 2, 1
    padded = jnp.pad(values, ((0, 0), (3, 3), (low_pad, high_pad)))
    count = total_rows // C_DEV

    def one_block(block):
        piece = lax.dynamic_slice_in_dim(padded, (block * C_DEV).astype(jnp.int32), C_DEV + 6, axis=1)
        result = lax.conv_general_dilated(piece[None], weight, (1, stride), "VALID", dimension_numbers=("NCHW", "OIHW", "NCHW"), preferred_element_type=jnp.float32)[0]
        return finish(result)

    stacked = lax.map(one_block, jnp.arange(count, dtype=jnp.int32))
    return jnp.transpose(stacked, (1, 0, 2, 3)).reshape(stacked.shape[1], total_rows, stacked.shape[3])


def activate(bias):
    def finish(result):
        return jnp.maximum(result + bias[:, None, None], 0.0).astype(jnp.bfloat16)
    return finish


def reference(recorded, partners, offsets, first_weight, first_bias, second_weight, second_bias, loop_weight, third_weight, third_bias, fourth_weight, fourth_bias):
    strain = jnp.transpose(recorded)[None]
    first = conv_layer(strain, first_weight, 1, activate(first_bias))

    def biased(result):
        return (result + second_bias[:, None, None]).astype(jnp.bfloat16)

    pre_second = conv_layer(first, second_weight, 4, biased)
    blocks = jnp.arange(BLOCKS, dtype=jnp.int32)
    taps = jnp.arange(7, dtype=jnp.int32)
    target = blocks[:, None] * C_DEV + offsets[:, None] + taps[None, :] - 3
    source = partners[:, None] * C_DEV + offsets[partners][:, None] + 3 - taps[None, :]
    quarter = pre_second.shape[2]
    gathered = pre_second[:, source.reshape(-1).astype(jnp.int32), :].reshape(F2, BLOCKS, 7, quarter).astype(jnp.float32)
    coupling = jnp.einsum("kof,fbkt->obkt", loop_weight.astype(jnp.float32), gathered)
    summed = pre_second.astype(jnp.float32).at[:, target.reshape(-1).astype(jnp.int32), :].add(coupling.reshape(F2, BLOCKS * 7, quarter))
    second = jnp.maximum(summed, 0.0).astype(jnp.bfloat16)
    third = conv_layer(second, third_weight, 1, activate(third_bias))
    return conv_layer(third, fourth_weight, 4, activate(fourth_bias))
```

```python
import jax
import jax.numpy as jnp
from jax import lax
from jax.sharding import PartitionSpec as P

F2 = 32
C_DEV = 8
REACH = 6
LEFT = 25
RIGHT = 24
LEAD = 5


def conv_valid(values, weight, stride):
    return lax.conv_general_dilated(
        values[None],
        weight,
        (1, stride),
        "VALID",
        dimension_numbers=("NCHW", "OIHW", "NCHW"),
        preferred_element_type=jnp.float32,
    )[0]


def edge_mask(rows, length, row0, col0, span):
    c = lax.axis_index("chan")
    t = lax.axis_index("tm")
    total_rows = lax.axis_size("chan") * C_DEV
    last = lax.axis_size("tm") - 1
    row = c * C_DEV + row0 + lax.broadcasted_iota(jnp.int32, (rows, length), 0)
    col = col0 + lax.broadcasted_iota(jnp.int32, (rows, length), 1)
    ok = (row >= 0) & (row < total_rows)
    ok = ok & ((t > 0) | (col >= 0)) & ((t < last) | (col < span))
    return ok[None]


def activate(values, bias, mask):
    return jnp.where(mask, jnp.maximum(values + bias[:, None, None], 0.0), 0.0).astype(jnp.bfloat16)


def on_device(
    recorded,
    partners,
    offsets,
    first_weight,
    first_bias,
    second_weight,
    second_bias,
    loop_weight,
    third_weight,
    third_bias,
    fourth_weight,
    fourth_bias,
):
    blocks = lax.axis_size("chan")
    times_here, nc = recorded.shape
    wide = C_DEV + 2 * REACH
    padded = jnp.pad(recorded, ((0, 0), (REACH, 3 * C_DEV - REACH)))
    windows = jnp.concatenate(
        [padded[:, k * C_DEV : k * C_DEV + nc].reshape(times_here, blocks, C_DEV) for k in range(3)], axis=2
    )[:, :, :wide]
    outgoing = jnp.transpose(windows, (1, 0, 2))
    arrived = lax.all_to_all(outgoing, "chan", split_axis=0, concat_axis=0, tiled=True)
    times = blocks * times_here
    strain = jnp.transpose(arrived.reshape(times, wide))
    tms = lax.axis_size("tm")
    up = [(i, i + 1) for i in range(tms - 1)]
    down = [(j, i) for i, j in up]
    before = lax.ppermute(strain[:, times - LEFT :], "tm", up)
    after = lax.ppermute(strain[:, :RIGHT], "tm", down)
    strain_wide = jnp.concatenate([before, strain, after], axis=1)

    first_pre = conv_valid(strain_wide[None], first_weight, 1)
    first = activate(first_pre, first_bias, edge_mask(wide - 6, first_pre.shape[2], 3 - REACH, 3 - LEFT, times))

    quarter = times // 4
    length = quarter + 2 * LEAD
    start = (3 - LEFT) + 4 * LEAD + 2
    first_cut = first[:, :, -start : -start + 4 * (length - 1) + 7]
    pre_second = (conv_valid(first_cut, second_weight, 4) + second_bias[:, None, None]).astype(jnp.bfloat16)

    own_offset = offsets[0]
    crossing = lax.dynamic_slice(pre_second, (0, own_offset - 3, 0), (F2, 7, length))
    packed = crossing.reshape(blocks, 1, -1)
    moved = jnp.take(
        lax.all_to_all(packed, "chan", split_axis=0, concat_axis=1, tiled=True), partners, axis=1
    )
    came = lax.all_to_all(moved, "chan", split_axis=1, concat_axis=0, tiled=True).reshape(F2, 7, length)
    flipped = came[:, ::-1, :]
    coupling = jnp.einsum("kof,fkt->okt", loop_weight, flipped, preferred_element_type=jnp.float32)
    extra = lax.dynamic_update_slice(
        jnp.zeros((F2, C_DEV, length), jnp.float32), coupling, (0, own_offset - 3, 0)
    )
    second_mask = edge_mask(C_DEV, length, 0, -LEAD, quarter)
    second = jnp.where(second_mask, jnp.maximum(pre_second.astype(jnp.float32) + extra, 0.0), 0.0).astype(
        jnp.bfloat16
    )

    ring_up = [(i, i + 1) for i in range(blocks - 1)]
    ring_down = [(j, i) for i, j in ring_up]
    above = lax.ppermute(second[:, C_DEV - REACH :, :], "chan", ring_up)
    below = lax.ppermute(second[:, :REACH, :], "chan", ring_down)
    second_wide = jnp.concatenate([above, second, below], axis=1)

    third_pre = conv_valid(second_wide, third_weight, 1)
    third = activate(third_pre, third_bias, edge_mask(wide - 6, third_pre.shape[2], 3 - REACH, 3 - LEAD, quarter))
    cut = 4 * (quarter // 4 - 1) + 7
    third_cut = third[:, :, LEAD - 5 : LEAD - 5 + cut]
    return activate(conv_valid(third_cut, fourth_weight, 4), fourth_bias, True)


def solution(mesh):
    return jax.shard_map(
        on_device,
        mesh=mesh,
        in_specs=(
            P(("tm", "chan"), None),
            P(),
            P("chan"),
            P(),
            P(),
            P(),
            P(),
            P(),
            P(),
            P(),
            P(),
            P(),
        ),
        out_specs=P(None, "chan", "tm"),
        check_vma=False,
    )
```

```python
import numpy as np
import jax
import jax.numpy as jnp
from jax import lax
from jax.experimental import pallas as pl
from jax.sharding import PartitionSpec as P

F2 = 32
C_DEV = 8
REACH = 6
PH = 4
WL = 7
WR = 8
LEAD = 5
LANE_BLOCK = 256


def banded(x, w_all, bias, mask, *, groups, shifts, n_out, relu, select=None, n_sel=0):
    flat = x.ndim == 2
    k_all = w_all.shape[1]
    row_step = k_all // 7
    r_out = (x.shape[0] // row_step if flat else x.shape[0]) - 6
    n_in = x.shape[-1]
    fout = w_all.shape[0] // (groups * shifts)
    if select is None:
        out_shape = (r_out, groups * fout, n_out)
    else:
        out_shape = (r_out, PH * fout, n_sel)

    def kernel(x_ref, w_ref, b_ref, m_ref, *rest):
        if select is None:
            (o_ref,) = rest
        else:
            s_ref, o_ref = rest

        def row(r, carry):
            if flat:
                xs = x_ref[r * row_step : r * row_step + k_all, :]
            else:
                xs = x_ref[pl.ds(r, 7), :, :].reshape(k_all, n_in)
            z = jnp.dot(w_ref[...], xs, preferred_element_type=jnp.float32)
            m_row = m_ref[r]
            for g in range(groups):
                base = g * shifts * fout
                acc = z[base : base + fout, 0:n_out]
                for s in range(1, shifts):
                    acc = acc + z[base + s * fout : base + (s + 1) * fout, s : s + n_out]
                acc = acc + b_ref[...]
                if relu:
                    acc = jnp.maximum(acc, 0.0)
                acc = (acc * m_row[g : g + 1, :]).astype(jnp.bfloat16)
                if select is None:
                    o_ref[r, g * fout : (g + 1) * fout, :] = acc
                else:
                    y = jnp.dot(acc, s_ref[...], preferred_element_type=jnp.float32)
                    for p in range(PH):
                        o_ref[r, p * fout : (p + 1) * fout, :] = y[
                            :, p * LANE_BLOCK : p * LANE_BLOCK + n_sel
                        ].astype(jnp.bfloat16)
            return carry

        if flat:
            for r in range(r_out):
                row(r, 0)
        else:
            lax.fori_loop(0, r_out, row, 0)

    args = [x, w_all, bias.reshape(fout, 1).astype(jnp.float32), mask]
    if select is not None:
        args.append(select)
    return pl.pallas_call(kernel, out_shape=jax.ShapeDtypeStruct(out_shape, jnp.bfloat16))(*args)


def weights_stride1(w):
    fout, fin = w.shape[:2]
    return jnp.transpose(w, (3, 0, 2, 1)).reshape(7 * fout, 7 * fin)


def weights_stride4(w, shifts, lag):
    fout, fin = w.shape[:2]
    s = np.arange(shifts)[:, None]
    p = np.arange(PH)[None, :]
    b = 4 * s + p - lag
    ok = (b >= 0) & (b <= 6)
    taps = jnp.take(w, np.clip(b, 0, 6).reshape(-1), axis=3).reshape(fout, fin, 7, shifts, PH)
    taps = jnp.where(ok[None, None, None], taps, jnp.zeros((), w.dtype))
    return jnp.transpose(taps, (3, 0, 2, 4, 1)).reshape(shifts * fout, 7 * PH * fin)


def weights_first(w):
    fout = w.shape[0]
    p = np.arange(PH)[:, None, None]
    dd = np.arange(4)[None, :, None]
    q = np.arange(PH)[None, None, :]
    b = 4 * (dd - 1) + q - p + 3
    ok = (b >= 0) & (b <= 6)
    taps = jnp.take(w[:, 0], np.clip(b, 0, 6).reshape(-1), axis=2).reshape(fout, 7, PH, 4, PH)
    taps = jnp.where(ok[None, None], taps, jnp.zeros((), w.dtype))
    return jnp.transpose(taps, (2, 3, 0, 1, 4)).reshape(PH * 4 * fout, 7 * PH)


def phase_select(n_in, n_sel):
    sel = np.zeros((n_in, PH * LANE_BLOCK), np.float32)
    for p in range(PH):
        for u in range(n_sel):
            if PH * u + p < n_in:
                sel[PH * u + p, p * LANE_BLOCK + u] = 1.0
    return jnp.asarray(sel, jnp.bfloat16)


def edge_mask(rows, groups, length, row0, time_of):
    c = lax.axis_index("chan")
    t = lax.axis_index("tm")
    total_rows = lax.axis_size("chan") * C_DEV
    last = lax.axis_size("tm") - 1
    shape = (rows, groups, length)
    row = c * C_DEV + row0 + lax.broadcasted_iota(jnp.int32, shape, 0)
    tau, span = time_of(lax.broadcasted_iota(jnp.int32, shape, 1), lax.broadcasted_iota(jnp.int32, shape, 2))
    ok = (row >= 0) & (row < total_rows)
    ok = ok & ((t > 0) | (tau >= 0)) & ((t < last) | (tau < span))
    return ok.astype(jnp.float32)


def on_device(
    recorded,
    partners,
    offsets,
    first_weight,
    first_bias,
    second_weight,
    second_bias,
    loop_weight,
    third_weight,
    third_bias,
    fourth_weight,
    fourth_bias,
):
    blocks = lax.axis_size("chan")
    times_here, nc = recorded.shape
    wide = C_DEV + 2 * REACH
    padded = jnp.pad(recorded, ((0, 0), (REACH, 3 * C_DEV - REACH)))
    windows = jnp.concatenate(
        [padded[:, k * C_DEV : k * C_DEV + nc].reshape(times_here, blocks, C_DEV) for k in range(3)], axis=2
    )[:, :, :wide]
    outgoing = jnp.transpose(windows, (1, 0, 2))
    arrived = lax.all_to_all(outgoing, "chan", split_axis=0, concat_axis=0, tiled=True)
    times = blocks * times_here
    cols = times // PH
    strain = jnp.transpose(arrived.reshape(blocks, times_here // PH, PH, wide), (3, 2, 0, 1)).reshape(wide, PH, cols)
    tms = lax.axis_size("tm")
    up = [(i, i + 1) for i in range(tms - 1)]
    down = [(j, i) for i, j in up]
    before = lax.ppermute(strain[:, :, cols - WL :], "tm", up)
    after = lax.ppermute(strain[:, :, :WR], "tm", down)
    strain_wide = jnp.concatenate([before, strain, after], axis=2)
    n_s = strain_wide.shape[2]

    n_f = n_s - 3
    first_mask = edge_mask(wide - 6, PH, n_f, 3 - REACH, lambda p, v: (PH * (v - (WL - 1)) + p, times))
    first = banded(
        strain_wide.reshape(wide * PH, n_s),
        weights_first(first_weight),
        first_bias,
        first_mask,
        groups=PH,
        shifts=4,
        n_out=n_f,
        relu=True,
    )

    quarter = times // 4
    length = quarter + 2 * LEAD
    pre_second = banded(
        first,
        weights_stride4(second_weight, 3, 2),
        second_bias,
        jnp.ones((C_DEV, 1, length), jnp.float32),
        groups=1,
        shifts=3,
        n_out=length,
        relu=False,
    )

    own_offset = offsets[0]
    crossing = lax.dynamic_slice(pre_second, (own_offset - 3, 0, 0), (7, F2, length))
    packed = crossing.reshape(blocks, 1, -1)
    moved = jnp.take(
        lax.all_to_all(packed, "chan", split_axis=0, concat_axis=1, tiled=True), partners, axis=1
    )
    came = lax.all_to_all(moved, "chan", split_axis=1, concat_axis=0, tiled=True).reshape(7, F2, length)
    flipped = came[::-1]
    coupling = jnp.einsum("kof,kft->kot", loop_weight, flipped, preferred_element_type=jnp.float32)
    extra = lax.dynamic_update_slice(
        jnp.zeros((C_DEV, F2, length), jnp.float32), coupling, (own_offset - 3, 0, 0)
    )
    second_mask = edge_mask(C_DEV, 1, length, 0, lambda p, j: (j - LEAD, quarter))
    second = (jnp.maximum(pre_second.astype(jnp.float32) + extra, 0.0) * second_mask).astype(jnp.bfloat16)

    ring_up = [(i, i + 1) for i in range(blocks - 1)]
    ring_down = [(j, i) for i, j in ring_up]
    above = lax.ppermute(second[C_DEV - REACH :], "chan", ring_up)
    below = lax.ppermute(second[:REACH], "chan", ring_down)
    second_wide = jnp.concatenate([above, second, below], axis=0)

    n_t = length - 6
    n_sel = quarter // 4 + 1
    third_mask = edge_mask(wide - 6, 1, n_t, 3 - REACH, lambda p, j: (j - (LEAD - 3), quarter))
    third = banded(
        second_wide,
        weights_stride1(third_weight),
        third_bias,
        third_mask,
        groups=1,
        shifts=7,
        n_out=n_t,
        relu=True,
        select=phase_select(n_t, n_sel),
        n_sel=n_sel,
    )
    features = banded(
        third,
        weights_stride4(fourth_weight, 2, 0),
        fourth_bias,
        jnp.ones((C_DEV, 1, quarter // 4), jnp.float32),
        groups=1,
        shifts=2,
        n_out=quarter // 4,
        relu=True,
    )
    return jnp.transpose(features, (1, 0, 2))


def solution(mesh):
    return jax.shard_map(
        on_device,
        mesh=mesh,
        in_specs=(
            P(("tm", "chan"), None),
            P(),
            P("chan"),
            P(),
            P(),
            P(),
            P(),
            P(),
            P(),
            P(),
            P(),
            P(),
        ),
        out_specs=P(None, "chan", "tm"),
        check_vma=False,
    )
```

```python
import numpy as np
import jax
import jax.numpy as jnp
from jax import lax
from jax.experimental import pallas as pl
from jax.sharding import PartitionSpec as P

F2 = 32
C_DEV = 8
REACH = 6
PH = 4
WL = 7
WR = 8
LEAD = 5
LANE_BLOCK = 256


def banded(x, w_all, bias, mask, *, groups, shifts, n_out, relu, select=None, n_sel=0):
    flat = x.ndim == 2
    k_all = w_all.shape[1]
    row_step = k_all // 7
    r_out = (x.shape[0] // row_step if flat else x.shape[0]) - 6
    n_in = x.shape[-1]
    fout = w_all.shape[0] // (groups * shifts)
    if select is None:
        out_shape = (r_out, groups * fout, n_out)
    else:
        out_shape = (r_out, PH * fout, n_sel)

    def kernel(x_ref, w_ref, b_ref, m_ref, *rest):
        if select is None:
            (o_ref,) = rest
        else:
            s_ref, o_ref = rest

        def row(r, carry):
            if flat:
                xs = x_ref[r * row_step : r * row_step + k_all, :]
            else:
                xs = x_ref[pl.ds(r, 7), :, :].reshape(k_all, n_in)
            z = jnp.dot(w_ref[...], xs, preferred_element_type=jnp.float32)
            m_row = m_ref[r]
            for g in range(groups):
                base = g * shifts * fout
                acc = z[base : base + fout, 0:n_out]
                for s in range(1, shifts):
                    acc = acc + z[base + s * fout : base + (s + 1) * fout, s : s + n_out]
                acc = acc + b_ref[...]
                if relu:
                    acc = jnp.maximum(acc, 0.0)
                acc = (acc * m_row[g : g + 1, :]).astype(jnp.bfloat16)
                if select is None:
                    o_ref[r, g * fout : (g + 1) * fout, :] = acc
                else:
                    y = jnp.dot(acc, s_ref[...], preferred_element_type=jnp.float32)
                    for p in range(PH):
                        o_ref[r, p * fout : (p + 1) * fout, :] = y[
                            :, p * LANE_BLOCK : p * LANE_BLOCK + n_sel
                        ].astype(jnp.bfloat16)
            return carry

        if flat:
            for r in range(r_out):
                row(r, 0)
        else:
            lax.fori_loop(0, r_out, row, 0)

    args = [x, w_all, bias.reshape(fout, 1).astype(jnp.float32), mask]
    if select is not None:
        args.append(select)
    return pl.pallas_call(kernel, out_shape=jax.ShapeDtypeStruct(out_shape, jnp.bfloat16))(*args)


def weights_stride1(w):
    fout, fin = w.shape[:2]
    return jnp.transpose(w, (3, 0, 2, 1)).reshape(7 * fout, 7 * fin)


def weights_stride4(w, shifts, lag):
    fout, fin = w.shape[:2]
    s = np.arange(shifts)[:, None]
    p = np.arange(PH)[None, :]
    b = 4 * s + p - lag
    ok = (b >= 0) & (b <= 6)
    taps = jnp.take(w, np.clip(b, 0, 6).reshape(-1), axis=3).reshape(fout, fin, 7, shifts, PH)
    taps = jnp.where(ok[None, None, None], taps, jnp.zeros((), w.dtype))
    return jnp.transpose(taps, (3, 0, 2, 4, 1)).reshape(shifts * fout, 7 * PH * fin)


def weights_first(w):
    fout = w.shape[0]
    p = np.arange(PH)[:, None, None]
    dd = np.arange(4)[None, :, None]
    q = np.arange(PH)[None, None, :]
    b = 4 * (dd - 1) + q - p + 3
    ok = (b >= 0) & (b <= 6)
    taps = jnp.take(w[:, 0], np.clip(b, 0, 6).reshape(-1), axis=2).reshape(fout, 7, PH, 4, PH)
    taps = jnp.where(ok[None, None], taps, jnp.zeros((), w.dtype))
    return jnp.transpose(taps, (2, 3, 0, 1, 4)).reshape(PH * 4 * fout, 7 * PH)


def phase_select(n_in, n_sel):
    sel = np.zeros((n_in, PH * LANE_BLOCK), np.float32)
    for p in range(PH):
        for u in range(n_sel):
            if PH * u + p < n_in:
                sel[PH * u + p, p * LANE_BLOCK + u] = 1.0
    return jnp.asarray(sel, jnp.bfloat16)


def edge_mask(rows, groups, length, row0, time_of, block):
    t = lax.axis_index("tm")
    total_rows = lax.axis_size("chan") * C_DEV
    last = lax.axis_size("tm") - 1
    shape = (rows, groups, length)
    row = block * C_DEV + row0 + lax.broadcasted_iota(jnp.int32, shape, 0)
    tau, span = time_of(lax.broadcasted_iota(jnp.int32, shape, 1), lax.broadcasted_iota(jnp.int32, shape, 2))
    ok = (row >= 0) & (row < total_rows)
    ok = ok & ((t > 0) | (tau >= 0)) & ((t < last) | (tau < span))
    return ok.astype(jnp.float32)


def lower_layers(strain_wide, block, first_weight, first_bias, second_weight, second_bias, times, length):
    wide = C_DEV + 2 * REACH
    n_s = strain_wide.shape[2]
    n_f = n_s - 3
    first_mask = edge_mask(wide - 6, PH, n_f, 3 - REACH, lambda p, v: (PH * (v - (WL - 1)) + p, times), block)
    first = banded(
        strain_wide.reshape(wide * PH, n_s),
        weights_first(first_weight),
        first_bias,
        first_mask,
        groups=PH,
        shifts=4,
        n_out=n_f,
        relu=True,
    )
    return banded(
        first,
        weights_stride4(second_weight, 3, 2),
        second_bias,
        jnp.ones((C_DEV, 1, length), jnp.float32),
        groups=1,
        shifts=3,
        n_out=length,
        relu=False,
    )


def on_device(
    recorded,
    partners,
    offsets,
    first_weight,
    first_bias,
    second_weight,
    second_bias,
    loop_weight,
    third_weight,
    third_bias,
    fourth_weight,
    fourth_bias,
):
    blocks = lax.axis_size("chan")
    me = lax.axis_index("chan")
    mate = partners[me]
    times_here, nc = recorded.shape
    wide = C_DEV + 2 * REACH
    padded = jnp.pad(recorded, ((0, 0), (REACH, 3 * C_DEV - REACH)))
    windows = jnp.concatenate(
        [padded[:, k * C_DEV : k * C_DEV + nc].reshape(times_here, blocks, C_DEV) for k in range(3)], axis=2
    )[:, :, :wide]
    tag = jnp.zeros((times_here, blocks, 1), recorded.dtype).at[0].set(offsets[0].astype(recorded.dtype))
    both = jnp.concatenate([windows, jnp.take(windows, partners, axis=1), tag], axis=2)
    outgoing = jnp.transpose(both, (1, 0, 2))
    arrived = lax.all_to_all(outgoing, "chan", split_axis=0, concat_axis=0, tiled=True)
    mate_offset = arrived[:, 0, 2 * wide].astype(jnp.int32)[mate]
    times = blocks * times_here
    cols = times // PH
    strain = jnp.transpose(
        arrived[:, :, : 2 * wide].reshape(blocks, times_here // PH, PH, 2 * wide), (3, 2, 0, 1)
    ).reshape(2 * wide, PH, cols)
    tms = lax.axis_size("tm")
    up = [(i, i + 1) for i in range(tms - 1)]
    down = [(j, i) for i, j in up]
    before = lax.ppermute(strain[:, :, cols - WL :], "tm", up)
    after = lax.ppermute(strain[:, :, :WR], "tm", down)
    strain_wide = jnp.concatenate([before, strain, after], axis=2)

    quarter = times // 4
    length = quarter + 2 * LEAD
    weights = (first_weight, first_bias, second_weight, second_bias, times, length)
    pre_second = lower_layers(strain_wide[:wide], me, *weights)
    mate_second = lower_layers(strain_wide[wide:], mate, *weights)

    own_offset = offsets[0]
    crossing = lax.dynamic_slice(mate_second, (mate_offset - 3, 0, 0), (7, F2, length))
    flipped = crossing[::-1]
    coupling = jnp.einsum("kof,kft->kot", loop_weight, flipped, preferred_element_type=jnp.float32)
    extra = lax.dynamic_update_slice(
        jnp.zeros((C_DEV, F2, length), jnp.float32), coupling, (own_offset - 3, 0, 0)
    )
    second_mask = edge_mask(C_DEV, 1, length, 0, lambda p, j: (j - LEAD, quarter), me)
    second = (jnp.maximum(pre_second.astype(jnp.float32) + extra, 0.0) * second_mask).astype(jnp.bfloat16)

    ring_up = [(i, i + 1) for i in range(blocks - 1)]
    ring_down = [(j, i) for i, j in ring_up]
    above = lax.ppermute(second[C_DEV - REACH :], "chan", ring_up)
    below = lax.ppermute(second[:REACH], "chan", ring_down)
    second_wide = jnp.concatenate([above, second, below], axis=0)

    n_t = length - 6
    n_sel = quarter // 4 + 1
    third_mask = edge_mask(wide - 6, 1, n_t, 3 - REACH, lambda p, j: (j - (LEAD - 3), quarter), me)
    third = banded(
        second_wide,
        weights_stride1(third_weight),
        third_bias,
        third_mask,
        groups=1,
        shifts=7,
        n_out=n_t,
        relu=True,
        select=phase_select(n_t, n_sel),
        n_sel=n_sel,
    )
    features = banded(
        third,
        weights_stride4(fourth_weight, 2, 0),
        fourth_bias,
        jnp.ones((C_DEV, 1, quarter // 4), jnp.float32),
        groups=1,
        shifts=2,
        n_out=quarter // 4,
        relu=True,
    )
    return jnp.transpose(features, (1, 0, 2))


def solution(mesh):
    return jax.shard_map(
        on_device,
        mesh=mesh,
        in_specs=(
            P(("tm", "chan"), None),
            P(),
            P("chan"),
            P(),
            P(),
            P(),
            P(),
            P(),
            P(),
            P(),
            P(),
            P(),
        ),
        out_specs=P(None, "chan", "tm"),
        check_vma=False,
    )
```

```python
import numpy as np
import jax
import jax.numpy as jnp
from jax import lax
from jax.experimental import pallas as pl
from jax.sharding import PartitionSpec as P

F2 = 32
C_DEV = 8
REACH = 6
PH = 4
WL = 7
WR = 8
LEAD = 5
LANE_BLOCK = 256


def banded(x, w_all, bias, b_row, mask, *, groups, shifts, n_out, relu, select=None, n_sel=0):
    windows = x.shape[0]
    flat = x.ndim == 3
    k_all = w_all.shape[1]
    row_step = k_all // 7
    r_out = (x.shape[1] // row_step if flat else x.shape[1]) - 6
    n_in = x.shape[-1]
    fout = w_all.shape[0] // (groups * shifts)
    if select is None:
        out_shape = (windows, r_out, groups * fout, n_out)
    else:
        out_shape = (windows, r_out, PH * fout, n_sel)

    def kernel(x_ref, w_ref, b_ref, m_ref, *rest):
        if select is None:
            (o_ref,) = rest
        else:
            s_ref, o_ref = rest
        b_val = b_ref[b_row : b_row + fout, :]

        def row(r, carry):
            if flat:
                xs = x_ref[r * row_step : r * row_step + k_all, :]
            else:
                xs = x_ref[pl.ds(r, 7), :, :].reshape(k_all, n_in)
            z = jnp.dot(w_ref[...], xs, preferred_element_type=jnp.float32)
            m_row = m_ref[r]
            for g in range(groups):
                base = g * shifts * fout
                acc = z[base : base + fout, 0:n_out]
                for s in range(1, shifts):
                    acc = acc + z[base + s * fout : base + (s + 1) * fout, s : s + n_out]
                acc = acc + b_val
                if relu:
                    acc = jnp.maximum(acc, 0.0)
                acc = (acc * m_row[g : g + 1, :]).astype(jnp.bfloat16)
                if select is None:
                    o_ref[r, g * fout : (g + 1) * fout, :] = acc
                    continue
                for k in range(pl.cdiv(n_out, LANE_BLOCK // 2)):
                    lo = k * (LANE_BLOCK // 2)
                    width = min(LANE_BLOCK // 2, n_out - lo)
                    n_u = pl.cdiv(width, PH)
                    y = jnp.dot(acc[:, lo : lo + width], s_ref[0:width, :], preferred_element_type=jnp.float32)
                    seg = LANE_BLOCK // 2 // PH
                    for p in range(PH):
                        o_ref[r, p * fout : (p + 1) * fout, lo // PH : lo // PH + n_u] = y[
                            :, p * seg : p * seg + n_u
                        ].astype(jnp.bfloat16)
            return carry

        if flat:
            for r in range(r_out):
                row(r, 0)
        else:
            lax.fori_loop(0, r_out, row, 0)

    def per_window(a):
        return pl.BlockSpec((None,) + a.shape[1:], lambda w, n=a.ndim - 1: (w,) + (0,) * n)

    def whole(a):
        return pl.BlockSpec(a.shape, lambda w, n=a.ndim: (0,) * n)

    args = [x, w_all, bias, mask]
    specs = [per_window(x), whole(w_all), whole(bias), per_window(mask)]
    if select is not None:
        args.append(select)
        specs.append(whole(select))
    return pl.pallas_call(
        kernel,
        grid=(windows,),
        in_specs=specs,
        out_specs=pl.BlockSpec((None,) + out_shape[1:], lambda w: (w, 0, 0, 0)),
        out_shape=jax.ShapeDtypeStruct(out_shape, jnp.bfloat16),
    )(*args)


def weights_stride1(w):
    fout, fin = w.shape[:2]
    return jnp.transpose(w, (3, 0, 2, 1)).reshape(7 * fout, 7 * fin)


def weights_stride4(w, shifts, lag):
    fout, fin = w.shape[:2]
    s = np.arange(shifts)[:, None]
    p = np.arange(PH)[None, :]
    b = 4 * s + p - lag
    ok = (b >= 0) & (b <= 6)
    taps = jnp.take(w, np.clip(b, 0, 6).reshape(-1), axis=3).reshape(fout, fin, 7, shifts, PH)
    taps = jnp.where(ok[None, None, None], taps, jnp.zeros((), w.dtype))
    return jnp.transpose(taps, (3, 0, 2, 4, 1)).reshape(shifts * fout, 7 * PH * fin)


def weights_first(w):
    fout = w.shape[0]
    p = np.arange(PH)[:, None, None]
    dd = np.arange(4)[None, :, None]
    q = np.arange(PH)[None, None, :]
    b = 4 * (dd - 1) + q - p + 3
    ok = (b >= 0) & (b <= 6)
    taps = jnp.take(w[:, 0], np.clip(b, 0, 6).reshape(-1), axis=2).reshape(fout, 7, PH, 4, PH)
    taps = jnp.where(ok[None, None], taps, jnp.zeros((), w.dtype))
    return jnp.transpose(taps, (2, 3, 0, 1, 4)).reshape(PH * 4 * fout, 7 * PH)


def phase_select():
    block = LANE_BLOCK // 2
    seg = block // PH
    sel = np.zeros((block, block), np.float32)
    for p in range(PH):
        for u in range(seg):
            sel[PH * u + p, p * seg + u] = 1.0
    return jnp.asarray(sel, jnp.bfloat16)


def edge_mask(rows, groups, length, row0, time_of, block):
    t = lax.axis_index("tm")
    total_rows = lax.axis_size("chan") * C_DEV
    last = lax.axis_size("tm") - 1
    shape = (rows, groups, length)
    row = block * C_DEV + row0 + lax.broadcasted_iota(jnp.int32, shape, 0)
    tau, span = time_of(lax.broadcasted_iota(jnp.int32, shape, 1), lax.broadcasted_iota(jnp.int32, shape, 2))
    ok = (row >= 0) & (row < total_rows)
    ok = ok & ((t > 0) | (tau >= 0)) & ((t < last) | (tau < span))
    return ok.astype(jnp.float32)


def lower_layers(strain_wide, blocks_of, first_weight, biases, second_weight, times, length):
    wide = C_DEV + 2 * REACH
    n_win, n_s = strain_wide.shape[0], strain_wide.shape[-1]
    n_f = n_s - 3
    first_mask = jnp.stack(
        [
            edge_mask(wide - 6, PH, n_f, 3 - REACH, lambda p, v: (PH * (v - (WL - 1)) + p, times), b)
            for b in blocks_of
        ]
    )
    first = banded(
        strain_wide.reshape(n_win, wide * PH, n_s),
        weights_first(first_weight),
        biases,
        0,
        first_mask,
        groups=PH,
        shifts=4,
        n_out=n_f,
        relu=True,
    )
    return banded(
        first,
        weights_stride4(second_weight, 3, 2),
        biases,
        16,
        jnp.ones((n_win, C_DEV, 1, length), jnp.float32),
        groups=1,
        shifts=3,
        n_out=length,
        relu=False,
    )


def on_device(
    recorded,
    partners,
    offsets,
    first_weight,
    first_bias,
    second_weight,
    second_bias,
    loop_weight,
    third_weight,
    third_bias,
    fourth_weight,
    fourth_bias,
):
    blocks = lax.axis_size("chan")
    me = lax.axis_index("chan")
    mate = partners[me]
    times_here, nc = recorded.shape
    wide = C_DEV + 2 * REACH
    padded = jnp.pad(recorded, ((0, 0), (REACH, 3 * C_DEV - REACH)))
    windows = jnp.concatenate(
        [padded[:, k * C_DEV : k * C_DEV + nc].reshape(times_here, blocks, C_DEV) for k in range(3)], axis=2
    )[:, :, :wide]
    tag = jnp.zeros((times_here, blocks, 1), recorded.dtype).at[0].set(offsets[0].astype(recorded.dtype))
    both = jnp.concatenate([windows, jnp.take(windows, partners, axis=1), tag], axis=2)
    outgoing = jnp.transpose(both, (1, 0, 2))
    arrived = lax.all_to_all(outgoing, "chan", split_axis=0, concat_axis=0, tiled=True)
    mate_offset = arrived[:, 0, 2 * wide].astype(jnp.int32)[mate]
    times = blocks * times_here
    cols = times // PH
    strain = jnp.transpose(
        arrived[:, :, : 2 * wide].reshape(blocks, times_here // PH, PH, 2 * wide), (3, 2, 0, 1)
    ).reshape(2 * wide, PH, cols)
    tms = lax.axis_size("tm")
    up = [(i, i + 1) for i in range(tms - 1)]
    down = [(j, i) for i, j in up]
    before = lax.ppermute(strain[:, :, cols - WL :], "tm", up)
    after = lax.ppermute(strain[:, :, :WR], "tm", down)
    strain_wide = jnp.concatenate([before, strain, after], axis=2)

    quarter = times // 4
    length = quarter + 2 * LEAD
    biases = jnp.concatenate([first_bias, second_bias, third_bias, fourth_bias]).reshape(-1, 1)
    lower = lower_layers(
        strain_wide.reshape(2, wide, PH, -1), (me, mate), first_weight, biases, second_weight, times, length
    )
    pre_second, mate_second = lower[0], lower[1]

    own_offset = offsets[0]
    crossing = lax.dynamic_slice(mate_second, (mate_offset - 3, 0, 0), (7, F2, length))
    flipped = crossing[::-1]
    coupling = jnp.einsum("kof,kft->kot", loop_weight, flipped, preferred_element_type=jnp.float32)
    extra = lax.dynamic_update_slice(
        jnp.zeros((C_DEV, F2, length), jnp.float32), coupling, (own_offset - 3, 0, 0)
    )
    second_mask = edge_mask(C_DEV, 1, length, 0, lambda p, j: (j - LEAD, quarter), me)
    second = (jnp.maximum(pre_second.astype(jnp.float32) + extra, 0.0) * second_mask).astype(jnp.bfloat16)

    ring_up = [(i, i + 1) for i in range(blocks - 1)]
    ring_down = [(j, i) for i, j in ring_up]
    above = lax.ppermute(second[C_DEV - REACH :], "chan", ring_up)
    below = lax.ppermute(second[:REACH], "chan", ring_down)
    second_wide = jnp.concatenate([above, second, below], axis=0)

    n_t = length - 6
    n_sel = quarter // 4 + 1
    third_mask = edge_mask(wide - 6, 1, n_t, 3 - REACH, lambda p, j: (j - (LEAD - 3), quarter), me)
    third = banded(
        second_wide[None],
        weights_stride1(third_weight),
        biases,
        48,
        third_mask[None],
        groups=1,
        shifts=7,
        n_out=n_t,
        relu=True,
        select=phase_select(),
        n_sel=n_sel,
    )
    features = banded(
        third,
        weights_stride4(fourth_weight, 2, 0),
        biases,
        80,
        jnp.ones((1, C_DEV, 1, quarter // 4), jnp.float32),
        groups=1,
        shifts=2,
        n_out=quarter // 4,
        relu=True,
    )
    return jnp.transpose(features[0], (1, 0, 2))


def solution(mesh):
    return jax.shard_map(
        on_device,
        mesh=mesh,
        in_specs=(
            P(("tm", "chan"), None),
            P(),
            P("chan"),
            P(),
            P(),
            P(),
            P(),
            P(),
            P(),
            P(),
            P(),
            P(),
        ),
        out_specs=P(None, "chan", "tm"),
        check_vma=False,
    )
```

```python
import numpy as np
import jax
import jax.numpy as jnp
from jax import lax
from jax.experimental import pallas as pl
from jax.sharding import PartitionSpec as P

F2 = 32
C_DEV = 8
REACH = 6
PH = 4
WL = 7
WR = 8
LEAD = 5
LANE_BLOCK = 256


def banded(x, w_all, bias, b_row, mask, *, groups, shifts, n_out, relu, select=None, n_sel=0):
    windows = x.shape[0]
    flat = x.ndim == 3
    k_all = w_all.shape[1]
    row_step = k_all // 7
    r_out = (x.shape[1] // row_step if flat else x.shape[1]) - 6
    n_in = x.shape[-1]
    fout = w_all.shape[0] // (groups * shifts)
    if select is None:
        out_shape = (windows, r_out, groups * fout, n_out)
    else:
        out_shape = (windows, r_out, PH * fout, n_sel)

    def kernel(x_ref, w_ref, b_ref, m_ref, *rest):
        if select is None:
            (o_ref,) = rest
        else:
            s_ref, o_ref = rest
        b_val = b_ref[b_row : b_row + fout, :]

        def row(r, carry):
            if flat:
                xs = x_ref[r * row_step : r * row_step + k_all, :]
            else:
                xs = x_ref[pl.ds(r, 7), :, :].reshape(k_all, n_in)
            z = jnp.dot(w_ref[...], xs, preferred_element_type=jnp.float32)
            m_row = m_ref[r]
            for g in range(groups):
                base = g * shifts * fout
                acc = z[base : base + fout, 0:n_out]
                for s in range(1, shifts):
                    acc = acc + z[base + s * fout : base + (s + 1) * fout, s : s + n_out]
                acc = acc + b_val
                if relu:
                    acc = jnp.maximum(acc, 0.0)
                acc = (acc * m_row[g : g + 1, :]).astype(jnp.bfloat16)
                if select is None:
                    o_ref[r, g * fout : (g + 1) * fout, :] = acc
                    continue
                for k in range(pl.cdiv(n_out, LANE_BLOCK // 2)):
                    lo = k * (LANE_BLOCK // 2)
                    width = min(LANE_BLOCK // 2, n_out - lo)
                    n_u = pl.cdiv(width, PH)
                    y = jnp.dot(acc[:, lo : lo + width], s_ref[0:width, :], preferred_element_type=jnp.float32)
                    seg = LANE_BLOCK // 2 // PH
                    for p in range(PH):
                        o_ref[r, p * fout : (p + 1) * fout, lo // PH : lo // PH + n_u] = y[
                            :, p * seg : p * seg + n_u
                        ].astype(jnp.bfloat16)
            return carry

        if flat:
            for r in range(r_out):
                row(r, 0)
        else:
            lax.fori_loop(0, r_out, row, 0)

    def per_window(a):
        return pl.BlockSpec((None,) + a.shape[1:], lambda w, n=a.ndim - 1: (w,) + (0,) * n)

    def whole(a):
        return pl.BlockSpec(a.shape, lambda w, n=a.ndim: (0,) * n)

    args = [x, w_all, bias, mask]
    specs = [per_window(x), whole(w_all), whole(bias), per_window(mask)]
    if select is not None:
        args.append(select)
        specs.append(whole(select))
    return pl.pallas_call(
        kernel,
        grid=(windows,),
        in_specs=specs,
        out_specs=pl.BlockSpec((None,) + out_shape[1:], lambda w: (w, 0, 0, 0)),
        out_shape=jax.ShapeDtypeStruct(out_shape, jnp.bfloat16),
    )(*args)


def weights_stride1(w):
    fout, fin = w.shape[:2]
    return jnp.transpose(w, (3, 0, 2, 1)).reshape(7 * fout, 7 * fin)


def weights_stride4(w, shifts, lag):
    fout, fin = w.shape[:2]
    s = np.arange(shifts)[:, None]
    p = np.arange(PH)[None, :]
    b = 4 * s + p - lag
    ok = (b >= 0) & (b <= 6)
    taps = jnp.take(w, np.clip(b, 0, 6).reshape(-1), axis=3).reshape(fout, fin, 7, shifts, PH)
    taps = jnp.where(ok[None, None, None], taps, jnp.zeros((), w.dtype))
    return jnp.transpose(taps, (3, 0, 2, 4, 1)).reshape(shifts * fout, 7 * PH * fin)


def weights_first(w):
    fout = w.shape[0]
    p = np.arange(PH)[:, None, None]
    dd = np.arange(4)[None, :, None]
    q = np.arange(PH)[None, None, :]
    b = 4 * (dd - 1) + q - p + 3
    ok = (b >= 0) & (b <= 6)
    taps = jnp.take(w[:, 0], np.clip(b, 0, 6).reshape(-1), axis=2).reshape(fout, 7, PH, 4, PH)
    taps = jnp.where(ok[None, None], taps, jnp.zeros((), w.dtype))
    return jnp.transpose(taps, (2, 3, 0, 1, 4)).reshape(PH * 4 * fout, 7 * PH)


def phase_select():
    block = LANE_BLOCK // 2
    seg = block // PH
    sel = np.zeros((block, block), np.float32)
    for p in range(PH):
        for u in range(seg):
            sel[PH * u + p, p * seg + u] = 1.0
    return jnp.asarray(sel, jnp.bfloat16)


def edge_mask(rows, groups, length, row0, time_of, block):
    t = lax.axis_index("tm")
    total_rows = lax.axis_size("chan") * C_DEV
    last = lax.axis_size("tm") - 1
    shape = (rows, groups, length)
    row = block * C_DEV + row0 + lax.broadcasted_iota(jnp.int32, shape, 0)
    tau, span = time_of(lax.broadcasted_iota(jnp.int32, shape, 1), lax.broadcasted_iota(jnp.int32, shape, 2))
    ok = (row >= 0) & (row < total_rows)
    ok = ok & ((t > 0) | (tau >= 0)) & ((t < last) | (tau < span))
    return ok.astype(jnp.float32)


def lower_layers(strain_wide, blocks_of, first_weight, biases, second_weight, times, length):
    wide = C_DEV + 2 * REACH
    n_win, n_s = strain_wide.shape[0], strain_wide.shape[-1]
    n_f = n_s - 3
    first_mask = jnp.stack(
        [
            edge_mask(wide - 6, PH, n_f, 3 - REACH, lambda p, v: (PH * (v - (WL - 1)) + p, times), b)
            for b in blocks_of
        ]
    )
    first = banded(
        strain_wide.reshape(n_win, wide * PH, n_s),
        weights_first(first_weight),
        biases,
        0,
        first_mask,
        groups=PH,
        shifts=4,
        n_out=n_f,
        relu=True,
    )
    return banded(
        first,
        weights_stride4(second_weight, 3, 2),
        biases,
        16,
        jnp.ones((n_win, C_DEV, 1, length), jnp.float32),
        groups=1,
        shifts=3,
        n_out=length,
        relu=False,
    )


def on_device(
    recorded,
    partners,
    offsets,
    first_weight,
    first_bias,
    second_weight,
    second_bias,
    loop_weight,
    third_weight,
    third_bias,
    fourth_weight,
    fourth_bias,
):
    blocks = lax.axis_size("chan")
    me = lax.axis_index("chan")
    mate = partners[me]
    times_here, nc = recorded.shape
    wide = C_DEV + 2 * REACH
    by_channel = jnp.pad(jnp.transpose(recorded), ((REACH, 3 * C_DEV - REACH), (0, 0)))
    windows = jnp.concatenate(
        [by_channel[k * C_DEV : k * C_DEV + nc].reshape(blocks, C_DEV, times_here) for k in range(3)], axis=1
    )[:, :wide]
    tag = jnp.zeros((blocks, 1, times_here), recorded.dtype).at[:, 0, 0].set(offsets[0].astype(recorded.dtype))
    both = jnp.concatenate([windows, jnp.take(windows, partners, axis=0), tag], axis=1)
    outgoing = jnp.transpose(both.reshape(blocks, 2 * wide + 1, times_here // PH, PH), (0, 1, 3, 2))
    arrived = lax.all_to_all(outgoing, "chan", split_axis=0, concat_axis=3, tiled=True)[0]
    times = blocks * times_here
    cols = times // PH
    mate_offset = arrived[2 * wide, 0].reshape(blocks, times_here // PH)[:, 0].astype(jnp.int32)[mate]
    strain = arrived[: 2 * wide]
    tms = lax.axis_size("tm")
    up = [(i, i + 1) for i in range(tms - 1)]
    down = [(j, i) for i, j in up]
    before = lax.ppermute(strain[:, :, cols - WL :], "tm", up)
    after = lax.ppermute(strain[:, :, :WR], "tm", down)
    strain_wide = jnp.concatenate([before, strain, after], axis=2)

    quarter = times // 4
    length = quarter + 2 * LEAD
    biases = jnp.concatenate([first_bias, second_bias, third_bias, fourth_bias]).reshape(-1, 1)
    lower = lower_layers(
        strain_wide.reshape(2, wide, PH, -1), (me, mate), first_weight, biases, second_weight, times, length
    )
    pre_second, mate_second = lower[0], lower[1]

    own_offset = offsets[0]
    crossing = lax.dynamic_slice(mate_second, (mate_offset - 3, 0, 0), (7, F2, length))
    flipped = crossing[::-1]
    coupling = jnp.einsum("kof,kft->kot", loop_weight, flipped, preferred_element_type=jnp.float32)
    extra = lax.dynamic_update_slice(
        jnp.zeros((C_DEV, F2, length), jnp.float32), coupling, (own_offset - 3, 0, 0)
    )
    second_mask = edge_mask(C_DEV, 1, length, 0, lambda p, j: (j - LEAD, quarter), me)
    second = (jnp.maximum(pre_second.astype(jnp.float32) + extra, 0.0) * second_mask).astype(jnp.bfloat16)

    ring_up = [(i, i + 1) for i in range(blocks - 1)]
    ring_down = [(j, i) for i, j in ring_up]
    above = lax.ppermute(second[C_DEV - REACH :], "chan", ring_up)
    below = lax.ppermute(second[:REACH], "chan", ring_down)
    second_wide = jnp.concatenate([above, second, below], axis=0)

    n_t = length - 6
    n_sel = quarter // 4 + 1
    third_mask = edge_mask(wide - 6, 1, n_t, 3 - REACH, lambda p, j: (j - (LEAD - 3), quarter), me)
    third = banded(
        second_wide[None],
        weights_stride1(third_weight),
        biases,
        48,
        third_mask[None],
        groups=1,
        shifts=7,
        n_out=n_t,
        relu=True,
        select=phase_select(),
        n_sel=n_sel,
    )
    features = banded(
        third,
        weights_stride4(fourth_weight, 2, 0),
        biases,
        80,
        jnp.ones((1, C_DEV, 1, quarter // 4), jnp.float32),
        groups=1,
        shifts=2,
        n_out=quarter // 4,
        relu=True,
    )
    return jnp.transpose(features[0], (1, 0, 2))


def solution(mesh):
    return jax.shard_map(
        on_device,
        mesh=mesh,
        in_specs=(
            P(("tm", "chan"), None),
            P(),
            P("chan"),
            P(),
            P(),
            P(),
            P(),
            P(),
            P(),
            P(),
            P(),
            P(),
        ),
        out_specs=P(None, "chan", "tm"),
        check_vma=False,
    )
```

```python
import numpy as np
import jax
import jax.numpy as jnp
from jax import lax
from jax.experimental import pallas as pl
from jax.sharding import PartitionSpec as P

F2 = 32
C_DEV = 8
REACH = 6
PH = 4
WL = 7
WR = 8
LEAD = 5
LANE_BLOCK = 256


def banded(x, w_all, bias, b_row, mask, *, groups, shifts, n_out, relu, select=None, n_sel=0):
    windows = x.shape[0]
    flat = x.ndim == 3
    k_all = w_all.shape[1]
    row_step = k_all // 7
    r_out = (x.shape[1] // row_step if flat else x.shape[1]) - 6
    n_in = x.shape[-1]
    fout = w_all.shape[0] // (groups * shifts)
    if select is None:
        out_shape = (windows, r_out, groups * fout, n_out)
    else:
        out_shape = (windows, r_out, PH * fout, n_sel)

    def kernel(x_ref, w_ref, b_ref, m_ref, *rest):
        if select is None:
            (o_ref,) = rest
        else:
            s_ref, o_ref = rest
        b_val = b_ref[b_row : b_row + fout, :]

        def row(r, carry):
            if flat:
                xs = x_ref[r * row_step : r * row_step + k_all, :]
            else:
                xs = x_ref[pl.ds(r, 7), :, :].reshape(k_all, n_in)
            z = jnp.dot(w_ref[...], xs, preferred_element_type=jnp.float32)
            m_row = m_ref[r]
            for g in range(groups):
                base = g * shifts * fout
                acc = z[base : base + fout, 0:n_out]
                for s in range(1, shifts):
                    acc = acc + z[base + s * fout : base + (s + 1) * fout, s : s + n_out]
                acc = acc + b_val
                if relu:
                    acc = jnp.maximum(acc, 0.0)
                acc = (acc * m_row[g : g + 1, :]).astype(jnp.bfloat16)
                if select is None:
                    o_ref[r, g * fout : (g + 1) * fout, :] = acc
                    continue
                for k in range(pl.cdiv(n_out, LANE_BLOCK // 2)):
                    lo = k * (LANE_BLOCK // 2)
                    width = min(LANE_BLOCK // 2, n_out - lo)
                    n_u = pl.cdiv(width, PH)
                    y = jnp.dot(acc[:, lo : lo + width], s_ref[0:width, :], preferred_element_type=jnp.float32)
                    seg = LANE_BLOCK // 2 // PH
                    for p in range(PH):
                        o_ref[r, p * fout : (p + 1) * fout, lo // PH : lo // PH + n_u] = y[
                            :, p * seg : p * seg + n_u
                        ].astype(jnp.bfloat16)
            return carry

        if flat:
            for r in range(r_out):
                row(r, 0)
        else:
            lax.fori_loop(0, r_out, row, 0)

    def per_window(a):
        return pl.BlockSpec((None,) + a.shape[1:], lambda w, n=a.ndim - 1: (w,) + (0,) * n)

    def whole(a):
        return pl.BlockSpec(a.shape, lambda w, n=a.ndim: (0,) * n)

    args = [x, w_all, bias, mask]
    specs = [per_window(x), whole(w_all), whole(bias), per_window(mask)]
    if select is not None:
        args.append(select)
        specs.append(whole(select))
    return pl.pallas_call(
        kernel,
        grid=(windows,),
        in_specs=specs,
        out_specs=pl.BlockSpec((None,) + out_shape[1:], lambda w: (w, 0, 0, 0)),
        out_shape=jax.ShapeDtypeStruct(out_shape, jnp.bfloat16),
    )(*args)


def strain_layout(raw, left, right, rows):
    channels = raw.shape[1]
    cols = raw.shape[0] // PH
    n_out = WL + cols + WR

    def kernel(raw_ref, l_ref, r_ref, o_ref):
        ci = lax.broadcasted_iota(jnp.int32, (rows, channels), 1)
        ri = lax.broadcasted_iota(jnp.int32, (rows, channels), 0)
        nt = (((1,), (1,)), ((), ()))
        pieces = ((l_ref, 0, left.shape[0] // PH, left.shape[0] // PH - WL), (raw_ref, WL, cols, 0), (r_ref, WL + cols, WR, 0))
        for src, lo, n, skip in pieces:
            acc = None
            for q in range(PH):
                e = (ri == ci * PH + q).astype(jnp.float32)
                piece = src[pl.ds(q, n, stride=PH), :].astype(jnp.float32)
                y = lax.dot_general(e, piece, nt, preferred_element_type=jnp.float32)
                acc = y if acc is None else acc + y
            o_ref[:, lo : lo + n - skip] = acc[:, skip:].astype(o_ref.dtype)

    return pl.pallas_call(kernel, out_shape=jax.ShapeDtypeStruct((rows, n_out), jnp.bfloat16))(raw, left, right)


def weights_stride1(w):
    fout, fin = w.shape[:2]
    return jnp.transpose(w, (3, 0, 2, 1)).reshape(7 * fout, 7 * fin)


def weights_stride4(w, shifts, lag):
    fout, fin = w.shape[:2]
    s = np.arange(shifts)[:, None]
    p = np.arange(PH)[None, :]
    b = 4 * s + p - lag
    ok = (b >= 0) & (b <= 6)
    taps = jnp.take(w, np.clip(b, 0, 6).reshape(-1), axis=3).reshape(fout, fin, 7, shifts, PH)
    taps = jnp.where(ok[None, None, None], taps, jnp.zeros((), w.dtype))
    return jnp.transpose(taps, (3, 0, 2, 4, 1)).reshape(shifts * fout, 7 * PH * fin)


def weights_first(w):
    fout = w.shape[0]
    p = np.arange(PH)[:, None, None]
    dd = np.arange(4)[None, :, None]
    q = np.arange(PH)[None, None, :]
    b = 4 * (dd - 1) + q - p + 3
    ok = (b >= 0) & (b <= 6)
    taps = jnp.take(w[:, 0], np.clip(b, 0, 6).reshape(-1), axis=2).reshape(fout, 7, PH, 4, PH)
    taps = jnp.where(ok[None, None], taps, jnp.zeros((), w.dtype))
    return jnp.transpose(taps, (2, 3, 0, 1, 4)).reshape(PH * 4 * fout, 7 * PH)


def phase_select():
    block = LANE_BLOCK // 2
    seg = block // PH
    sel = np.zeros((block, block), np.float32)
    for p in range(PH):
        for u in range(seg):
            sel[PH * u + p, p * seg + u] = 1.0
    return jnp.asarray(sel, jnp.bfloat16)


def edge_mask(rows, groups, length, row0, time_of, block):
    t = lax.axis_index("tm")
    total_rows = lax.axis_size("chan") * C_DEV
    last = lax.axis_size("tm") - 1
    shape = (rows, groups, length)
    row = block * C_DEV + row0 + lax.broadcasted_iota(jnp.int32, shape, 0)
    tau, span = time_of(lax.broadcasted_iota(jnp.int32, shape, 1), lax.broadcasted_iota(jnp.int32, shape, 2))
    ok = (row >= 0) & (row < total_rows)
    ok = ok & ((t > 0) | (tau >= 0)) & ((t < last) | (tau < span))
    return ok.astype(jnp.float32)


def lower_layers(strain_wide, blocks_of, first_weight, biases, second_weight, times, length):
    wide = C_DEV + 2 * REACH
    n_win, n_s = strain_wide.shape[0], strain_wide.shape[-1]
    n_f = n_s - 3
    first_mask = jnp.stack(
        [
            edge_mask(wide - 6, PH, n_f, 3 - REACH, lambda p, v: (PH * (v - (WL - 1)) + p, times), b)
            for b in blocks_of
        ]
    )
    first = banded(
        strain_wide.reshape(n_win, wide * PH, n_s),
        weights_first(first_weight),
        biases,
        0,
        first_mask,
        groups=PH,
        shifts=4,
        n_out=n_f,
        relu=True,
    )
    return banded(
        first,
        weights_stride4(second_weight, 3, 2),
        biases,
        16,
        jnp.ones((n_win, C_DEV, 1, length), jnp.float32),
        groups=1,
        shifts=3,
        n_out=length,
        relu=False,
    )


def on_device(
    recorded,
    partners,
    offsets,
    first_weight,
    first_bias,
    second_weight,
    second_bias,
    loop_weight,
    third_weight,
    third_bias,
    fourth_weight,
    fourth_bias,
):
    blocks = lax.axis_size("chan")
    me = lax.axis_index("chan")
    mate = partners[me]
    times_here, nc = recorded.shape
    wide = C_DEV + 2 * REACH
    padded = jnp.pad(recorded, ((0, 0), (REACH, 3 * C_DEV - REACH)))
    windows = jnp.concatenate(
        [padded[:, k * C_DEV : k * C_DEV + nc].reshape(times_here, blocks, C_DEV) for k in range(3)], axis=2
    )[:, :, :wide]
    tag = jnp.zeros((times_here, blocks, 1), recorded.dtype).at[0].set(offsets[0].astype(recorded.dtype))
    both = jnp.concatenate([windows, jnp.take(windows, partners, axis=1), tag], axis=2)
    outgoing = jnp.transpose(both, (1, 0, 2))
    arrived = lax.all_to_all(outgoing, "chan", split_axis=0, concat_axis=0, tiled=True)
    mate_offset = arrived[:, 0, 2 * wide].astype(jnp.int32)[mate]
    times = blocks * times_here
    tms = lax.axis_size("tm")
    up = [(i, i + 1) for i in range(tms - 1)]
    down = [(j, i) for i, j in up]
    before = lax.ppermute(arrived[blocks - 1], "tm", up)
    after = lax.ppermute(arrived[0, : PH * WR], "tm", down)
    strain_wide = strain_layout(arrived.reshape(times, -1), before, after, 2 * wide * PH)

    quarter = times // 4
    length = quarter + 2 * LEAD
    biases = jnp.concatenate([first_bias, second_bias, third_bias, fourth_bias]).reshape(-1, 1)
    lower = lower_layers(
        strain_wide.reshape(2, wide, PH, -1), (me, mate), first_weight, biases, second_weight, times, length
    )
    pre_second, mate_second = lower[0], lower[1]

    own_offset = offsets[0]
    crossing = lax.dynamic_slice(mate_second, (mate_offset - 3, 0, 0), (7, F2, length))
    flipped = crossing[::-1]
    coupling = jnp.einsum("kof,kft->kot", loop_weight, flipped, preferred_element_type=jnp.float32)
    extra = lax.dynamic_update_slice(
        jnp.zeros((C_DEV, F2, length), jnp.float32), coupling, (own_offset - 3, 0, 0)
    )
    second_mask = edge_mask(C_DEV, 1, length, 0, lambda p, j: (j - LEAD, quarter), me)
    second = (jnp.maximum(pre_second.astype(jnp.float32) + extra, 0.0) * second_mask).astype(jnp.bfloat16)

    ring_up = [(i, i + 1) for i in range(blocks - 1)]
    ring_down = [(j, i) for i, j in ring_up]
    above = lax.ppermute(second[C_DEV - REACH :], "chan", ring_up)
    below = lax.ppermute(second[:REACH], "chan", ring_down)
    second_wide = jnp.concatenate([above, second, below], axis=0)

    n_t = length - 6
    n_sel = quarter // 4 + 1
    third_mask = edge_mask(wide - 6, 1, n_t, 3 - REACH, lambda p, j: (j - (LEAD - 3), quarter), me)
    third = banded(
        second_wide[None],
        weights_stride1(third_weight),
        biases,
        48,
        third_mask[None],
        groups=1,
        shifts=7,
        n_out=n_t,
        relu=True,
        select=phase_select(),
        n_sel=n_sel,
    )
    features = banded(
        third,
        weights_stride4(fourth_weight, 2, 0),
        biases,
        80,
        jnp.ones((1, C_DEV, 1, quarter // 4), jnp.float32),
        groups=1,
        shifts=2,
        n_out=quarter // 4,
        relu=True,
    )
    return jnp.transpose(features[0], (1, 0, 2))


def solution(mesh):
    return jax.shard_map(
        on_device,
        mesh=mesh,
        in_specs=(
            P(("tm", "chan"), None),
            P(),
            P("chan"),
            P(),
            P(),
            P(),
            P(),
            P(),
            P(),
            P(),
            P(),
            P(),
        ),
        out_specs=P(None, "chan", "tm"),
        check_vma=False,
    )
```

```python
import numpy as np
import jax
import jax.numpy as jnp
from jax import lax
from jax.experimental import pallas as pl
from jax.sharding import PartitionSpec as P

F2 = 32
C_DEV = 8
REACH = 6
PH = 4
WL = 7
WR = 8
LEAD = 5
LANE_BLOCK = 256


def banded(x, w_all, bias, b_row, mask, *, groups, shifts, n_out, relu, select=None, n_sel=0):
    windows = x.shape[0]
    flat = x.ndim == 3
    k_all = w_all.shape[1]
    row_step = k_all // 7
    r_out = (x.shape[1] // row_step if flat else x.shape[1]) - 6
    n_in = x.shape[-1]
    fout = w_all.shape[0] // (groups * shifts)
    if select is None:
        out_shape = (windows, r_out, groups * fout, n_out)
    else:
        out_shape = (windows, r_out, PH * fout, n_sel)

    def kernel(x_ref, w_ref, b_ref, m_ref, *rest):
        if select is None:
            (o_ref,) = rest
        else:
            s_ref, o_ref = rest
        b_val = b_ref[b_row : b_row + fout, :]

        def row(r, carry):
            if flat:
                xs = x_ref[r * row_step : r * row_step + k_all, :]
            else:
                xs = x_ref[r : r + 7, :, :].reshape(k_all, n_in)
            z = jnp.dot(w_ref[...], xs, preferred_element_type=jnp.float32)
            m_row = m_ref[r]
            for g in range(groups):
                base = g * shifts * fout
                acc = z[base : base + fout, 0:n_out]
                for s in range(1, shifts):
                    acc = acc + z[base + s * fout : base + (s + 1) * fout, s : s + n_out]
                acc = acc + b_val
                if relu:
                    acc = jnp.maximum(acc, 0.0)
                acc = (acc * m_row[g : g + 1, :]).astype(jnp.bfloat16)
                if select is None:
                    o_ref[r, g * fout : (g + 1) * fout, :] = acc
                    continue
                for k in range(pl.cdiv(n_out, LANE_BLOCK // 2)):
                    lo = k * (LANE_BLOCK // 2)
                    width = min(LANE_BLOCK // 2, n_out - lo)
                    n_u = pl.cdiv(width, PH)
                    y = jnp.dot(acc[:, lo : lo + width], s_ref[0:width, :], preferred_element_type=jnp.float32)
                    seg = LANE_BLOCK // 2 // PH
                    for p in range(PH):
                        o_ref[r, p * fout : (p + 1) * fout, lo // PH : lo // PH + n_u] = y[
                            :, p * seg : p * seg + n_u
                        ].astype(jnp.bfloat16)
            return carry

        for r in range(r_out):
            row(r, 0)

    def per_window(a):
        return pl.BlockSpec((None,) + a.shape[1:], lambda w, n=a.ndim - 1: (w,) + (0,) * n)

    def whole(a):
        return pl.BlockSpec(a.shape, lambda w, n=a.ndim: (0,) * n)

    args = [x, w_all, bias, mask]
    specs = [per_window(x), whole(w_all), whole(bias), per_window(mask)]
    if select is not None:
        args.append(select)
        specs.append(whole(select))
    return pl.pallas_call(
        kernel,
        grid=(windows,),
        in_specs=specs,
        out_specs=pl.BlockSpec((None,) + out_shape[1:], lambda w: (w, 0, 0, 0)),
        out_shape=jax.ShapeDtypeStruct(out_shape, jnp.bfloat16),
    )(*args)


def strain_layout(raw, left, right, rows):
    channels = raw.shape[1]
    cols = raw.shape[0] // PH
    n_out = WL + cols + WR

    def kernel(raw_ref, l_ref, r_ref, o_ref):
        ci = lax.broadcasted_iota(jnp.int32, (rows, channels), 1)
        ri = lax.broadcasted_iota(jnp.int32, (rows, channels), 0)
        nt = (((1,), (1,)), ((), ()))
        pieces = ((l_ref, 0, left.shape[0] // PH, left.shape[0] // PH - WL), (raw_ref, WL, cols, 0), (r_ref, WL + cols, WR, 0))
        for src, lo, n, skip in pieces:
            acc = None
            for q in range(PH):
                e = (ri == ci * PH + q).astype(jnp.float32)
                piece = src[pl.ds(q, n, stride=PH), :].astype(jnp.float32)
                y = lax.dot_general(e, piece, nt, preferred_element_type=jnp.float32)
                acc = y if acc is None else acc + y
            o_ref[:, lo : lo + n - skip] = acc[:, skip:].astype(o_ref.dtype)

    return pl.pallas_call(kernel, out_shape=jax.ShapeDtypeStruct((rows, n_out), jnp.bfloat16))(raw, left, right)


def weights_stride1(w):
    fout, fin = w.shape[:2]
    return jnp.transpose(w, (3, 0, 2, 1)).reshape(7 * fout, 7 * fin)


def weights_stride4(w, shifts, lag):
    fout, fin = w.shape[:2]
    s = np.arange(shifts)[:, None]
    p = np.arange(PH)[None, :]
    b = 4 * s + p - lag
    ok = (b >= 0) & (b <= 6)
    taps = jnp.take(w, np.clip(b, 0, 6).reshape(-1), axis=3).reshape(fout, fin, 7, shifts, PH)
    taps = jnp.where(ok[None, None, None], taps, jnp.zeros((), w.dtype))
    return jnp.transpose(taps, (3, 0, 2, 4, 1)).reshape(shifts * fout, 7 * PH * fin)


def weights_first(w):
    fout = w.shape[0]
    p = np.arange(PH)[:, None, None]
    dd = np.arange(4)[None, :, None]
    q = np.arange(PH)[None, None, :]
    b = 4 * (dd - 1) + q - p + 3
    ok = (b >= 0) & (b <= 6)
    taps = jnp.take(w[:, 0], np.clip(b, 0, 6).reshape(-1), axis=2).reshape(fout, 7, PH, 4, PH)
    taps = jnp.where(ok[None, None], taps, jnp.zeros((), w.dtype))
    return jnp.transpose(taps, (2, 3, 0, 1, 4)).reshape(PH * 4 * fout, 7 * PH)


def phase_select():
    block = LANE_BLOCK // 2
    seg = block // PH
    sel = np.zeros((block, block), np.float32)
    for p in range(PH):
        for u in range(seg):
            sel[PH * u + p, p * seg + u] = 1.0
    return jnp.asarray(sel, jnp.bfloat16)


def edge_mask(rows, groups, length, row0, time_of, block):
    t = lax.axis_index("tm")
    total_rows = lax.axis_size("chan") * C_DEV
    last = lax.axis_size("tm") - 1
    shape = (rows, groups, length)
    row = block * C_DEV + row0 + lax.broadcasted_iota(jnp.int32, shape, 0)
    tau, span = time_of(lax.broadcasted_iota(jnp.int32, shape, 1), lax.broadcasted_iota(jnp.int32, shape, 2))
    ok = (row >= 0) & (row < total_rows)
    ok = ok & ((t > 0) | (tau >= 0)) & ((t < last) | (tau < span))
    return ok.astype(jnp.float32)


def lower_layers(strain_wide, blocks_of, first_weight, biases, second_weight, times, length):
    wide = C_DEV + 2 * REACH
    n_win, n_s = strain_wide.shape[0], strain_wide.shape[-1]
    n_f = n_s - 3
    first_mask = jnp.stack(
        [
            edge_mask(wide - 6, PH, n_f, 3 - REACH, lambda p, v: (PH * (v - (WL - 1)) + p, times), b)
            for b in blocks_of
        ]
    )
    first = banded(
        strain_wide.reshape(n_win, wide * PH, n_s),
        weights_first(first_weight),
        biases,
        0,
        first_mask,
        groups=PH,
        shifts=4,
        n_out=n_f,
        relu=True,
    )
    return banded(
        first,
        weights_stride4(second_weight, 3, 2),
        biases,
        16,
        jnp.ones((n_win, C_DEV, 1, length), jnp.float32),
        groups=1,
        shifts=3,
        n_out=length,
        relu=False,
    )


def on_device(
    recorded,
    partners,
    offsets,
    first_weight,
    first_bias,
    second_weight,
    second_bias,
    loop_weight,
    third_weight,
    third_bias,
    fourth_weight,
    fourth_bias,
):
    blocks = lax.axis_size("chan")
    me = lax.axis_index("chan")
    mate = partners[me]
    times_here, nc = recorded.shape
    wide = C_DEV + 2 * REACH
    padded = jnp.pad(recorded, ((0, 0), (REACH, 3 * C_DEV - REACH)))
    windows = jnp.concatenate(
        [padded[:, k * C_DEV : k * C_DEV + nc].reshape(times_here, blocks, C_DEV) for k in range(3)], axis=2
    )[:, :, :wide]
    tag = jnp.zeros((times_here, blocks, 1), recorded.dtype).at[0].set(offsets[0].astype(recorded.dtype))
    both = jnp.concatenate([windows, jnp.take(windows, partners, axis=1), tag], axis=2)
    outgoing = jnp.transpose(both, (1, 0, 2))
    arrived = lax.all_to_all(outgoing, "chan", split_axis=0, concat_axis=0, tiled=True)
    mate_offset = arrived[:, 0, 2 * wide].astype(jnp.int32)[mate]
    times = blocks * times_here
    tms = lax.axis_size("tm")
    up = [(i, i + 1) for i in range(tms - 1)]
    down = [(j, i) for i, j in up]
    before = lax.ppermute(arrived[blocks - 1], "tm", up)
    after = lax.ppermute(arrived[0, : PH * WR], "tm", down)
    strain_wide = strain_layout(arrived.reshape(times, -1), before, after, 2 * wide * PH)

    quarter = times // 4
    length = quarter + 2 * LEAD
    biases = jnp.concatenate([first_bias, second_bias, third_bias, fourth_bias]).reshape(-1, 1)
    lower = lower_layers(
        strain_wide.reshape(2, wide, PH, -1), (me, mate), first_weight, biases, second_weight, times, length
    )
    pre_second, mate_second = lower[0], lower[1]

    own_offset = offsets[0]
    crossing = lax.dynamic_slice(mate_second, (mate_offset - 3, 0, 0), (7, F2, length))
    flipped = crossing[::-1]
    coupling = jnp.einsum("kof,kft->kot", loop_weight, flipped, preferred_element_type=jnp.float32)
    extra = lax.dynamic_update_slice(
        jnp.zeros((C_DEV, F2, length), jnp.float32), coupling, (own_offset - 3, 0, 0)
    )
    second_mask = edge_mask(C_DEV, 1, length, 0, lambda p, j: (j - LEAD, quarter), me)
    second = (jnp.maximum(pre_second.astype(jnp.float32) + extra, 0.0) * second_mask).astype(jnp.bfloat16)

    ring_up = [(i, i + 1) for i in range(blocks - 1)]
    ring_down = [(j, i) for i, j in ring_up]
    above = lax.ppermute(second[C_DEV - REACH :], "chan", ring_up)
    below = lax.ppermute(second[:REACH], "chan", ring_down)
    second_wide = jnp.concatenate([above, second, below], axis=0)

    n_t = length - 6
    n_sel = quarter // 4 + 1
    third_mask = edge_mask(wide - 6, 1, n_t, 3 - REACH, lambda p, j: (j - (LEAD - 3), quarter), me)
    third = banded(
        second_wide[None],
        weights_stride1(third_weight),
        biases,
        48,
        third_mask[None],
        groups=1,
        shifts=7,
        n_out=n_t,
        relu=True,
        select=phase_select(),
        n_sel=n_sel,
    )
    features = banded(
        third,
        weights_stride4(fourth_weight, 2, 0),
        biases,
        80,
        jnp.ones((1, C_DEV, 1, quarter // 4), jnp.float32),
        groups=1,
        shifts=2,
        n_out=quarter // 4,
        relu=True,
    )
    return jnp.transpose(features[0], (1, 0, 2))


def solution(mesh):
    return jax.shard_map(
        on_device,
        mesh=mesh,
        in_specs=(
            P(("tm", "chan"), None),
            P(),
            P("chan"),
            P(),
            P(),
            P(),
            P(),
            P(),
            P(),
            P(),
            P(),
            P(),
        ),
        out_specs=P(None, "chan", "tm"),
        check_vma=False,
    )
```

```python
import numpy as np
import jax
import jax.numpy as jnp
from jax import lax
from jax.experimental import pallas as pl
from jax.sharding import PartitionSpec as P

F2 = 32
C_DEV = 8
REACH = 6
PH = 4
WL = 7
WR = 8
LEAD = 5
LANE_BLOCK = 256


def banded(x, w_all, bias, b_row, mask, *, groups, shifts, n_out, relu, select=None, n_sel=0):
    windows = x.shape[0]
    flat = x.ndim == 3
    k_all = w_all.shape[1]
    row_step = k_all // 7
    r_out = (x.shape[1] // row_step if flat else x.shape[1]) - 6
    n_in = x.shape[-1]
    fout = w_all.shape[0] // (groups * shifts)
    if select is None:
        out_shape = (windows, r_out, groups * fout, n_out)
    else:
        out_shape = (windows, r_out, PH * fout, n_sel)

    def kernel(x_ref, w_ref, b_ref, m_ref, *rest):
        if select is None:
            (o_ref,) = rest
        else:
            s_ref, o_ref = rest
        b_val = b_ref[b_row : b_row + fout, :]

        def row(r, carry):
            if flat:
                xs = x_ref[r * row_step : r * row_step + k_all, :]
            else:
                xs = x_ref[r : r + 7, :, :].reshape(k_all, n_in)
            z = jnp.dot(w_ref[...], xs, preferred_element_type=jnp.float32)
            m_row = m_ref[r]
            for g in range(groups):
                base = g * shifts * fout
                acc = z[base : base + fout, 0:n_out]
                for s in range(1, shifts):
                    acc = acc + z[base + s * fout : base + (s + 1) * fout, s : s + n_out]
                acc = acc + b_val
                if relu:
                    acc = jnp.maximum(acc, 0.0)
                acc = (acc * m_row[g : g + 1, :]).astype(jnp.bfloat16)
                if select is None:
                    o_ref[r, g * fout : (g + 1) * fout, :] = acc
                    continue
                for k in range(pl.cdiv(n_out, LANE_BLOCK // 2)):
                    lo = k * (LANE_BLOCK // 2)
                    width = min(LANE_BLOCK // 2, n_out - lo)
                    n_u = pl.cdiv(width, PH)
                    y = jnp.dot(acc[:, lo : lo + width], s_ref[0:width, :], preferred_element_type=jnp.float32)
                    seg = LANE_BLOCK // 2 // PH
                    for p in range(PH):
                        o_ref[r, p * fout : (p + 1) * fout, lo // PH : lo // PH + n_u] = y[
                            :, p * seg : p * seg + n_u
                        ].astype(jnp.bfloat16)
            return carry

        for r in range(r_out):
            row(r, 0)

    def per_window(a):
        return pl.BlockSpec((None,) + a.shape[1:], lambda w, n=a.ndim - 1: (w,) + (0,) * n)

    def whole(a):
        return pl.BlockSpec(a.shape, lambda w, n=a.ndim: (0,) * n)

    args = [x, w_all, bias, mask]
    specs = [per_window(x), whole(w_all), whole(bias), per_window(mask)]
    if select is not None:
        args.append(select)
        specs.append(whole(select))
    return pl.pallas_call(
        kernel,
        grid=(windows,),
        in_specs=specs,
        out_specs=pl.BlockSpec((None,) + out_shape[1:], lambda w: (w, 0, 0, 0)),
        out_shape=jax.ShapeDtypeStruct(out_shape, jnp.bfloat16),
    )(*args)


def strain_layout(raw, left, right, rows):
    channels = raw.shape[1]
    cols = raw.shape[0] // PH
    n_out = WL + cols + WR

    def kernel(raw_ref, l_ref, r_ref, o_ref):
        ci = lax.broadcasted_iota(jnp.int32, (rows, channels), 1)
        ri = lax.broadcasted_iota(jnp.int32, (rows, channels), 0)
        nt = (((1,), (1,)), ((), ()))
        pieces = ((l_ref, 0, left.shape[0] // PH, left.shape[0] // PH - WL), (raw_ref, WL, cols, 0), (r_ref, WL + cols, WR, 0))
        for src, lo, n, skip in pieces:
            acc = None
            for q in range(PH):
                e = (ri == ci * PH + q).astype(jnp.float32)
                piece = src[pl.ds(q, n, stride=PH), :].astype(jnp.float32)
                y = lax.dot_general(e, piece, nt, preferred_element_type=jnp.float32)
                acc = y if acc is None else acc + y
            o_ref[:, lo : lo + n - skip] = acc[:, skip:].astype(o_ref.dtype)

    return pl.pallas_call(kernel, out_shape=jax.ShapeDtypeStruct((rows, n_out), jnp.bfloat16))(raw, left, right)


def weights_stride1(w):
    fout, fin = w.shape[:2]
    return jnp.transpose(w, (3, 0, 2, 1)).reshape(7 * fout, 7 * fin)


def weights_stride4(w, shifts, lag):
    fout, fin = w.shape[:2]
    s = np.arange(shifts)[:, None]
    p = np.arange(PH)[None, :]
    b = 4 * s + p - lag
    ok = (b >= 0) & (b <= 6)
    taps = jnp.take(w, np.clip(b, 0, 6).reshape(-1), axis=3).reshape(fout, fin, 7, shifts, PH)
    taps = jnp.where(ok[None, None, None], taps, jnp.zeros((), w.dtype))
    return jnp.transpose(taps, (3, 0, 2, 4, 1)).reshape(shifts * fout, 7 * PH * fin)


def weights_first(w):
    fout = w.shape[0]
    p = np.arange(PH)[:, None, None]
    dd = np.arange(4)[None, :, None]
    q = np.arange(PH)[None, None, :]
    b = 4 * (dd - 1) + q - p + 3
    ok = (b >= 0) & (b <= 6)
    taps = jnp.take(w[:, 0], np.clip(b, 0, 6).reshape(-1), axis=2).reshape(fout, 7, PH, 4, PH)
    taps = jnp.where(ok[None, None], taps, jnp.zeros((), w.dtype))
    return jnp.transpose(taps, (2, 3, 0, 1, 4)).reshape(PH * 4 * fout, 7 * PH)


def phase_select():
    block = LANE_BLOCK // 2
    seg = block // PH
    sel = np.zeros((block, block), np.float32)
    for p in range(PH):
        for u in range(seg):
            sel[PH * u + p, p * seg + u] = 1.0
    return jnp.asarray(sel, jnp.bfloat16)


def edge_mask(rows, groups, length, row0, time_of, block):
    t = lax.axis_index("tm")
    total_rows = lax.axis_size("chan") * C_DEV
    last = lax.axis_size("tm") - 1
    shape = (rows, groups, length)
    row = block * C_DEV + row0 + lax.broadcasted_iota(jnp.int32, shape, 0)
    tau, span = time_of(lax.broadcasted_iota(jnp.int32, shape, 1), lax.broadcasted_iota(jnp.int32, shape, 2))
    ok = (row >= 0) & (row < total_rows)
    ok = ok & ((t > 0) | (tau >= 0)) & ((t < last) | (tau < span))
    return ok.astype(jnp.float32)


def lower_layers(strain_wide, blocks_of, first_weight, biases, second_weight, times, length):
    wide = C_DEV + 2 * REACH
    n_win, n_s = strain_wide.shape[0], strain_wide.shape[-1]
    n_f = n_s - 3
    first_mask = jnp.stack(
        [
            edge_mask(wide - 6, PH, n_f, 3 - REACH, lambda p, v: (PH * (v - (WL - 1)) + p, times), b)
            for b in blocks_of
        ]
    )
    first = banded(
        strain_wide.reshape(n_win, wide * PH, n_s),
        first_weight,
        biases,
        0,
        first_mask,
        groups=PH,
        shifts=4,
        n_out=n_f,
        relu=True,
    )
    return banded(
        first,
        second_weight,
        biases,
        16,
        jnp.ones((n_win, C_DEV, 1, length), jnp.float32),
        groups=1,
        shifts=3,
        n_out=length,
        relu=False,
    )


def on_device(
    recorded,
    partners,
    offsets,
    first_weight,
    first_bias,
    second_weight,
    second_bias,
    loop_weight,
    third_weight,
    third_bias,
    fourth_weight,
    fourth_bias,
):
    blocks = lax.axis_size("chan")
    me = lax.axis_index("chan")
    mate = partners[me]
    times_here, nc = recorded.shape
    wide = C_DEV + 2 * REACH
    padded = jnp.pad(recorded, ((0, 0), (REACH, 3 * C_DEV - REACH)))
    windows = jnp.concatenate(
        [padded[:, k * C_DEV : k * C_DEV + nc].reshape(times_here, blocks, C_DEV) for k in range(3)], axis=2
    )[:, :, :wide]
    tag = jnp.zeros((times_here, blocks, 1), recorded.dtype).at[0].set(offsets[0].astype(recorded.dtype))
    both = jnp.concatenate([windows, jnp.take(windows, partners, axis=1), tag], axis=2)
    outgoing = jnp.transpose(both, (1, 0, 2))
    arrived = lax.all_to_all(outgoing, "chan", split_axis=0, concat_axis=0, tiled=True)
    biases = jnp.concatenate([first_bias, second_bias, third_bias, fourth_bias]).reshape(-1, 1)
    prepared = (
        weights_first(first_weight),
        weights_stride4(second_weight, 3, 2),
        weights_stride1(third_weight),
        weights_stride4(fourth_weight, 2, 0),
        biases,
    )
    arrived, (first_weight, second_weight, third_weight, fourth_weight, biases) = lax.optimization_barrier(
        (arrived, prepared)
    )
    mate_offset = arrived[:, 0, 2 * wide].astype(jnp.int32)[mate]
    times = blocks * times_here
    tms = lax.axis_size("tm")
    up = [(i, i + 1) for i in range(tms - 1)]
    down = [(j, i) for i, j in up]
    before = lax.ppermute(arrived[blocks - 1], "tm", up)
    after = lax.ppermute(arrived[0, : PH * WR], "tm", down)
    strain_wide = strain_layout(arrived.reshape(times, -1), before, after, 2 * wide * PH)

    quarter = times // 4
    length = quarter + 2 * LEAD
    lower = lower_layers(
        strain_wide.reshape(2, wide, PH, -1), (me, mate), first_weight, biases, second_weight, times, length
    )
    pre_second, mate_second = lower[0], lower[1]

    own_offset = offsets[0]
    crossing = lax.dynamic_slice(mate_second, (mate_offset - 3, 0, 0), (7, F2, length))
    flipped = crossing[::-1]
    coupling = jnp.einsum("kof,kft->kot", loop_weight, flipped, preferred_element_type=jnp.float32)
    extra = lax.dynamic_update_slice(
        jnp.zeros((C_DEV, F2, length), jnp.float32), coupling, (own_offset - 3, 0, 0)
    )
    second_mask = edge_mask(C_DEV, 1, length, 0, lambda p, j: (j - LEAD, quarter), me)
    second = (jnp.maximum(pre_second.astype(jnp.float32) + extra, 0.0) * second_mask).astype(jnp.bfloat16)

    ring_up = [(i, i + 1) for i in range(blocks - 1)]
    ring_down = [(j, i) for i, j in ring_up]
    above = lax.ppermute(second[C_DEV - REACH :], "chan", ring_up)
    below = lax.ppermute(second[:REACH], "chan", ring_down)
    second_wide = jnp.concatenate([above, second, below], axis=0)

    n_t = length - 6
    n_sel = quarter // 4 + 1
    third_mask = edge_mask(wide - 6, 1, n_t, 3 - REACH, lambda p, j: (j - (LEAD - 3), quarter), me)
    third = banded(
        second_wide[None],
        third_weight,
        biases,
        48,
        third_mask[None],
        groups=1,
        shifts=7,
        n_out=n_t,
        relu=True,
        select=phase_select(),
        n_sel=n_sel,
    )
    features = banded(
        third,
        fourth_weight,
        biases,
        80,
        jnp.ones((1, C_DEV, 1, quarter // 4), jnp.float32),
        groups=1,
        shifts=2,
        n_out=quarter // 4,
        relu=True,
    )
    return jnp.transpose(features[0], (1, 0, 2))


def solution(mesh):
    return jax.shard_map(
        on_device,
        mesh=mesh,
        in_specs=(
            P(("tm", "chan"), None),
            P(),
            P("chan"),
            P(),
            P(),
            P(),
            P(),
            P(),
            P(),
            P(),
            P(),
            P(),
        ),
        out_specs=P(None, "chan", "tm"),
        check_vma=False,
    )
```

```python
import numpy as np
import jax
import jax.numpy as jnp
from jax import lax
from jax.experimental import pallas as pl
from jax.sharding import PartitionSpec as P

F2 = 32
C_DEV = 8
REACH = 6
PH = 4
WL = 7
WR = 8
LEAD = 5
LANE_BLOCK = 256


def banded(x, w_all, bias, b_row, mask, *, groups, shifts, n_out, relu, select=None, n_sel=0):
    windows = x.shape[0]
    flat = x.ndim == 3
    k_all = w_all.shape[1]
    row_step = k_all // 7
    r_out = (x.shape[1] // row_step if flat else x.shape[1]) - 6
    n_in = x.shape[-1]
    fout = w_all.shape[0] // (groups * shifts)
    if select is None:
        out_shape = (windows, r_out, groups * fout, n_out)
    else:
        out_shape = (windows, r_out, PH * fout, n_sel)

    def kernel(x_ref, w_ref, b_ref, *rest):
        if mask is None:
            m_ref, rest = None, rest
        else:
            m_ref, rest = rest[0], rest[1:]
        if select is None:
            (o_ref,) = rest
        else:
            s_ref, o_ref = rest
        b_val = b_ref[b_row : b_row + fout, :]

        def row(r, carry):
            if flat:
                xs = x_ref[r * row_step : r * row_step + k_all, :]
            else:
                xs = x_ref[r : r + 7, :, :].reshape(k_all, n_in)
            z = jnp.dot(w_ref[...], xs, preferred_element_type=jnp.float32)
            m_row = None if m_ref is None else m_ref[r]
            for g in range(groups):
                base = g * shifts * fout
                acc = z[base : base + fout, 0:n_out]
                for s in range(1, shifts):
                    acc = acc + z[base + s * fout : base + (s + 1) * fout, s : s + n_out]
                acc = acc + b_val
                if relu:
                    acc = jnp.maximum(acc, 0.0)
                if m_row is not None:
                    acc = acc * m_row[g : g + 1, :]
                acc = acc.astype(jnp.bfloat16)
                if select is None:
                    o_ref[r, g * fout : (g + 1) * fout, :] = acc
                    continue
                for k in range(pl.cdiv(n_out, LANE_BLOCK // 2)):
                    lo = k * (LANE_BLOCK // 2)
                    width = min(LANE_BLOCK // 2, n_out - lo)
                    n_u = pl.cdiv(width, PH)
                    y = jnp.dot(acc[:, lo : lo + width], s_ref[0:width, :], preferred_element_type=jnp.float32)
                    seg = LANE_BLOCK // 2 // PH
                    for p in range(PH):
                        o_ref[r, p * fout : (p + 1) * fout, lo // PH : lo // PH + n_u] = y[
                            :, p * seg : p * seg + n_u
                        ].astype(jnp.bfloat16)
            return carry

        for r in range(r_out):
            row(r, 0)

    def per_window(a):
        return pl.BlockSpec((None,) + a.shape[1:], lambda w, n=a.ndim - 1: (w,) + (0,) * n)

    def whole(a):
        return pl.BlockSpec(a.shape, lambda w, n=a.ndim: (0,) * n)

    args = [x, w_all, bias]
    specs = [per_window(x), whole(w_all), whole(bias)]
    if mask is not None:
        args.append(mask)
        specs.append(per_window(mask))
    if select is not None:
        args.append(select)
        specs.append(whole(select))
    return pl.pallas_call(
        kernel,
        grid=(windows,),
        in_specs=specs,
        out_specs=pl.BlockSpec((None,) + out_shape[1:], lambda w: (w, 0, 0, 0)),
        out_shape=jax.ShapeDtypeStruct(out_shape, jnp.bfloat16),
    )(*args)


def strain_layout(raw, left, right, rows):
    channels = raw.shape[1]
    cols = raw.shape[0] // PH
    n_out = WL + cols + WR

    def kernel(raw_ref, l_ref, r_ref, o_ref):
        ci = lax.broadcasted_iota(jnp.int32, (rows, channels), 1)
        ri = lax.broadcasted_iota(jnp.int32, (rows, channels), 0)
        nt = (((1,), (1,)), ((), ()))
        pieces = ((l_ref, 0, left.shape[0] // PH, left.shape[0] // PH - WL), (raw_ref, WL, cols, 0), (r_ref, WL + cols, WR, 0))
        for src, lo, n, skip in pieces:
            acc = None
            for q in range(PH):
                e = (ri == ci * PH + q).astype(jnp.float32)
                piece = src[pl.ds(q, n, stride=PH), :].astype(jnp.float32)
                y = lax.dot_general(e, piece, nt, preferred_element_type=jnp.float32)
                acc = y if acc is None else acc + y
            o_ref[:, lo : lo + n - skip] = acc[:, skip:].astype(o_ref.dtype)

    return pl.pallas_call(kernel, out_shape=jax.ShapeDtypeStruct((rows, n_out), jnp.bfloat16))(raw, left, right)


def weights_stride1(w):
    fout, fin = w.shape[:2]
    return jnp.transpose(w, (3, 0, 2, 1)).reshape(7 * fout, 7 * fin)


def weights_stride4(w, shifts, lag):
    fout, fin = w.shape[:2]
    s = np.arange(shifts)[:, None]
    p = np.arange(PH)[None, :]
    b = 4 * s + p - lag
    ok = (b >= 0) & (b <= 6)
    taps = jnp.take(w, np.clip(b, 0, 6).reshape(-1), axis=3).reshape(fout, fin, 7, shifts, PH)
    taps = jnp.where(ok[None, None, None], taps, jnp.zeros((), w.dtype))
    return jnp.transpose(taps, (3, 0, 2, 4, 1)).reshape(shifts * fout, 7 * PH * fin)


def weights_first(w):
    fout = w.shape[0]
    p = np.arange(PH)[:, None, None]
    dd = np.arange(4)[None, :, None]
    q = np.arange(PH)[None, None, :]
    b = 4 * (dd - 1) + q - p + 3
    ok = (b >= 0) & (b <= 6)
    taps = jnp.take(w[:, 0], np.clip(b, 0, 6).reshape(-1), axis=2).reshape(fout, 7, PH, 4, PH)
    taps = jnp.where(ok[None, None], taps, jnp.zeros((), w.dtype))
    return jnp.transpose(taps, (2, 3, 0, 1, 4)).reshape(PH * 4 * fout, 7 * PH)


def phase_select():
    block = LANE_BLOCK // 2
    seg = block // PH
    sel = np.zeros((block, block), np.float32)
    for p in range(PH):
        for u in range(seg):
            sel[PH * u + p, p * seg + u] = 1.0
    return jnp.asarray(sel, jnp.bfloat16)


def edge_mask(rows, groups, length, row0, time_of, block):
    t = lax.axis_index("tm")
    total_rows = lax.axis_size("chan") * C_DEV
    last = lax.axis_size("tm") - 1
    shape = (rows, groups, length)
    row = block * C_DEV + row0 + lax.broadcasted_iota(jnp.int32, shape, 0)
    tau, span = time_of(lax.broadcasted_iota(jnp.int32, shape, 1), lax.broadcasted_iota(jnp.int32, shape, 2))
    ok = (row >= 0) & (row < total_rows)
    ok = ok & ((t > 0) | (tau >= 0)) & ((t < last) | (tau < span))
    return ok.astype(jnp.float32)


def lower_layers(strain_wide, blocks_of, first_weight, biases, second_weight, times, length):
    wide = C_DEV + 2 * REACH
    n_win, n_s = strain_wide.shape[0], strain_wide.shape[-1]
    n_f = n_s - 3
    first_mask = jnp.stack(
        [
            edge_mask(wide - 6, PH, n_f, 3 - REACH, lambda p, v: (PH * (v - (WL - 1)) + p, times), b)
            for b in blocks_of
        ]
    )
    first = banded(
        strain_wide.reshape(n_win, wide * PH, n_s),
        first_weight,
        biases,
        0,
        first_mask,
        groups=PH,
        shifts=4,
        n_out=n_f,
        relu=True,
    )
    return banded(
        first,
        second_weight,
        biases,
        16,
        None,
        groups=1,
        shifts=3,
        n_out=length,
        relu=False,
    )


def on_device(
    recorded,
    partners,
    offsets,
    first_weight,
    first_bias,
    second_weight,
    second_bias,
    loop_weight,
    third_weight,
    third_bias,
    fourth_weight,
    fourth_bias,
):
    blocks = lax.axis_size("chan")
    me = lax.axis_index("chan")
    mate = partners[me]
    times_here, nc = recorded.shape
    wide = C_DEV + 2 * REACH
    padded = jnp.pad(recorded, ((0, 0), (REACH, 3 * C_DEV - REACH)))
    windows = jnp.concatenate(
        [padded[:, k * C_DEV : k * C_DEV + nc].reshape(times_here, blocks, C_DEV) for k in range(3)], axis=2
    )[:, :, :wide]
    tag = jnp.zeros((times_here, blocks, 1), recorded.dtype).at[0].set(offsets[0].astype(recorded.dtype))
    both = jnp.concatenate([windows, jnp.take(windows, partners, axis=1, mode="clip"), tag], axis=2)
    outgoing = jnp.transpose(both, (1, 0, 2))
    arrived = lax.all_to_all(outgoing, "chan", split_axis=0, concat_axis=0, tiled=True)
    biases = jnp.concatenate([first_bias, second_bias, third_bias, fourth_bias]).reshape(-1, 1)
    prepared = (
        weights_first(first_weight),
        weights_stride4(second_weight, 3, 2),
        weights_stride1(third_weight),
        weights_stride4(fourth_weight, 2, 0),
        biases,
    )
    quarter = blocks * times_here // 4
    length = quarter + 2 * LEAD
    n_t = length - 6
    masks = (
        edge_mask(C_DEV, 1, length, 0, lambda p, j: (j - LEAD, quarter), me),
        edge_mask(wide - 6, 1, n_t, 3 - REACH, lambda p, j: (j - (LEAD - 3), quarter), me),
    )
    arrived, prepared, masks = lax.optimization_barrier((arrived, prepared, masks))
    first_weight, second_weight, third_weight, fourth_weight, biases = prepared
    second_mask, third_mask = masks
    mate_offset = arrived[:, 0, 2 * wide].astype(jnp.int32)[mate]
    times = blocks * times_here
    tms = lax.axis_size("tm")
    up = [(i, i + 1) for i in range(tms - 1)]
    down = [(j, i) for i, j in up]
    before = lax.ppermute(arrived[blocks - 1], "tm", up)
    after = lax.ppermute(arrived[0, : PH * WR], "tm", down)
    strain_wide = strain_layout(arrived.reshape(times, -1), before, after, 2 * wide * PH)

    quarter = times // 4
    length = quarter + 2 * LEAD
    lower = lower_layers(
        strain_wide.reshape(2, wide, PH, -1), (me, mate), first_weight, biases, second_weight, times, length
    )
    pre_second, mate_second = lower[0], lower[1]

    own_offset = offsets[0]
    crossing = lax.dynamic_slice(mate_second, (mate_offset - 3, 0, 0), (7, F2, length))
    flipped = crossing[::-1]
    coupling = jnp.einsum("kof,kft->kot", loop_weight, flipped, preferred_element_type=jnp.float32)
    extra = lax.dynamic_update_slice(
        jnp.zeros((C_DEV, F2, length), jnp.float32), coupling, (own_offset - 3, 0, 0)
    )
    second = (jnp.maximum(pre_second.astype(jnp.float32) + extra, 0.0) * second_mask).astype(jnp.bfloat16)

    ring_up = [(i, i + 1) for i in range(blocks - 1)]
    ring_down = [(j, i) for i, j in ring_up]
    above = lax.ppermute(second[C_DEV - REACH :], "chan", ring_up)
    below = lax.ppermute(second[:REACH], "chan", ring_down)
    second_wide = jnp.concatenate([above, second, below], axis=0)

    n_t = length - 6
    n_sel = quarter // 4 + 1
    third = banded(
        second_wide[None],
        third_weight,
        biases,
        48,
        third_mask[None],
        groups=1,
        shifts=7,
        n_out=n_t,
        relu=True,
        select=phase_select(),
        n_sel=n_sel,
    )
    features = banded(
        third,
        fourth_weight,
        biases,
        80,
        None,
        groups=1,
        shifts=2,
        n_out=quarter // 4,
        relu=True,
    )
    return jnp.transpose(features[0], (1, 0, 2))


def solution(mesh):
    return jax.shard_map(
        on_device,
        mesh=mesh,
        in_specs=(
            P(("tm", "chan"), None),
            P(),
            P("chan"),
            P(),
            P(),
            P(),
            P(),
            P(),
            P(),
            P(),
            P(),
            P(),
        ),
        out_specs=P(None, "chan", "tm"),
        check_vma=False,
    )
```

```python
import numpy as np
import jax
import jax.numpy as jnp
from jax import lax
from jax.experimental import pallas as pl
from jax.sharding import PartitionSpec as P

F2 = 32
C_DEV = 8
REACH = 6
PH = 4
WL = 7
WR = 8
LEAD = 5
LANE_BLOCK = 256


def banded(x, w_all, bias, b_row, mask, *, groups, shifts, n_out, relu, select=None, n_sel=0, rows_inner=False):
    windows = x.shape[0]
    flat = x.ndim == 3
    k_all = w_all.shape[1]
    row_step = k_all // 7
    r_out = (x.shape[1] // row_step if flat else x.shape[1]) - 6
    n_in = x.shape[-1]
    fout = w_all.shape[0] // (groups * shifts)
    if rows_inner:
        out_shape = (windows, groups * fout, r_out, n_out)
    elif select is None:
        out_shape = (windows, r_out, groups * fout, n_out)
    else:
        out_shape = (windows, r_out, PH * fout, n_sel)

    def kernel(x_ref, w_ref, b_ref, *rest):
        if mask is None:
            m_ref, rest = None, rest
        else:
            m_ref, rest = rest[0], rest[1:]
        if select is None:
            (o_ref,) = rest
        else:
            s_ref, o_ref = rest
        b_val = b_ref[b_row : b_row + fout, :]

        def row(r, carry):
            if flat:
                xs = x_ref[r * row_step : r * row_step + k_all, :]
            else:
                xs = x_ref[r : r + 7, :, :].reshape(k_all, n_in)
            z = jnp.dot(w_ref[...], xs, preferred_element_type=jnp.float32)
            m_row = None if m_ref is None else m_ref[r]
            for g in range(groups):
                base = g * shifts * fout
                acc = z[base : base + fout, 0:n_out]
                for s in range(1, shifts):
                    acc = acc + z[base + s * fout : base + (s + 1) * fout, s : s + n_out]
                acc = acc + b_val
                if relu:
                    acc = jnp.maximum(acc, 0.0)
                if m_row is not None:
                    acc = acc * m_row[g : g + 1, :]
                acc = acc.astype(jnp.bfloat16)
                if rows_inner:
                    o_ref[g * fout : (g + 1) * fout, r : r + 1, :] = acc[:, None, :]
                    continue
                if select is None:
                    o_ref[r, g * fout : (g + 1) * fout, :] = acc
                    continue
                for k in range(pl.cdiv(n_out, LANE_BLOCK // 2)):
                    lo = k * (LANE_BLOCK // 2)
                    width = min(LANE_BLOCK // 2, n_out - lo)
                    n_u = pl.cdiv(width, PH)
                    y = jnp.dot(acc[:, lo : lo + width], s_ref[0:width, :], preferred_element_type=jnp.float32)
                    seg = LANE_BLOCK // 2 // PH
                    for p in range(PH):
                        o_ref[r, p * fout : (p + 1) * fout, lo // PH : lo // PH + n_u] = y[
                            :, p * seg : p * seg + n_u
                        ].astype(jnp.bfloat16)
            return carry

        for r in range(r_out):
            row(r, 0)

    def per_window(a):
        return pl.BlockSpec((None,) + a.shape[1:], lambda w, n=a.ndim - 1: (w,) + (0,) * n)

    def whole(a):
        return pl.BlockSpec(a.shape, lambda w, n=a.ndim: (0,) * n)

    args = [x, w_all, bias]
    specs = [per_window(x), whole(w_all), whole(bias)]
    if mask is not None:
        args.append(mask)
        specs.append(per_window(mask))
    if select is not None:
        args.append(select)
        specs.append(whole(select))
    return pl.pallas_call(
        kernel,
        grid=(windows,),
        in_specs=specs,
        out_specs=pl.BlockSpec((None,) + out_shape[1:], lambda w: (w, 0, 0, 0)),
        out_shape=jax.ShapeDtypeStruct(out_shape, jnp.bfloat16),
    )(*args)


def strain_layout(raw, left, right, rows):
    channels = raw.shape[1]
    cols = raw.shape[0] // PH
    n_out = WL + cols + WR

    def kernel(raw_ref, l_ref, r_ref, o_ref):
        ci = lax.broadcasted_iota(jnp.int32, (rows, channels), 1)
        ri = lax.broadcasted_iota(jnp.int32, (rows, channels), 0)
        nt = (((1,), (1,)), ((), ()))
        pieces = ((l_ref, 0, left.shape[0] // PH, left.shape[0] // PH - WL), (raw_ref, WL, cols, 0), (r_ref, WL + cols, WR, 0))
        for src, lo, n, skip in pieces:
            acc = None
            for q in range(PH):
                e = (ri == ci * PH + q).astype(jnp.float32)
                piece = src[pl.ds(q, n, stride=PH), :].astype(jnp.float32)
                y = lax.dot_general(e, piece, nt, preferred_element_type=jnp.float32)
                acc = y if acc is None else acc + y
            o_ref[:, lo : lo + n - skip] = acc[:, skip:].astype(o_ref.dtype)

    return pl.pallas_call(kernel, out_shape=jax.ShapeDtypeStruct((rows, n_out), jnp.bfloat16))(raw, left, right)


def weights_stride1(w):
    fout, fin = w.shape[:2]
    return jnp.transpose(w, (3, 0, 2, 1)).reshape(7 * fout, 7 * fin)


def weights_stride4(w, shifts, lag):
    fout, fin = w.shape[:2]
    s = np.arange(shifts)[:, None]
    p = np.arange(PH)[None, :]
    b = 4 * s + p - lag
    ok = (b >= 0) & (b <= 6)
    taps = jnp.take(w, np.clip(b, 0, 6).reshape(-1), axis=3).reshape(fout, fin, 7, shifts, PH)
    taps = jnp.where(ok[None, None, None], taps, jnp.zeros((), w.dtype))
    return jnp.transpose(taps, (3, 0, 2, 4, 1)).reshape(shifts * fout, 7 * PH * fin)


def weights_first(w):
    fout = w.shape[0]
    p = np.arange(PH)[:, None, None]
    dd = np.arange(4)[None, :, None]
    q = np.arange(PH)[None, None, :]
    b = 4 * (dd - 1) + q - p + 3
    ok = (b >= 0) & (b <= 6)
    taps = jnp.take(w[:, 0], np.clip(b, 0, 6).reshape(-1), axis=2).reshape(fout, 7, PH, 4, PH)
    taps = jnp.where(ok[None, None], taps, jnp.zeros((), w.dtype))
    return jnp.transpose(taps, (2, 3, 0, 1, 4)).reshape(PH * 4 * fout, 7 * PH)


def phase_select():
    block = LANE_BLOCK // 2
    seg = block // PH
    sel = np.zeros((block, block), np.float32)
    for p in range(PH):
        for u in range(seg):
            sel[PH * u + p, p * seg + u] = 1.0
    return jnp.asarray(sel, jnp.bfloat16)


def edge_mask(rows, groups, length, row0, time_of, block):
    t = lax.axis_index("tm")
    total_rows = lax.axis_size("chan") * C_DEV
    last = lax.axis_size("tm") - 1
    shape = (rows, groups, length)
    row = block * C_DEV + row0 + lax.broadcasted_iota(jnp.int32, shape, 0)
    tau, span = time_of(lax.broadcasted_iota(jnp.int32, shape, 1), lax.broadcasted_iota(jnp.int32, shape, 2))
    ok = (row >= 0) & (row < total_rows)
    ok = ok & ((t > 0) | (tau >= 0)) & ((t < last) | (tau < span))
    return ok.astype(jnp.float32)


def lower_layers(strain_wide, blocks_of, first_weight, biases, second_weight, times, length):
    wide = C_DEV + 2 * REACH
    n_win, n_s = strain_wide.shape[0], strain_wide.shape[-1]
    n_f = n_s - 3
    first_mask = jnp.stack(
        [
            edge_mask(wide - 6, PH, n_f, 3 - REACH, lambda p, v: (PH * (v - (WL - 1)) + p, times), b)
            for b in blocks_of
        ]
    )
    first = banded(
        strain_wide.reshape(n_win, wide * PH, n_s),
        first_weight,
        biases,
        0,
        first_mask,
        groups=PH,
        shifts=4,
        n_out=n_f,
        relu=True,
    )
    return banded(
        first,
        second_weight,
        biases,
        16,
        None,
        groups=1,
        shifts=3,
        n_out=length,
        relu=False,
    )


def on_device(
    recorded,
    partners,
    offsets,
    first_weight,
    first_bias,
    second_weight,
    second_bias,
    loop_weight,
    third_weight,
    third_bias,
    fourth_weight,
    fourth_bias,
):
    blocks = lax.axis_size("chan")
    me = lax.axis_index("chan")
    mate = partners[me]
    times_here, nc = recorded.shape
    wide = C_DEV + 2 * REACH
    padded = jnp.pad(recorded, ((0, 0), (REACH, 3 * C_DEV - REACH)))
    windows = jnp.concatenate(
        [padded[:, k * C_DEV : k * C_DEV + nc].reshape(times_here, blocks, C_DEV) for k in range(3)], axis=2
    )[:, :, :wide]
    tag = jnp.zeros((times_here, blocks, 1), recorded.dtype).at[0].set(offsets[0].astype(recorded.dtype))
    both = jnp.concatenate([windows, jnp.take(windows, partners, axis=1, mode="clip"), tag], axis=2)
    outgoing = jnp.transpose(both, (1, 0, 2))
    arrived = lax.all_to_all(outgoing, "chan", split_axis=0, concat_axis=0, tiled=True)
    biases = jnp.concatenate([first_bias, second_bias, third_bias, fourth_bias]).reshape(-1, 1)
    prepared = (
        weights_first(first_weight),
        weights_stride4(second_weight, 3, 2),
        weights_stride1(third_weight),
        weights_stride4(fourth_weight, 2, 0),
        biases,
    )
    quarter = blocks * times_here // 4
    length = quarter + 2 * LEAD
    n_t = length - 6
    masks = (
        edge_mask(C_DEV, 1, length, 0, lambda p, j: (j - LEAD, quarter), me),
        edge_mask(wide - 6, 1, n_t, 3 - REACH, lambda p, j: (j - (LEAD - 3), quarter), me),
    )
    arrived, prepared, masks = lax.optimization_barrier((arrived, prepared, masks))
    first_weight, second_weight, third_weight, fourth_weight, biases = prepared
    second_mask, third_mask = masks
    mate_offset = arrived[:, 0, 2 * wide].astype(jnp.int32)[mate]
    times = blocks * times_here
    tms = lax.axis_size("tm")
    up = [(i, i + 1) for i in range(tms - 1)]
    down = [(j, i) for i, j in up]
    before = lax.ppermute(arrived[blocks - 1], "tm", up)
    after = lax.ppermute(arrived[0, : PH * WR], "tm", down)
    strain_wide = strain_layout(arrived.reshape(times, -1), before, after, 2 * wide * PH)

    quarter = times // 4
    length = quarter + 2 * LEAD
    lower = lower_layers(
        strain_wide.reshape(2, wide, PH, -1), (me, mate), first_weight, biases, second_weight, times, length
    )
    pre_second, mate_second = lower[0], lower[1]

    own_offset = offsets[0]
    crossing = lax.dynamic_slice(mate_second, (mate_offset - 3, 0, 0), (7, F2, length))
    flipped = crossing[::-1]
    coupling = jnp.einsum("kof,kft->kot", loop_weight, flipped, preferred_element_type=jnp.float32)
    extra = lax.dynamic_update_slice(
        jnp.zeros((C_DEV, F2, length), jnp.float32), coupling, (own_offset - 3, 0, 0)
    )
    second = (jnp.maximum(pre_second.astype(jnp.float32) + extra, 0.0) * second_mask).astype(jnp.bfloat16)

    ring_up = [(i, i + 1) for i in range(blocks - 1)]
    ring_down = [(j, i) for i, j in ring_up]
    above = lax.ppermute(second[C_DEV - REACH :], "chan", ring_up)
    below = lax.ppermute(second[:REACH], "chan", ring_down)
    second_wide = jnp.concatenate([above, second, below], axis=0)

    n_t = length - 6
    n_sel = quarter // 4 + 1
    third = banded(
        second_wide[None],
        third_weight,
        biases,
        48,
        third_mask[None],
        groups=1,
        shifts=7,
        n_out=n_t,
        relu=True,
        select=phase_select(),
        n_sel=n_sel,
    )
    features = banded(
        third,
        fourth_weight,
        biases,
        80,
        None,
        groups=1,
        shifts=2,
        n_out=quarter // 4,
        relu=True,
        rows_inner=True,
    )
    return features[0]


def solution(mesh):
    return jax.shard_map(
        on_device,
        mesh=mesh,
        in_specs=(
            P(("tm", "chan"), None),
            P(),
            P("chan"),
            P(),
            P(),
            P(),
            P(),
            P(),
            P(),
            P(),
            P(),
            P(),
        ),
        out_specs=P(None, "chan", "tm"),
        check_vma=False,
    )
```

```python
import numpy as np
import jax
import jax.numpy as jnp
from jax import lax
from jax.experimental import pallas as pl
from jax.sharding import PartitionSpec as P

F2 = 32
C_DEV = 8
REACH = 6
PH = 4
WL = 7
WR = 8
LEAD = 5
LANE_BLOCK = 256


def banded(x, w_all, bias, b_row, mask, *, groups, shifts, n_out, relu, select=None, n_sel=0, rows_inner=False):
    windows = x.shape[0]
    flat = x.ndim == 3
    k_all = w_all.shape[1]
    row_step = k_all // 7
    r_out = (x.shape[1] // row_step if flat else x.shape[1]) - 6
    n_in = x.shape[-1]
    fout = w_all.shape[0] // (groups * shifts)
    if rows_inner:
        out_shape = (windows, groups * fout, r_out, n_out)
    elif select is None:
        out_shape = (windows, r_out, groups * fout, n_out)
    else:
        out_shape = (windows, r_out, PH * fout, n_sel)

    def kernel(x_ref, w_ref, b_ref, *rest):
        if mask is None:
            m_ref, rest = None, rest
        else:
            m_ref, rest = rest[0], rest[1:]
        if select is None:
            (o_ref,) = rest
        else:
            s_ref, o_ref = rest
        b_val = b_ref[b_row : b_row + fout, :]

        def row(r, carry):
            if flat:
                xs = x_ref[r * row_step : r * row_step + k_all, :]
            else:
                xs = x_ref[r : r + 7, :, :].reshape(k_all, n_in)
            z = jnp.dot(w_ref[...], xs, preferred_element_type=jnp.float32)
            m_row = None if m_ref is None else m_ref[r]
            for g in range(groups):
                base = g * shifts * fout
                acc = z[base : base + fout, 0:n_out]
                for s in range(1, shifts):
                    acc = acc + z[base + s * fout : base + (s + 1) * fout, s : s + n_out]
                acc = acc + b_val
                if relu:
                    acc = jnp.maximum(acc, 0.0)
                if m_row is not None:
                    acc = acc * m_row[g : g + 1, :]
                acc = acc.astype(jnp.bfloat16)
                if rows_inner:
                    o_ref[g * fout : (g + 1) * fout, r : r + 1, :] = acc[:, None, :]
                    continue
                if select is None:
                    o_ref[r, g * fout : (g + 1) * fout, :] = acc
                    continue
                for k in range(pl.cdiv(n_out, LANE_BLOCK // 2)):
                    lo = k * (LANE_BLOCK // 2)
                    width = min(LANE_BLOCK // 2, n_out - lo)
                    n_u = pl.cdiv(width, PH)
                    y = jnp.dot(acc[:, lo : lo + width], s_ref[0:width, :], preferred_element_type=jnp.float32)
                    seg = LANE_BLOCK // 2 // PH
                    for p in range(PH):
                        o_ref[r, p * fout : (p + 1) * fout, lo // PH : lo // PH + n_u] = y[
                            :, p * seg : p * seg + n_u
                        ].astype(jnp.bfloat16)
            return carry

        for r in range(r_out):
            row(r, 0)

    def per_window(a):
        return pl.BlockSpec((None,) + a.shape[1:], lambda w, n=a.ndim - 1: (w,) + (0,) * n)

    def whole(a):
        return pl.BlockSpec(a.shape, lambda w, n=a.ndim: (0,) * n)

    args = [x, w_all, bias]
    specs = [per_window(x), whole(w_all), whole(bias)]
    if mask is not None:
        args.append(mask)
        specs.append(per_window(mask))
    if select is not None:
        args.append(select)
        specs.append(whole(select))
    return pl.pallas_call(
        kernel,
        grid=(windows,),
        in_specs=specs,
        out_specs=pl.BlockSpec((None,) + out_shape[1:], lambda w: (w, 0, 0, 0)),
        out_shape=jax.ShapeDtypeStruct(out_shape, jnp.bfloat16),
    )(*args)


def strain_layout(arrived, rows):
    blocks, span, channels = arrived.shape
    here = span // 3
    per = here // PH
    cols = blocks * per
    n_out = WL + cols + WR

    def kernel(a_ref, o_ref):
        ci = lax.broadcasted_iota(jnp.int32, (rows, channels), 1)
        ri = lax.broadcasted_iota(jnp.int32, (rows, channels), 0)
        nt = (((1,), (1,)), ((), ()))
        picks = (
            (lambda q: a_ref[blocks - 1, pl.ds(here + q, per, stride=PH), :], 0, per - WL),
            (lambda q: a_ref[:, pl.ds(q, per, stride=PH), :].astype(jnp.float32).reshape(cols, channels), WL, 0),
            (lambda q: a_ref[0, pl.ds(2 * here + q, per, stride=PH), :], WL + cols, per - WR),
        )
        for take, lo, skip in picks:
            acc = None
            for q in range(PH):
                e = (ri == ci * PH + q).astype(jnp.float32)
                piece = take(q).astype(jnp.float32)
                y = lax.dot_general(e, piece, nt, preferred_element_type=jnp.float32)
                acc = y if acc is None else acc + y
            width = acc.shape[1] - skip
            if lo == 0:
                o_ref[:, 0:width] = acc[:, skip:].astype(o_ref.dtype)
            else:
                o_ref[:, lo : lo + width] = acc[:, :width].astype(o_ref.dtype)

    return pl.pallas_call(kernel, out_shape=jax.ShapeDtypeStruct((rows, n_out), jnp.bfloat16))(arrived)


def weights_stride1(w):
    fout, fin = w.shape[:2]
    return jnp.transpose(w, (3, 0, 2, 1)).reshape(7 * fout, 7 * fin)


def weights_stride4(w, shifts, lag):
    fout, fin = w.shape[:2]
    s = np.arange(shifts)[:, None]
    p = np.arange(PH)[None, :]
    b = 4 * s + p - lag
    ok = (b >= 0) & (b <= 6)
    taps = jnp.take(w, np.clip(b, 0, 6).reshape(-1), axis=3).reshape(fout, fin, 7, shifts, PH)
    taps = jnp.where(ok[None, None, None], taps, jnp.zeros((), w.dtype))
    return jnp.transpose(taps, (3, 0, 2, 4, 1)).reshape(shifts * fout, 7 * PH * fin)


def weights_first(w):
    fout = w.shape[0]
    p = np.arange(PH)[:, None, None]
    dd = np.arange(4)[None, :, None]
    q = np.arange(PH)[None, None, :]
    b = 4 * (dd - 1) + q - p + 3
    ok = (b >= 0) & (b <= 6)
    taps = jnp.take(w[:, 0], np.clip(b, 0, 6).reshape(-1), axis=2).reshape(fout, 7, PH, 4, PH)
    taps = jnp.where(ok[None, None], taps, jnp.zeros((), w.dtype))
    return jnp.transpose(taps, (2, 3, 0, 1, 4)).reshape(PH * 4 * fout, 7 * PH)


def phase_select():
    block = LANE_BLOCK // 2
    seg = block // PH
    sel = np.zeros((block, block), np.float32)
    for p in range(PH):
        for u in range(seg):
            sel[PH * u + p, p * seg + u] = 1.0
    return jnp.asarray(sel, jnp.bfloat16)


def edge_mask(rows, groups, length, row0, time_of, block):
    t = lax.axis_index("tm")
    total_rows = lax.axis_size("chan") * C_DEV
    last = lax.axis_size("tm") - 1
    shape = (rows, groups, length)
    row = block * C_DEV + row0 + lax.broadcasted_iota(jnp.int32, shape, 0)
    tau, span = time_of(lax.broadcasted_iota(jnp.int32, shape, 1), lax.broadcasted_iota(jnp.int32, shape, 2))
    ok = (row >= 0) & (row < total_rows)
    ok = ok & ((t > 0) | (tau >= 0)) & ((t < last) | (tau < span))
    return ok.astype(jnp.float32)


def lower_layers(strain_wide, blocks_of, first_weight, biases, second_weight, times, length):
    wide = C_DEV + 2 * REACH
    n_win, n_s = strain_wide.shape[0], strain_wide.shape[-1]
    n_f = n_s - 3
    first_mask = jnp.stack(
        [
            edge_mask(wide - 6, PH, n_f, 3 - REACH, lambda p, v: (PH * (v - (WL - 1)) + p, times), b)
            for b in blocks_of
        ]
    )
    first = banded(
        strain_wide.reshape(n_win, wide * PH, n_s),
        first_weight,
        biases,
        0,
        first_mask,
        groups=PH,
        shifts=4,
        n_out=n_f,
        relu=True,
    )
    return banded(
        first,
        second_weight,
        biases,
        16,
        None,
        groups=1,
        shifts=3,
        n_out=length,
        relu=False,
    )


def on_device(
    recorded,
    partners,
    offsets,
    first_weight,
    first_bias,
    second_weight,
    second_bias,
    loop_weight,
    third_weight,
    third_bias,
    fourth_weight,
    fourth_bias,
):
    blocks = lax.axis_size("chan")
    me = lax.axis_index("chan")
    mate = partners[me]
    times_here, nc = recorded.shape
    wide = C_DEV + 2 * REACH
    tms = lax.axis_size("tm")
    up = [(i, i + 1) for i in range(tms - 1)]
    down = [(j, i) for i, j in up]
    spread = jnp.concatenate([recorded, lax.ppermute(recorded, "tm", up), lax.ppermute(recorded, "tm", down)])
    padded = jnp.pad(spread, ((0, 0), (REACH, 3 * C_DEV - REACH)))
    windows = jnp.concatenate(
        [padded[:, k * C_DEV : k * C_DEV + nc].reshape(3 * times_here, blocks, C_DEV) for k in range(3)], axis=2
    )[:, :, :wide]
    tag = jnp.zeros((3 * times_here, blocks, 1), recorded.dtype).at[0].set(offsets[0].astype(recorded.dtype))
    both = jnp.concatenate([windows, jnp.take(windows, partners, axis=1, mode="clip"), tag], axis=2)
    outgoing = jnp.transpose(both, (1, 0, 2))
    arrived = lax.all_to_all(outgoing, "chan", split_axis=0, concat_axis=0, tiled=True)
    biases = jnp.concatenate([first_bias, second_bias, third_bias, fourth_bias]).reshape(-1, 1)
    prepared = (
        weights_first(first_weight),
        weights_stride4(second_weight, 3, 2),
        weights_stride1(third_weight),
        weights_stride4(fourth_weight, 2, 0),
        biases,
    )
    quarter = blocks * times_here // 4
    length = quarter + 2 * LEAD
    n_t = length - 6
    masks = (
        edge_mask(C_DEV, 1, length, 0, lambda p, j: (j - LEAD, quarter), me),
        edge_mask(wide - 6, 1, n_t, 3 - REACH, lambda p, j: (j - (LEAD - 3), quarter), me),
    )
    arrived, prepared, masks = lax.optimization_barrier((arrived, prepared, masks))
    first_weight, second_weight, third_weight, fourth_weight, biases = prepared
    second_mask, third_mask = masks
    mate_offset = arrived[:, 0, 2 * wide].astype(jnp.int32)[mate]
    times = blocks * times_here
    strain_wide = strain_layout(arrived, 2 * wide * PH)

    quarter = times // 4
    length = quarter + 2 * LEAD
    lower = lower_layers(
        strain_wide.reshape(2, wide, PH, -1), (me, mate), first_weight, biases, second_weight, times, length
    )
    pre_second, mate_second = lower[0], lower[1]

    own_offset = offsets[0]
    crossing = lax.dynamic_slice(mate_second, (mate_offset - 3, 0, 0), (7, F2, length))
    flipped = crossing[::-1]
    coupling = jnp.einsum("kof,kft->kot", loop_weight, flipped, preferred_element_type=jnp.float32)
    extra = lax.dynamic_update_slice(
        jnp.zeros((C_DEV, F2, length), jnp.float32), coupling, (own_offset - 3, 0, 0)
    )
    second = (jnp.maximum(pre_second.astype(jnp.float32) + extra, 0.0) * second_mask).astype(jnp.bfloat16)

    ring_up = [(i, i + 1) for i in range(blocks - 1)]
    ring_down = [(j, i) for i, j in ring_up]
    above = lax.ppermute(second[C_DEV - REACH :], "chan", ring_up)
    below = lax.ppermute(second[:REACH], "chan", ring_down)
    second_wide = jnp.concatenate([above, second, below], axis=0)

    n_t = length - 6
    n_sel = quarter // 4 + 1
    third = banded(
        second_wide[None],
        third_weight,
        biases,
        48,
        third_mask[None],
        groups=1,
        shifts=7,
        n_out=n_t,
        relu=True,
        select=phase_select(),
        n_sel=n_sel,
    )
    features = banded(
        third,
        fourth_weight,
        biases,
        80,
        None,
        groups=1,
        shifts=2,
        n_out=quarter // 4,
        relu=True,
        rows_inner=True,
    )
    return features[0]


def solution(mesh):
    return jax.shard_map(
        on_device,
        mesh=mesh,
        in_specs=(
            P(("tm", "chan"), None),
            P(),
            P("chan"),
            P(),
            P(),
            P(),
            P(),
            P(),
            P(),
            P(),
            P(),
            P(),
        ),
        out_specs=P(None, "chan", "tm"),
        check_vma=False,
    )
```

```python
import numpy as np
import jax
import jax.numpy as jnp
from jax import lax
from jax.experimental import pallas as pl
from jax.sharding import PartitionSpec as P

F2 = 32
C_DEV = 8
REACH = 6
PH = 4
WL = 7
WR = 8
LEAD = 5
LANE_BLOCK = 256


def banded(x, w_all, bias, b_row, mask, *, groups, shifts, n_out, relu, select=None, n_sel=0, rows_inner=False):
    windows = x.shape[0]
    flat = x.ndim == 3
    k_all = w_all.shape[1]
    row_step = k_all // 7
    r_out = (x.shape[1] // row_step if flat else x.shape[1]) - 6
    n_in = x.shape[-1]
    fout = w_all.shape[0] // (groups * shifts)
    if rows_inner:
        out_shape = (windows, groups * fout, r_out, n_out)
    elif select is None:
        out_shape = (windows, r_out, groups * fout, n_out)
    else:
        out_shape = (windows, r_out, PH * fout, n_sel)

    def kernel(x_ref, w_ref, b_ref, *rest):
        if mask is None:
            m_ref, rest = None, rest
        else:
            m_ref, rest = rest[0], rest[1:]
        if select is None:
            (o_ref,) = rest
        else:
            s_ref, o_ref = rest
        b_val = b_ref[b_row : b_row + fout, :]

        def row(r, carry):
            if flat:
                xs = x_ref[r * row_step : r * row_step + k_all, :]
            else:
                xs = x_ref[r : r + 7, :, :].reshape(k_all, n_in)
            z = jnp.dot(w_ref[...], xs, preferred_element_type=jnp.float32)
            m_row = None if m_ref is None else m_ref[r]
            for g in range(groups):
                base = g * shifts * fout
                acc = z[base : base + fout, 0:n_out]
                for s in range(1, shifts):
                    acc = acc + z[base + s * fout : base + (s + 1) * fout, s : s + n_out]
                acc = acc + b_val
                if relu:
                    acc = jnp.maximum(acc, 0.0)
                if m_row is not None:
                    acc = acc * m_row[g : g + 1, :]
                acc = acc.astype(jnp.bfloat16)
                if rows_inner:
                    o_ref[g * fout : (g + 1) * fout, r : r + 1, :] = acc[:, None, :]
                    continue
                if select is None:
                    o_ref[r, g * fout : (g + 1) * fout, :] = acc
                    continue
                for k in range(pl.cdiv(n_out, LANE_BLOCK // 2)):
                    lo = k * (LANE_BLOCK // 2)
                    width = min(LANE_BLOCK // 2, n_out - lo)
                    n_u = pl.cdiv(width, PH)
                    y = jnp.dot(acc[:, lo : lo + width], s_ref[0:width, :], preferred_element_type=jnp.float32)
                    seg = LANE_BLOCK // 2 // PH
                    for p in range(PH):
                        o_ref[r, p * fout : (p + 1) * fout, lo // PH : lo // PH + n_u] = y[
                            :, p * seg : p * seg + n_u
                        ].astype(jnp.bfloat16)
            return carry

        for r in range(r_out):
            row(r, 0)

    def per_window(a):
        return pl.BlockSpec((None,) + a.shape[1:], lambda w, n=a.ndim - 1: (w,) + (0,) * n)

    def whole(a):
        return pl.BlockSpec(a.shape, lambda w, n=a.ndim: (0,) * n)

    args = [x, w_all, bias]
    specs = [per_window(x), whole(w_all), whole(bias)]
    if mask is not None:
        args.append(mask)
        specs.append(per_window(mask))
    if select is not None:
        args.append(select)
        specs.append(whole(select))
    return pl.pallas_call(
        kernel,
        grid=(windows,),
        in_specs=specs,
        out_specs=pl.BlockSpec((None,) + out_shape[1:], lambda w: (w, 0, 0, 0)),
        out_shape=jax.ShapeDtypeStruct(out_shape, jnp.bfloat16),
    )(*args)


def strain_layout(raw, left, right, rows):
    channels = raw.shape[1]
    cols = raw.shape[0] // PH
    n_out = WL + cols + WR

    def kernel(raw_ref, l_ref, r_ref, o_ref):
        ci = lax.broadcasted_iota(jnp.int32, (rows, channels), 1)
        ri = lax.broadcasted_iota(jnp.int32, (rows, channels), 0)
        nt = (((1,), (1,)), ((), ()))
        pieces = ((l_ref, 0, left.shape[0] // PH, left.shape[0] // PH - WL), (raw_ref, WL, cols, 0), (r_ref, WL + cols, WR, 0))
        for src, lo, n, skip in pieces:
            acc = None
            for q in range(PH):
                e = (ri == ci * PH + q).astype(jnp.float32)
                piece = src[pl.ds(q, n, stride=PH), :].astype(jnp.float32)
                y = lax.dot_general(e, piece, nt, preferred_element_type=jnp.float32)
                acc = y if acc is None else acc + y
            o_ref[:, lo : lo + n - skip] = acc[:, skip:].astype(o_ref.dtype)

    return pl.pallas_call(kernel, out_shape=jax.ShapeDtypeStruct((rows, n_out), jnp.bfloat16))(raw, left, right)


def settled(arrays):
    n = len(arrays)

    def kernel(*refs):
        for src_ref, dst_ref in zip(refs[:n], refs[n:]):
            dst_ref[...] = src_ref[...]

    return pl.pallas_call(kernel, out_shape=tuple(jax.ShapeDtypeStruct(a.shape, a.dtype) for a in arrays))(*arrays)


def weights_stride1(w):
    fout, fin = w.shape[:2]
    return jnp.transpose(w, (3, 0, 2, 1)).reshape(7 * fout, 7 * fin)


def weights_stride4(w, shifts, lag):
    fout, fin = w.shape[:2]
    s = np.arange(shifts)[:, None]
    p = np.arange(PH)[None, :]
    b = 4 * s + p - lag
    ok = (b >= 0) & (b <= 6)
    taps = jnp.take(w, np.clip(b, 0, 6).reshape(-1), axis=3).reshape(fout, fin, 7, shifts, PH)
    taps = jnp.where(ok[None, None, None], taps, jnp.zeros((), w.dtype))
    return jnp.transpose(taps, (3, 0, 2, 4, 1)).reshape(shifts * fout, 7 * PH * fin)


def weights_first(w):
    fout = w.shape[0]
    p = np.arange(PH)[:, None, None]
    dd = np.arange(4)[None, :, None]
    q = np.arange(PH)[None, None, :]
    b = 4 * (dd - 1) + q - p + 3
    ok = (b >= 0) & (b <= 6)
    taps = jnp.take(w[:, 0], np.clip(b, 0, 6).reshape(-1), axis=2).reshape(fout, 7, PH, 4, PH)
    taps = jnp.where(ok[None, None], taps, jnp.zeros((), w.dtype))
    return jnp.transpose(taps, (2, 3, 0, 1, 4)).reshape(PH * 4 * fout, 7 * PH)


def phase_select():
    block = LANE_BLOCK // 2
    seg = block // PH
    sel = np.zeros((block, block), np.float32)
    for p in range(PH):
        for u in range(seg):
            sel[PH * u + p, p * seg + u] = 1.0
    return jnp.asarray(sel, jnp.bfloat16)


def edge_mask(rows, groups, length, row0, time_of, block):
    t = lax.axis_index("tm")
    total_rows = lax.axis_size("chan") * C_DEV
    last = lax.axis_size("tm") - 1
    shape = (rows, groups, length)
    row = block * C_DEV + row0 + lax.broadcasted_iota(jnp.int32, shape, 0)
    tau, span = time_of(lax.broadcasted_iota(jnp.int32, shape, 1), lax.broadcasted_iota(jnp.int32, shape, 2))
    ok = (row >= 0) & (row < total_rows)
    ok = ok & ((t > 0) | (tau >= 0)) & ((t < last) | (tau < span))
    return ok.astype(jnp.float32)


def lower_layers(strain_wide, blocks_of, first_weight, biases, second_weight, times, length):
    wide = C_DEV + 2 * REACH
    n_win, n_s = strain_wide.shape[0], strain_wide.shape[-1]
    n_f = n_s - 3
    first_mask = jnp.stack(
        [
            edge_mask(wide - 6, PH, n_f, 3 - REACH, lambda p, v: (PH * (v - (WL - 1)) + p, times), b)
            for b in blocks_of
        ]
    )
    first = banded(
        strain_wide.reshape(n_win, wide * PH, n_s),
        first_weight,
        biases,
        0,
        first_mask,
        groups=PH,
        shifts=4,
        n_out=n_f,
        relu=True,
    )
    return banded(
        first,
        second_weight,
        biases,
        16,
        None,
        groups=1,
        shifts=3,
        n_out=length,
        relu=False,
    )


def on_device(
    recorded,
    partners,
    offsets,
    first_weight,
    first_bias,
    second_weight,
    second_bias,
    loop_weight,
    third_weight,
    third_bias,
    fourth_weight,
    fourth_bias,
):
    blocks = lax.axis_size("chan")
    me = lax.axis_index("chan")
    mate = partners[me]
    times_here, nc = recorded.shape
    wide = C_DEV + 2 * REACH
    padded = jnp.pad(recorded, ((0, 0), (REACH, 3 * C_DEV - REACH)))
    windows = jnp.concatenate(
        [padded[:, k * C_DEV : k * C_DEV + nc].reshape(times_here, blocks, C_DEV) for k in range(3)], axis=2
    )[:, :, :wide]
    tag = jnp.zeros((times_here, blocks, 1), recorded.dtype).at[0].set(offsets[0].astype(recorded.dtype))
    both = jnp.concatenate([windows, jnp.take(windows, partners, axis=1, mode="clip"), tag], axis=2)
    outgoing = jnp.transpose(both, (1, 0, 2))
    arrived = lax.all_to_all(outgoing, "chan", split_axis=0, concat_axis=0, tiled=True)
    biases = jnp.concatenate([first_bias, second_bias, third_bias, fourth_bias]).reshape(-1, 1)
    prepared = (
        weights_first(first_weight),
        weights_stride4(second_weight, 3, 2),
        weights_stride1(third_weight),
        weights_stride4(fourth_weight, 2, 0),
        biases,
    )
    quarter = blocks * times_here // 4
    length = quarter + 2 * LEAD
    n_t = length - 6
    masks = (
        edge_mask(C_DEV, 1, length, 0, lambda p, j: (j - LEAD, quarter), me),
        edge_mask(wide - 6, 1, n_t, 3 - REACH, lambda p, j: (j - (LEAD - 3), quarter), me),
    )
    prepared = settled(prepared)
    arrived, prepared, masks = lax.optimization_barrier((arrived, prepared, masks))
    first_weight, second_weight, third_weight, fourth_weight, biases = prepared
    second_mask, third_mask = masks
    mate_offset = arrived[:, 0, 2 * wide].astype(jnp.int32)[mate]
    times = blocks * times_here
    tms = lax.axis_size("tm")
    up = [(i, i + 1) for i in range(tms - 1)]
    down = [(j, i) for i, j in up]
    before = lax.ppermute(arrived[blocks - 1], "tm", up)
    after = lax.ppermute(arrived[0, : PH * WR], "tm", down)
    strain_wide = strain_layout(arrived.reshape(times, -1), before, after, 2 * wide * PH)

    quarter = times // 4
    length = quarter + 2 * LEAD
    lower = lower_layers(
        strain_wide.reshape(2, wide, PH, -1), (me, mate), first_weight, biases, second_weight, times, length
    )
    pre_second, mate_second = lower[0], lower[1]

    own_offset = offsets[0]
    crossing = lax.dynamic_slice(mate_second, (mate_offset - 3, 0, 0), (7, F2, length))
    flipped = crossing[::-1]
    coupling = jnp.einsum("kof,kft->kot", loop_weight, flipped, preferred_element_type=jnp.float32)
    extra = lax.dynamic_update_slice(
        jnp.zeros((C_DEV, F2, length), jnp.float32), coupling, (own_offset - 3, 0, 0)
    )
    second = (jnp.maximum(pre_second.astype(jnp.float32) + extra, 0.0) * second_mask).astype(jnp.bfloat16)

    ring_up = [(i, i + 1) for i in range(blocks - 1)]
    ring_down = [(j, i) for i, j in ring_up]
    above = lax.ppermute(second[C_DEV - REACH :], "chan", ring_up)
    below = lax.ppermute(second[:REACH], "chan", ring_down)
    second_wide = jnp.concatenate([above, second, below], axis=0)

    n_t = length - 6
    n_sel = quarter // 4 + 1
    third = banded(
        second_wide[None],
        third_weight,
        biases,
        48,
        third_mask[None],
        groups=1,
        shifts=7,
        n_out=n_t,
        relu=True,
        select=phase_select(),
        n_sel=n_sel,
    )
    features = banded(
        third,
        fourth_weight,
        biases,
        80,
        None,
        groups=1,
        shifts=2,
        n_out=quarter // 4,
        relu=True,
        rows_inner=True,
    )
    return features[0]


def solution(mesh):
    return jax.shard_map(
        on_device,
        mesh=mesh,
        in_specs=(
            P(("tm", "chan"), None),
            P(),
            P("chan"),
            P(),
            P(),
            P(),
            P(),
            P(),
            P(),
            P(),
            P(),
            P(),
        ),
        out_specs=P(None, "chan", "tm"),
        check_vma=False,
    )
```

```python
import numpy as np
import jax
import jax.numpy as jnp
from jax import lax
from jax.experimental import pallas as pl
from jax.sharding import PartitionSpec as P

F2 = 32
C_DEV = 8
REACH = 6
PH = 4
WL = 7
WR = 8
LEAD = 5
LANE_BLOCK = 256


def banded(x, w_all, bias, b_row, mask, *, groups, shifts, n_out, relu, select=None, n_sel=0, rows_inner=False):
    windows = x.shape[0]
    flat = x.ndim == 3
    k_all = w_all.shape[1]
    row_step = k_all // 7
    r_out = (x.shape[1] // row_step if flat else x.shape[1]) - 6
    n_in = x.shape[-1]
    fout = w_all.shape[0] // (groups * shifts)
    if rows_inner:
        out_shape = (windows, groups * fout, r_out, n_out)
    elif select is None:
        out_shape = (windows, r_out, groups * fout, n_out)
    else:
        out_shape = (windows, r_out, PH * fout, n_sel)

    def kernel(x_ref, w_ref, b_ref, *rest):
        if mask is None:
            m_ref, rest = None, rest
        else:
            m_ref, rest = rest[0], rest[1:]
        if select is None:
            (o_ref,) = rest
        else:
            s_ref, o_ref = rest
        b_val = b_ref[b_row : b_row + fout, :]

        def row(r, carry):
            if flat:
                xs = x_ref[r * row_step : r * row_step + k_all, :]
            else:
                xs = x_ref[r : r + 7, :, :].reshape(k_all, n_in)
            z = jnp.dot(w_ref[...], xs, preferred_element_type=jnp.float32)
            m_row = None if m_ref is None else m_ref[r]
            for g in range(groups):
                base = g * shifts * fout
                acc = z[base : base + fout, 0:n_out]
                for s in range(1, shifts):
                    acc = acc + z[base + s * fout : base + (s + 1) * fout, s : s + n_out]
                acc = acc + b_val
                if relu:
                    acc = jnp.maximum(acc, 0.0)
                if m_row is not None:
                    acc = acc * m_row[g : g + 1, :]
                acc = acc.astype(jnp.bfloat16)
                if rows_inner:
                    o_ref[g * fout : (g + 1) * fout, r : r + 1, :] = acc[:, None, :]
                    continue
                if select is None:
                    o_ref[r, g * fout : (g + 1) * fout, :] = acc
                    continue
                for k in range(pl.cdiv(n_out, LANE_BLOCK // 2)):
                    lo = k * (LANE_BLOCK // 2)
                    width = min(LANE_BLOCK // 2, n_out - lo)
                    n_u = pl.cdiv(width, PH)
                    y = jnp.dot(acc[:, lo : lo + width], s_ref[0:width, :], preferred_element_type=jnp.float32)
                    seg = LANE_BLOCK // 2 // PH
                    for p in range(PH):
                        o_ref[r, p * fout : (p + 1) * fout, lo // PH : lo // PH + n_u] = y[
                            :, p * seg : p * seg + n_u
                        ].astype(jnp.bfloat16)
            return carry

        for r in range(r_out):
            row(r, 0)

    def per_window(a):
        return pl.BlockSpec((None,) + a.shape[1:], lambda w, n=a.ndim - 1: (w,) + (0,) * n)

    def whole(a):
        return pl.BlockSpec(a.shape, lambda w, n=a.ndim: (0,) * n)

    args = [x, w_all, bias]
    specs = [per_window(x), whole(w_all), whole(bias)]
    if mask is not None:
        args.append(mask)
        specs.append(per_window(mask))
    if select is not None:
        args.append(select)
        specs.append(whole(select))
    return pl.pallas_call(
        kernel,
        grid=(windows,),
        in_specs=specs,
        out_specs=pl.BlockSpec((None,) + out_shape[1:], lambda w: (w, 0, 0, 0)),
        out_shape=jax.ShapeDtypeStruct(out_shape, jnp.bfloat16),
    )(*args)


def strain_layout(raw, left, right, rows):
    channels = raw.shape[1]
    cols = raw.shape[0] // PH
    n_out = WL + cols + WR

    def kernel(raw_ref, l_ref, r_ref, o_ref):
        ci = lax.broadcasted_iota(jnp.int32, (rows, channels), 1)
        ri = lax.broadcasted_iota(jnp.int32, (rows, channels), 0)
        nt = (((1,), (1,)), ((), ()))
        pieces = ((l_ref, 0, left.shape[0] // PH, left.shape[0] // PH - WL), (raw_ref, WL, cols, 0), (r_ref, WL + cols, WR, 0))
        for src, lo, n, skip in pieces:
            acc = None
            for q in range(PH):
                e = (ri == ci * PH + q).astype(jnp.float32)
                piece = src[pl.ds(q, n, stride=PH), :].astype(jnp.float32)
                y = lax.dot_general(e, piece, nt, preferred_element_type=jnp.float32)
                acc = y if acc is None else acc + y
            o_ref[:, lo : lo + n - skip] = acc[:, skip:].astype(o_ref.dtype)

    return pl.pallas_call(kernel, out_shape=jax.ShapeDtypeStruct((rows, n_out), jnp.bfloat16))(raw, left, right)


def settled(arrays):
    n = len(arrays)

    def kernel(*refs):
        for src_ref, dst_ref in zip(refs[:n], refs[n:]):
            dst_ref[...] = src_ref[...]

    return pl.pallas_call(kernel, out_shape=tuple(jax.ShapeDtypeStruct(a.shape, a.dtype) for a in arrays))(*arrays)


def weights_stride1(w):
    fout, fin = w.shape[:2]
    return jnp.transpose(w, (3, 0, 2, 1)).reshape(7 * fout, 7 * fin)


def weights_stride4(w, shifts, lag):
    fout, fin = w.shape[:2]
    s = np.arange(shifts)[:, None]
    p = np.arange(PH)[None, :]
    b = 4 * s + p - lag
    ok = (b >= 0) & (b <= 6)
    taps = jnp.take(w, np.clip(b, 0, 6).reshape(-1), axis=3).reshape(fout, fin, 7, shifts, PH)
    taps = jnp.where(ok[None, None, None], taps, jnp.zeros((), w.dtype))
    return jnp.transpose(taps, (3, 0, 2, 4, 1)).reshape(shifts * fout, 7 * PH * fin)


def weights_first(w):
    fout = w.shape[0]
    p = np.arange(PH)[:, None, None]
    dd = np.arange(4)[None, :, None]
    q = np.arange(PH)[None, None, :]
    b = 4 * (dd - 1) + q - p + 3
    ok = (b >= 0) & (b <= 6)
    taps = jnp.take(w[:, 0], np.clip(b, 0, 6).reshape(-1), axis=2).reshape(fout, 7, PH, 4, PH)
    taps = jnp.where(ok[None, None], taps, jnp.zeros((), w.dtype))
    return jnp.transpose(taps, (2, 3, 0, 1, 4)).reshape(PH * 4 * fout, 7 * PH)


def phase_select():
    block = LANE_BLOCK // 2
    seg = block // PH
    sel = np.zeros((block, block), np.float32)
    for p in range(PH):
        for u in range(seg):
            sel[PH * u + p, p * seg + u] = 1.0
    return jnp.asarray(sel, jnp.bfloat16)


def edge_mask(rows, groups, length, row0, time_of, block):
    t = lax.axis_index("tm")
    total_rows = lax.axis_size("chan") * C_DEV
    last = lax.axis_size("tm") - 1
    shape = (rows, groups, length)
    row = block * C_DEV + row0 + lax.broadcasted_iota(jnp.int32, shape, 0)
    tau, span = time_of(lax.broadcasted_iota(jnp.int32, shape, 1), lax.broadcasted_iota(jnp.int32, shape, 2))
    ok = (row >= 0) & (row < total_rows)
    ok = ok & ((t > 0) | (tau >= 0)) & ((t < last) | (tau < span))
    return ok.astype(jnp.float32)


def lower_layers(strain_wide, first_mask, first_weight, biases, second_weight, length):
    wide = C_DEV + 2 * REACH
    n_win, n_s = strain_wide.shape[0], strain_wide.shape[-1]
    n_f = n_s - 3
    first = banded(
        strain_wide.reshape(n_win, wide * PH, n_s),
        first_weight,
        biases,
        0,
        first_mask,
        groups=PH,
        shifts=4,
        n_out=n_f,
        relu=True,
    )
    return banded(
        first,
        second_weight,
        biases,
        16,
        None,
        groups=1,
        shifts=3,
        n_out=length,
        relu=False,
    )


def on_device(
    recorded,
    partners,
    offsets,
    first_weight,
    first_bias,
    second_weight,
    second_bias,
    loop_weight,
    third_weight,
    third_bias,
    fourth_weight,
    fourth_bias,
):
    blocks = lax.axis_size("chan")
    me = lax.axis_index("chan")
    mate = partners[me]
    times_here, nc = recorded.shape
    wide = C_DEV + 2 * REACH
    padded = jnp.pad(recorded, ((0, 0), (REACH, 3 * C_DEV - REACH)))
    windows = jnp.concatenate(
        [padded[:, k * C_DEV : k * C_DEV + nc].reshape(times_here, blocks, C_DEV) for k in range(3)], axis=2
    )[:, :, :wide]
    tag = jnp.zeros((times_here, blocks, 1), recorded.dtype).at[0].set(offsets[0].astype(recorded.dtype))
    both = jnp.concatenate([windows, jnp.take(windows, partners, axis=1, mode="clip"), tag], axis=2)
    outgoing = jnp.transpose(both, (1, 0, 2))
    arrived = lax.all_to_all(outgoing, "chan", split_axis=0, concat_axis=0, tiled=True)
    biases = jnp.concatenate([first_bias, second_bias, third_bias, fourth_bias]).reshape(-1, 1)
    prepared = (
        weights_first(first_weight),
        weights_stride4(second_weight, 3, 2),
        weights_stride1(third_weight),
        weights_stride4(fourth_weight, 2, 0),
        biases,
    )
    quarter = blocks * times_here // 4
    length = quarter + 2 * LEAD
    n_t = length - 6
    n_f = WL + blocks * times_here // PH + WR - 3
    first_time = lambda p, v: (PH * (v - (WL - 1)) + p, blocks * times_here)
    masks = (
        jnp.stack([edge_mask(wide - 6, PH, n_f, 3 - REACH, first_time, b) for b in (me, mate)]),
        edge_mask(C_DEV, 1, length, 0, lambda p, j: (j - LEAD, quarter), me),
        edge_mask(wide - 6, 1, n_t, 3 - REACH, lambda p, j: (j - (LEAD - 3), quarter), me),
    )
    prepared = settled(prepared)
    arrived, prepared, masks = lax.optimization_barrier((arrived, prepared, masks))
    first_weight, second_weight, third_weight, fourth_weight, biases = prepared
    first_mask, second_mask, third_mask = masks
    mate_offset = arrived[:, 0, 2 * wide].astype(jnp.int32)[mate]
    times = blocks * times_here
    tms = lax.axis_size("tm")
    up = [(i, i + 1) for i in range(tms - 1)]
    down = [(j, i) for i, j in up]
    before = lax.ppermute(arrived[blocks - 1], "tm", up)
    after = lax.ppermute(arrived[0, : PH * WR], "tm", down)
    strain_wide = strain_layout(arrived.reshape(times, -1), before, after, 2 * wide * PH)

    quarter = times // 4
    length = quarter + 2 * LEAD
    lower = lower_layers(
        strain_wide.reshape(2, wide, PH, -1), first_mask, first_weight, biases, second_weight, length
    )
    pre_second, mate_second = lower[0], lower[1]

    own_offset = offsets[0]
    crossing = lax.dynamic_slice(mate_second, (mate_offset - 3, 0, 0), (7, F2, length))
    flipped = crossing[::-1]
    coupling = jnp.einsum("kof,kft->kot", loop_weight, flipped, preferred_element_type=jnp.float32)
    extra = lax.dynamic_update_slice(
        jnp.zeros((C_DEV, F2, length), jnp.float32), coupling, (own_offset - 3, 0, 0)
    )
    second = (jnp.maximum(pre_second.astype(jnp.float32) + extra, 0.0) * second_mask).astype(jnp.bfloat16)

    ring_up = [(i, i + 1) for i in range(blocks - 1)]
    ring_down = [(j, i) for i, j in ring_up]
    above = lax.ppermute(second[C_DEV - REACH :], "chan", ring_up)
    below = lax.ppermute(second[:REACH], "chan", ring_down)
    second_wide = jnp.concatenate([above, second, below], axis=0)

    n_t = length - 6
    n_sel = quarter // 4 + 1
    third = banded(
        second_wide[None],
        third_weight,
        biases,
        48,
        third_mask[None],
        groups=1,
        shifts=7,
        n_out=n_t,
        relu=True,
        select=phase_select(),
        n_sel=n_sel,
    )
    features = banded(
        third,
        fourth_weight,
        biases,
        80,
        None,
        groups=1,
        shifts=2,
        n_out=quarter // 4,
        relu=True,
        rows_inner=True,
    )
    return features[0]


def solution(mesh):
    return jax.shard_map(
        on_device,
        mesh=mesh,
        in_specs=(
            P(("tm", "chan"), None),
            P(),
            P("chan"),
            P(),
            P(),
            P(),
            P(),
            P(),
            P(),
            P(),
            P(),
            P(),
        ),
        out_specs=P(None, "chan", "tm"),
        check_vma=False,
    )
```

```python
import numpy as np
import jax
import jax.numpy as jnp
from jax import lax
from jax.experimental import pallas as pl
from jax.sharding import PartitionSpec as P

F2 = 32
C_DEV = 8
REACH = 6
PH = 4
WL = 7
WR = 8
LEAD = 5
LANE_BLOCK = 256


def banded(x, w_all, bias, b_row, mask, *, groups, shifts, n_out, relu, select=None, n_sel=0, rows_inner=False):
    windows = x.shape[0]
    flat = x.ndim == 3
    k_all = w_all.shape[1]
    row_step = k_all // 7
    r_out = (x.shape[1] // row_step if flat else x.shape[1]) - 6
    n_in = x.shape[-1]
    fout = w_all.shape[0] // (groups * shifts)
    if rows_inner:
        out_shape = (windows, groups * fout, r_out, n_out)
    elif select is None:
        out_shape = (windows, r_out, groups * fout, n_out)
    else:
        out_shape = (windows, r_out, PH * fout, n_sel)

    def kernel(x_ref, w_ref, b_ref, *rest):
        if mask is None:
            m_ref, rest = None, rest
        else:
            m_ref, rest = rest[0], rest[1:]
        if select is None:
            (o_ref,) = rest
        else:
            s_ref, o_ref = rest
        b_val = b_ref[b_row : b_row + fout, :]

        def row(r, carry):
            if flat:
                xs = x_ref[r * row_step : r * row_step + k_all, :]
            else:
                xs = x_ref[r : r + 7, :, :].reshape(k_all, n_in)
            z = jnp.dot(w_ref[...], xs, preferred_element_type=jnp.float32)
            m_row = None if m_ref is None else m_ref[r]
            for g in range(groups):
                base = g * shifts * fout
                acc = z[base : base + fout, 0:n_out]
                for s in range(1, shifts):
                    acc = acc + z[base + s * fout : base + (s + 1) * fout, s : s + n_out]
                acc = acc + b_val
                if relu:
                    acc = jnp.maximum(acc, 0.0)
                if m_row is not None:
                    acc = acc * m_row[g : g + 1, :]
                acc = acc.astype(jnp.bfloat16)
                if rows_inner:
                    o_ref[g * fout : (g + 1) * fout, r : r + 1, :] = acc[:, None, :]
                    continue
                if select is None:
                    o_ref[r, g * fout : (g + 1) * fout, :] = acc
                    continue
                for k in range(pl.cdiv(n_out, LANE_BLOCK // 2)):
                    lo = k * (LANE_BLOCK // 2)
                    width = min(LANE_BLOCK // 2, n_out - lo)
                    n_u = pl.cdiv(width, PH)
                    y = jnp.dot(acc[:, lo : lo + width], s_ref[0:width, :], preferred_element_type=jnp.float32)
                    seg = LANE_BLOCK // 2 // PH
                    for p in range(PH):
                        o_ref[r, p * fout : (p + 1) * fout, lo // PH : lo // PH + n_u] = y[
                            :, p * seg : p * seg + n_u
                        ].astype(jnp.bfloat16)
            return carry

        for r in range(r_out):
            row(r, 0)

    def per_window(a):
        return pl.BlockSpec((None,) + a.shape[1:], lambda w, n=a.ndim - 1: (w,) + (0,) * n)

    def whole(a):
        return pl.BlockSpec(a.shape, lambda w, n=a.ndim: (0,) * n)

    args = [x, w_all, bias]
    specs = [per_window(x), whole(w_all), whole(bias)]
    if mask is not None:
        args.append(mask)
        specs.append(per_window(mask))
    if select is not None:
        args.append(select)
        specs.append(whole(select))
    return pl.pallas_call(
        kernel,
        grid=(windows,),
        in_specs=specs,
        out_specs=pl.BlockSpec((None,) + out_shape[1:], lambda w: (w, 0, 0, 0)),
        out_shape=jax.ShapeDtypeStruct(out_shape, jnp.bfloat16),
    )(*args)


def strain_layout(raw, left, right, rows):
    channels = raw.shape[1]
    cols = raw.shape[0] // PH
    n_out = WL + cols + WR

    def kernel(raw_ref, l_ref, r_ref, o_ref):
        ci = lax.broadcasted_iota(jnp.int32, (rows, channels), 1)
        ri = lax.broadcasted_iota(jnp.int32, (rows, channels), 0)
        nt = (((1,), (1,)), ((), ()))
        pieces = ((l_ref, 0, left.shape[0] // PH, left.shape[0] // PH - WL), (raw_ref, WL, cols, 0), (r_ref, WL + cols, WR, 0))
        for src, lo, n, skip in pieces:
            acc = None
            for q in range(PH):
                e = (ri == ci * PH + q).astype(jnp.float32)
                piece = src[pl.ds(q, n, stride=PH), :].astype(jnp.float32)
                y = lax.dot_general(e, piece, nt, preferred_element_type=jnp.float32)
                acc = y if acc is None else acc + y
            o_ref[:, lo : lo + n - skip] = acc[:, skip:].astype(o_ref.dtype)

    return pl.pallas_call(kernel, out_shape=jax.ShapeDtypeStruct((rows, n_out), jnp.bfloat16))(raw, left, right)


def settled(arrays):
    n = len(arrays)

    def kernel(*refs):
        for src_ref, dst_ref in zip(refs[:n], refs[n:]):
            dst_ref[...] = src_ref[...]

    return pl.pallas_call(kernel, out_shape=tuple(jax.ShapeDtypeStruct(a.shape, a.dtype) for a in arrays))(*arrays)


def weights_stride1(w):
    fout, fin = w.shape[:2]
    return jnp.transpose(w, (3, 0, 2, 1)).reshape(7 * fout, 7 * fin)


def weights_stride4(w, shifts, lag):
    fout, fin = w.shape[:2]
    taps = jnp.pad(w, ((0, 0), (0, 0), (0, 0), (lag, shifts * PH - 7 - lag))).reshape(fout, fin, 7, shifts, PH)
    return jnp.transpose(taps, (3, 0, 2, 4, 1)).reshape(shifts * fout, 7 * PH * fin)


def weights_first(w):
    fout = w.shape[0]
    per_p = [jnp.pad(w[:, 0], ((0, 0), (0, 0), (p + 1, 8 - p))).reshape(fout, 7, 4, PH) for p in range(PH)]
    return jnp.transpose(jnp.stack(per_p), (0, 3, 1, 2, 4)).reshape(PH * 4 * fout, 7 * PH)


def phase_select():
    block = LANE_BLOCK // 2
    seg = block // PH
    sel = np.zeros((block, block), np.float32)
    for p in range(PH):
        for u in range(seg):
            sel[PH * u + p, p * seg + u] = 1.0
    return jnp.asarray(sel, jnp.bfloat16)


def edge_mask(rows, groups, length, row0, time_of, block):
    t = lax.axis_index("tm")
    total_rows = lax.axis_size("chan") * C_DEV
    last = lax.axis_size("tm") - 1
    shape = (rows, groups, length)
    row = block * C_DEV + row0 + lax.broadcasted_iota(jnp.int32, shape, 0)
    tau, span = time_of(lax.broadcasted_iota(jnp.int32, shape, 1), lax.broadcasted_iota(jnp.int32, shape, 2))
    ok = (row >= 0) & (row < total_rows)
    ok = ok & ((t > 0) | (tau >= 0)) & ((t < last) | (tau < span))
    return ok.astype(jnp.float32)


def lower_layers(strain_wide, first_mask, first_weight, biases, second_weight, length):
    wide = C_DEV + 2 * REACH
    n_win, n_s = strain_wide.shape[0], strain_wide.shape[-1]
    n_f = n_s - 3
    first = banded(
        strain_wide.reshape(n_win, wide * PH, n_s),
        first_weight,
        biases,
        0,
        first_mask,
        groups=PH,
        shifts=4,
        n_out=n_f,
        relu=True,
    )
    return banded(
        first,
        second_weight,
        biases,
        16,
        None,
        groups=1,
        shifts=3,
        n_out=length,
        relu=False,
    )


def on_device(
    recorded,
    partners,
    offsets,
    first_weight,
    first_bias,
    second_weight,
    second_bias,
    loop_weight,
    third_weight,
    third_bias,
    fourth_weight,
    fourth_bias,
):
    blocks = lax.axis_size("chan")
    me = lax.axis_index("chan")
    mate = partners[me]
    times_here, nc = recorded.shape
    wide = C_DEV + 2 * REACH
    padded = jnp.pad(recorded, ((0, 0), (REACH, 3 * C_DEV - REACH)))
    windows = jnp.concatenate(
        [padded[:, k * C_DEV : k * C_DEV + nc].reshape(times_here, blocks, C_DEV) for k in range(3)], axis=2
    )[:, :, :wide]
    tag = jnp.zeros((times_here, blocks, 1), recorded.dtype).at[0].set(offsets[0].astype(recorded.dtype))
    both = jnp.concatenate([windows, jnp.take(windows, partners, axis=1, mode="clip"), tag], axis=2)
    outgoing = jnp.transpose(both, (1, 0, 2))
    arrived = lax.all_to_all(outgoing, "chan", split_axis=0, concat_axis=0, tiled=True)
    biases = jnp.concatenate([first_bias, second_bias, third_bias, fourth_bias]).reshape(-1, 1)
    prepared = (
        weights_first(first_weight),
        weights_stride4(second_weight, 3, 2),
        weights_stride1(third_weight),
        weights_stride4(fourth_weight, 2, 0),
        biases,
    )
    quarter = blocks * times_here // 4
    length = quarter + 2 * LEAD
    n_t = length - 6
    n_f = WL + blocks * times_here // PH + WR - 3
    first_time = lambda p, v: (PH * (v - (WL - 1)) + p, blocks * times_here)
    masks = (
        jnp.stack([edge_mask(wide - 6, PH, n_f, 3 - REACH, first_time, b) for b in (me, mate)]),
        edge_mask(C_DEV, 1, length, 0, lambda p, j: (j - LEAD, quarter), me),
        edge_mask(wide - 6, 1, n_t, 3 - REACH, lambda p, j: (j - (LEAD - 3), quarter), me),
    )
    prepared = settled(prepared)
    arrived, prepared, masks = lax.optimization_barrier((arrived, prepared, masks))
    first_weight, second_weight, third_weight, fourth_weight, biases = prepared
    first_mask, second_mask, third_mask = masks
    mate_offset = arrived[:, 0, 2 * wide].astype(jnp.int32)[mate]
    times = blocks * times_here
    tms = lax.axis_size("tm")
    up = [(i, i + 1) for i in range(tms - 1)]
    down = [(j, i) for i, j in up]
    before = lax.ppermute(arrived[blocks - 1], "tm", up)
    after = lax.ppermute(arrived[0, : PH * WR], "tm", down)
    strain_wide = strain_layout(arrived.reshape(times, -1), before, after, 2 * wide * PH)

    quarter = times // 4
    length = quarter + 2 * LEAD
    lower = lower_layers(
        strain_wide.reshape(2, wide, PH, -1), first_mask, first_weight, biases, second_weight, length
    )
    pre_second, mate_second = lower[0], lower[1]

    own_offset = offsets[0]
    crossing = lax.dynamic_slice(mate_second, (mate_offset - 3, 0, 0), (7, F2, length))
    flipped = crossing[::-1]
    coupling = jnp.einsum("kof,kft->kot", loop_weight, flipped, preferred_element_type=jnp.float32)
    extra = lax.dynamic_update_slice(
        jnp.zeros((C_DEV, F2, length), jnp.float32), coupling, (own_offset - 3, 0, 0)
    )
    second = (jnp.maximum(pre_second.astype(jnp.float32) + extra, 0.0) * second_mask).astype(jnp.bfloat16)

    ring_up = [(i, i + 1) for i in range(blocks - 1)]
    ring_down = [(j, i) for i, j in ring_up]
    above = lax.ppermute(second[C_DEV - REACH :], "chan", ring_up)
    below = lax.ppermute(second[:REACH], "chan", ring_down)
    second_wide = jnp.concatenate([above, second, below], axis=0)

    n_t = length - 6
    n_sel = quarter // 4 + 1
    third = banded(
        second_wide[None],
        third_weight,
        biases,
        48,
        third_mask[None],
        groups=1,
        shifts=7,
        n_out=n_t,
        relu=True,
        select=phase_select(),
        n_sel=n_sel,
    )
    features = banded(
        third,
        fourth_weight,
        biases,
        80,
        None,
        groups=1,
        shifts=2,
        n_out=quarter // 4,
        relu=True,
        rows_inner=True,
    )
    return features[0]


def solution(mesh):
    return jax.shard_map(
        on_device,
        mesh=mesh,
        in_specs=(
            P(("tm", "chan"), None),
            P(),
            P("chan"),
            P(),
            P(),
            P(),
            P(),
            P(),
            P(),
            P(),
            P(),
            P(),
        ),
        out_specs=P(None, "chan", "tm"),
        check_vma=False,
    )
```

```python
import numpy as np
import jax
import jax.numpy as jnp
from jax import lax
from jax.experimental import pallas as pl
from jax.sharding import PartitionSpec as P

F2 = 32
C_DEV = 8
REACH = 6
PH = 4
WL = 7
WR = 8
LEAD = 5
LANE_BLOCK = 256


def banded(x, w_all, bias, b_row, mask, *, groups, shifts, n_out, relu, select=None, n_sel=0, rows_inner=False):
    windows = x.shape[0]
    flat = x.ndim == 3
    k_all = w_all.shape[1]
    row_step = k_all // 7
    r_out = (x.shape[1] // row_step if flat else x.shape[1]) - 6
    n_in = x.shape[-1]
    fout = w_all.shape[0] // (groups * shifts)
    if rows_inner:
        out_shape = (windows, groups * fout, r_out, n_out)
    elif select is None:
        out_shape = (windows, r_out, groups * fout, n_out)
    else:
        out_shape = (windows, r_out, PH * fout, n_sel)

    def kernel(x_ref, w_ref, b_ref, *rest):
        if mask is None:
            m_ref, rest = None, rest
        else:
            m_ref, rest = rest[0], rest[1:]
        if select is None:
            (o_ref,) = rest
        else:
            s_ref, o_ref = rest
        b_val = b_ref[b_row : b_row + fout, :]

        def row(r, carry):
            if flat:
                xs = x_ref[r * row_step : r * row_step + k_all, :]
            else:
                xs = x_ref[r : r + 7, :, :].reshape(k_all, n_in)
            z = jnp.dot(w_ref[...], xs, preferred_element_type=jnp.float32)
            m_row = None if m_ref is None else m_ref[r]
            for g in range(groups):
                base = g * shifts * fout
                acc = z[base : base + fout, 0:n_out]
                for s in range(1, shifts):
                    acc = acc + z[base + s * fout : base + (s + 1) * fout, s : s + n_out]
                acc = acc + b_val
                if relu:
                    acc = jnp.maximum(acc, 0.0)
                if m_row is not None:
                    acc = acc * m_row[g : g + 1, :]
                acc = acc.astype(jnp.bfloat16)
                if rows_inner:
                    o_ref[g * fout : (g + 1) * fout, r : r + 1, :] = acc[:, None, :]
                    continue
                if select is None:
                    o_ref[r, g * fout : (g + 1) * fout, :] = acc
                    continue
                for k in range(pl.cdiv(n_out, LANE_BLOCK // 2)):
                    lo = k * (LANE_BLOCK // 2)
                    width = min(LANE_BLOCK // 2, n_out - lo)
                    n_u = pl.cdiv(width, PH)
                    y = jnp.dot(acc[:, lo : lo + width], s_ref[0:width, :], preferred_element_type=jnp.float32)
                    seg = LANE_BLOCK // 2 // PH
                    for p in range(PH):
                        o_ref[r, p * fout : (p + 1) * fout, lo // PH : lo // PH + n_u] = y[
                            :, p * seg : p * seg + n_u
                        ].astype(jnp.bfloat16)
            return carry

        for r in range(r_out):
            row(r, 0)

    def per_window(a):
        return pl.BlockSpec((None,) + a.shape[1:], lambda w, n=a.ndim - 1: (w,) + (0,) * n)

    def whole(a):
        return pl.BlockSpec(a.shape, lambda w, n=a.ndim: (0,) * n)

    args = [x, w_all, bias]
    specs = [per_window(x), whole(w_all), whole(bias)]
    if mask is not None:
        args.append(mask)
        specs.append(per_window(mask))
    if select is not None:
        args.append(select)
        specs.append(whole(select))
    return pl.pallas_call(
        kernel,
        grid=(windows,),
        in_specs=specs,
        out_specs=pl.BlockSpec((None,) + out_shape[1:], lambda w: (w, 0, 0, 0)),
        out_shape=jax.ShapeDtypeStruct(out_shape, jnp.bfloat16),
    )(*args)


def strain_layout(raw, left, right, rows):
    channels = raw.shape[1]
    cols = raw.shape[0] // PH
    n_out = WL + cols + WR

    def kernel(raw_ref, l_ref, r_ref, o_ref):
        ci = lax.broadcasted_iota(jnp.int32, (rows, channels), 1)
        ri = lax.broadcasted_iota(jnp.int32, (rows, channels), 0)
        nt = (((1,), (1,)), ((), ()))
        pieces = ((l_ref, 0, left.shape[0] // PH, left.shape[0] // PH - WL), (raw_ref, WL, cols, 0), (r_ref, WL + cols, WR, 0))
        for src, lo, n, skip in pieces:
            acc = None
            for q in range(PH):
                e = (ri == ci * PH + q + PH * (ci // (rows // (2 * PH) - 1))).astype(jnp.float32)
                piece = src[pl.ds(q, n, stride=PH), :].astype(jnp.float32)
                y = lax.dot_general(e, piece, nt, preferred_element_type=jnp.float32)
                acc = y if acc is None else acc + y
            o_ref[:, lo : lo + n - skip] = acc[:, skip:].astype(o_ref.dtype)

    return pl.pallas_call(kernel, out_shape=jax.ShapeDtypeStruct((rows, n_out), jnp.bfloat16))(raw, left, right)


def settled(arrays):
    n = len(arrays)

    def kernel(*refs):
        for src_ref, dst_ref in zip(refs[:n], refs[n:]):
            dst_ref[...] = src_ref[...]

    return pl.pallas_call(kernel, out_shape=tuple(jax.ShapeDtypeStruct(a.shape, a.dtype) for a in arrays))(*arrays)


def first_layer(x, w_all, bias, mask):
    windows, rows_in, n_in = x.shape
    n_out = n_in - 3
    r_out = rows_in // PH - 7
    fout = w_all.shape[0] // PH

    def kernel(x_ref, w_ref, b_ref, m_ref, o_ref):
        b_val = b_ref[0 : PH * fout, :]
        for r in range(r_out):
            base = x_ref[PH * r : PH * r + 8 * PH, :]
            xs = jnp.concatenate([base[:, d : d + n_out] for d in range(4)], axis=0)
            acc = jnp.dot(w_ref[...], xs, preferred_element_type=jnp.float32) + b_val
            acc = jnp.maximum(acc, 0.0)
            m_row = m_ref[r]
            for p in range(PH):
                o_ref[r, p * fout : (p + 1) * fout, :] = (acc[p * fout : (p + 1) * fout] * m_row[p : p + 1, :]).astype(
                    jnp.bfloat16
                )

    return pl.pallas_call(
        kernel,
        grid=(windows,),
        in_specs=[
            pl.BlockSpec((None, rows_in, n_in), lambda w: (w, 0, 0)),
            pl.BlockSpec(w_all.shape, lambda w: (0, 0)),
            pl.BlockSpec(bias.shape, lambda w: (0, 0)),
            pl.BlockSpec((None,) + mask.shape[1:], lambda w: (w, 0, 0, 0)),
        ],
        out_specs=pl.BlockSpec((None, r_out, PH * fout, n_out), lambda w: (w, 0, 0, 0)),
        out_shape=jax.ShapeDtypeStruct((windows, r_out, PH * fout, n_out), jnp.bfloat16),
    )(x, w_all, bias, mask)


def weights_stride1(w):
    fout, fin = w.shape[:2]
    return jnp.transpose(w, (3, 0, 2, 1)).reshape(7 * fout, 7 * fin)


def weights_stride4(w, shifts, lag):
    fout, fin = w.shape[:2]
    taps = jnp.pad(w, ((0, 0), (0, 0), (0, 0), (lag, shifts * PH - 7 - lag))).reshape(fout, fin, 7, shifts, PH)
    return jnp.transpose(taps, (3, 0, 2, 4, 1)).reshape(shifts * fout, 7 * PH * fin)


def weights_first(w):
    fout = w.shape[0]
    per_p = [jnp.pad(w[:, 0], ((0, 0), (0, 1), (p + 1, 8 - p))).reshape(fout, 8, 4, PH) for p in range(PH)]
    return jnp.transpose(jnp.stack(per_p), (0, 1, 3, 2, 4)).reshape(PH * fout, 4 * 8 * PH)


def phase_select():
    block = LANE_BLOCK // 2
    seg = block // PH
    sel = np.zeros((block, block), np.float32)
    for p in range(PH):
        for u in range(seg):
            sel[PH * u + p, p * seg + u] = 1.0
    return jnp.asarray(sel, jnp.bfloat16)


def edge_mask(rows, groups, length, row0, time_of, block):
    t = lax.axis_index("tm")
    total_rows = lax.axis_size("chan") * C_DEV
    last = lax.axis_size("tm") - 1
    shape = (rows, groups, length)
    row = block * C_DEV + row0 + lax.broadcasted_iota(jnp.int32, shape, 0)
    tau, span = time_of(lax.broadcasted_iota(jnp.int32, shape, 1), lax.broadcasted_iota(jnp.int32, shape, 2))
    ok = (row >= 0) & (row < total_rows)
    ok = ok & ((t > 0) | (tau >= 0)) & ((t < last) | (tau < span))
    return ok.astype(jnp.float32)


def lower_layers(strain_wide, first_mask, first_weight, biases, second_weight, length):
    wide = C_DEV + 2 * REACH
    n_win, n_s = strain_wide.shape[0], strain_wide.shape[-1]
    n_f = n_s - 3
    first = first_layer(strain_wide, first_weight, biases, first_mask)
    return banded(
        first,
        second_weight,
        biases,
        64,
        None,
        groups=1,
        shifts=3,
        n_out=length,
        relu=False,
    )


def on_device(
    recorded,
    partners,
    offsets,
    first_weight,
    first_bias,
    second_weight,
    second_bias,
    loop_weight,
    third_weight,
    third_bias,
    fourth_weight,
    fourth_bias,
):
    blocks = lax.axis_size("chan")
    me = lax.axis_index("chan")
    mate = partners[me]
    times_here, nc = recorded.shape
    wide = C_DEV + 2 * REACH
    padded = jnp.pad(recorded, ((0, 0), (REACH, 3 * C_DEV - REACH)))
    windows = jnp.concatenate(
        [padded[:, k * C_DEV : k * C_DEV + nc].reshape(times_here, blocks, C_DEV) for k in range(3)], axis=2
    )[:, :, :wide]
    tag = jnp.zeros((times_here, blocks, 1), recorded.dtype).at[0].set(offsets[0].astype(recorded.dtype))
    both = jnp.concatenate([windows, jnp.take(windows, partners, axis=1, mode="clip"), tag], axis=2)
    outgoing = jnp.transpose(both, (1, 0, 2))
    arrived = lax.all_to_all(outgoing, "chan", split_axis=0, concat_axis=0, tiled=True)
    biases = jnp.concatenate([jnp.tile(first_bias, PH), second_bias, third_bias, fourth_bias]).reshape(-1, 1)
    prepared = (
        weights_first(first_weight),
        weights_stride4(second_weight, 3, 2),
        weights_stride1(third_weight),
        weights_stride4(fourth_weight, 2, 0),
        biases,
    )
    quarter = blocks * times_here // 4
    length = quarter + 2 * LEAD
    n_t = length - 6
    n_f = WL + blocks * times_here // PH + WR - 3
    first_time = lambda p, v: (PH * (v - (WL - 1)) + p, blocks * times_here)
    masks = (
        jnp.stack([edge_mask(wide - 6, PH, n_f, 3 - REACH, first_time, b) for b in (me, mate)]),
        edge_mask(C_DEV, 1, length, 0, lambda p, j: (j - LEAD, quarter), me),
        edge_mask(wide - 6, 1, n_t, 3 - REACH, lambda p, j: (j - (LEAD - 3), quarter), me),
    )
    prepared = settled(prepared)
    arrived, prepared, masks = lax.optimization_barrier((arrived, prepared, masks))
    first_weight, second_weight, third_weight, fourth_weight, biases = prepared
    first_mask, second_mask, third_mask = masks
    mate_offset = arrived[:, 0, 2 * wide].astype(jnp.int32)[mate]
    times = blocks * times_here
    tms = lax.axis_size("tm")
    up = [(i, i + 1) for i in range(tms - 1)]
    down = [(j, i) for i, j in up]
    before = lax.ppermute(arrived[blocks - 1], "tm", up)
    after = lax.ppermute(arrived[0, : PH * WR], "tm", down)
    strain_wide = strain_layout(arrived.reshape(times, -1), before, after, 2 * (wide + 1) * PH)

    quarter = times // 4
    length = quarter + 2 * LEAD
    lower = lower_layers(
        strain_wide.reshape(2, (wide + 1) * PH, -1), first_mask, first_weight, biases, second_weight, length
    )
    pre_second, mate_second = lower[0], lower[1]

    own_offset = offsets[0]
    crossing = lax.dynamic_slice(mate_second, (mate_offset - 3, 0, 0), (7, F2, length))
    flipped = crossing[::-1]
    coupling = jnp.einsum("kof,kft->kot", loop_weight, flipped, preferred_element_type=jnp.float32)
    extra = lax.dynamic_update_slice(
        jnp.zeros((C_DEV, F2, length), jnp.float32), coupling, (own_offset - 3, 0, 0)
    )
    second = (jnp.maximum(pre_second.astype(jnp.float32) + extra, 0.0) * second_mask).astype(jnp.bfloat16)

    ring_up = [(i, i + 1) for i in range(blocks - 1)]
    ring_down = [(j, i) for i, j in ring_up]
    above = lax.ppermute(second[C_DEV - REACH :], "chan", ring_up)
    below = lax.ppermute(second[:REACH], "chan", ring_down)
    second_wide = jnp.concatenate([above, second, below], axis=0)

    n_t = length - 6
    n_sel = quarter // 4 + 1
    third = banded(
        second_wide[None],
        third_weight,
        biases,
        96,
        third_mask[None],
        groups=1,
        shifts=7,
        n_out=n_t,
        relu=True,
        select=phase_select(),
        n_sel=n_sel,
    )
    features = banded(
        third,
        fourth_weight,
        biases,
        128,
        None,
        groups=1,
        shifts=2,
        n_out=quarter // 4,
        relu=True,
        rows_inner=True,
    )
    return features[0]


def solution(mesh):
    return jax.shard_map(
        on_device,
        mesh=mesh,
        in_specs=(
            P(("tm", "chan"), None),
            P(),
            P("chan"),
            P(),
            P(),
            P(),
            P(),
            P(),
            P(),
            P(),
            P(),
            P(),
        ),
        out_specs=P(None, "chan", "tm"),
        check_vma=False,
    )
```

```python
import numpy as np
import jax
import jax.numpy as jnp
from jax import lax
from jax.experimental import pallas as pl
from jax.sharding import PartitionSpec as P

F2 = 32
C_DEV = 8
REACH = 6
PH = 4
WL = 7
WR = 8
LEAD = 5
LANE_BLOCK = 256
WIN_ROWS = (C_DEV + 2 * REACH) * PH
WIN_PAD = 96


def banded(x, w_all, bias, b_row, mask, *, groups, shifts, n_out, relu, select=None, n_sel=0, rows_inner=False):
    windows = x.shape[0]
    flat = x.ndim == 3
    k_all = w_all.shape[1]
    row_step = k_all // 7
    r_out = (x.shape[1] // row_step if flat else x.shape[1]) - 6
    n_in = x.shape[-1]
    fout = w_all.shape[0] // (groups * shifts)
    if rows_inner:
        out_shape = (windows, groups * fout, r_out, n_out)
    elif select is None:
        out_shape = (windows, r_out, groups * fout, n_out)
    else:
        out_shape = (windows, r_out, PH * fout, n_sel)

    def kernel(x_ref, w_ref, b_ref, *rest):
        if mask is None:
            m_ref, rest = None, rest
        else:
            m_ref, rest = rest[0], rest[1:]
        if select is None:
            (o_ref,) = rest
        else:
            s_ref, o_ref = rest
        b_val = b_ref[b_row : b_row + fout, :]

        def row(r, carry):
            if flat:
                xs = x_ref[r * row_step : r * row_step + k_all, :]
            else:
                xs = x_ref[r : r + 7, :, :].reshape(k_all, n_in)
            z = jnp.dot(w_ref[...], xs, preferred_element_type=jnp.float32)
            m_row = None if m_ref is None else m_ref[r]
            for g in range(groups):
                base = g * shifts * fout
                acc = z[base : base + fout, 0:n_out]
                for s in range(1, shifts):
                    acc = acc + z[base + s * fout : base + (s + 1) * fout, s : s + n_out]
                acc = acc + b_val
                if relu:
                    acc = jnp.maximum(acc, 0.0)
                if m_row is not None:
                    acc = acc * m_row[g : g + 1, :]
                acc = acc.astype(jnp.bfloat16)
                if rows_inner:
                    o_ref[g * fout : (g + 1) * fout, r : r + 1, :] = acc[:, None, :]
                    continue
                if select is None:
                    o_ref[r, g * fout : (g + 1) * fout, :] = acc
                    continue
                for k in range(pl.cdiv(n_out, LANE_BLOCK // 2)):
                    lo = k * (LANE_BLOCK // 2)
                    width = min(LANE_BLOCK // 2, n_out - lo)
                    n_u = pl.cdiv(width, PH)
                    y = jnp.dot(acc[:, lo : lo + width], s_ref[0:width, :], preferred_element_type=jnp.float32)
                    seg = LANE_BLOCK // 2 // PH
                    for p in range(PH):
                        o_ref[r, p * fout : (p + 1) * fout, lo // PH : lo // PH + n_u] = y[
                            :, p * seg : p * seg + n_u
                        ].astype(jnp.bfloat16)
            return carry

        for r in range(r_out):
            row(r, 0)

    def per_window(a):
        return pl.BlockSpec((None,) + a.shape[1:], lambda w, n=a.ndim - 1: (w,) + (0,) * n)

    def whole(a):
        return pl.BlockSpec(a.shape, lambda w, n=a.ndim: (0,) * n)

    args = [x, w_all, bias]
    specs = [per_window(x), whole(w_all), whole(bias)]
    if mask is not None:
        args.append(mask)
        specs.append(per_window(mask))
    if select is not None:
        args.append(select)
        specs.append(whole(select))
    return pl.pallas_call(
        kernel,
        grid=(windows,),
        in_specs=specs,
        out_specs=pl.BlockSpec((None,) + out_shape[1:], lambda w: (w, 0, 0, 0)),
        out_shape=jax.ShapeDtypeStruct(out_shape, jnp.bfloat16),
    )(*args)


def strain_layout(raw, left, right, rows):
    channels = raw.shape[1]
    cols = raw.shape[0] // PH
    n_out = WL + cols + WR

    def kernel(raw_ref, l_ref, r_ref, o_ref):
        ci = lax.broadcasted_iota(jnp.int32, (rows, channels), 1)
        ri = lax.broadcasted_iota(jnp.int32, (rows, channels), 0)
        nt = (((1,), (1,)), ((), ()))
        pieces = ((l_ref, 0, left.shape[0] // PH, left.shape[0] // PH - WL), (raw_ref, WL, cols, 0), (r_ref, WL + cols, WR, 0))
        for src, lo, n, skip in pieces:
            acc = None
            for q in range(PH):
                e = (ri == ci * PH + q + (rows // 2 - WIN_ROWS) * (ci // (WIN_ROWS // PH))).astype(jnp.float32)
                piece = src[pl.ds(q, n, stride=PH), :].astype(jnp.float32)
                y = lax.dot_general(e, piece, nt, preferred_element_type=jnp.float32)
                acc = y if acc is None else acc + y
            o_ref[:, lo : lo + n - skip] = acc[:, skip:].astype(o_ref.dtype)

    return pl.pallas_call(kernel, out_shape=jax.ShapeDtypeStruct((rows, n_out), jnp.bfloat16))(raw, left, right)


def settled(arrays):
    n = len(arrays)

    def kernel(*refs):
        for src_ref, dst_ref in zip(refs[:n], refs[n:]):
            dst_ref[...] = src_ref[...]

    return pl.pallas_call(kernel, out_shape=tuple(jax.ShapeDtypeStruct(a.shape, a.dtype) for a in arrays))(*arrays)


def first_layer(x, w_all, bias, mask):
    windows, rows_in, n_in = x.shape
    n_out = n_in - 3
    r_out = WIN_ROWS // PH - 6
    fout = w_all.shape[0] // PH

    def kernel(x_ref, w_ref, b_ref, m_ref, o_ref):
        b_val = b_ref[0 : PH * fout, :]
        for r in range(r_out):
            base = x_ref[PH * r : PH * r + 8 * PH, :]
            xs = jnp.concatenate([base[:, d : d + n_out] for d in range(4)], axis=0)
            acc = jnp.dot(w_ref[...], xs, preferred_element_type=jnp.float32) + b_val
            acc = jnp.maximum(acc, 0.0)
            m_row = m_ref[r]
            for p in range(PH):
                o_ref[r, p * fout : (p + 1) * fout, :] = (acc[p * fout : (p + 1) * fout] * m_row[p : p + 1, :]).astype(
                    jnp.bfloat16
                )

    return pl.pallas_call(
        kernel,
        grid=(windows,),
        in_specs=[
            pl.BlockSpec((None, rows_in, n_in), lambda w: (w, 0, 0)),
            pl.BlockSpec(w_all.shape, lambda w: (0, 0)),
            pl.BlockSpec(bias.shape, lambda w: (0, 0)),
            pl.BlockSpec((None,) + mask.shape[1:], lambda w: (w, 0, 0, 0)),
        ],
        out_specs=pl.BlockSpec((None, r_out, PH * fout, n_out), lambda w: (w, 0, 0, 0)),
        out_shape=jax.ShapeDtypeStruct((windows, r_out, PH * fout, n_out), jnp.bfloat16),
    )(x, w_all, bias, mask)


def weights_stride1(w):
    fout, fin = w.shape[:2]
    return jnp.transpose(w, (3, 0, 2, 1)).reshape(7 * fout, 7 * fin)


def weights_stride4(w, shifts, lag):
    fout, fin = w.shape[:2]
    taps = jnp.pad(w, ((0, 0), (0, 0), (0, 0), (lag, shifts * PH - 7 - lag))).reshape(fout, fin, 7, shifts, PH)
    return jnp.transpose(taps, (3, 0, 2, 4, 1)).reshape(shifts * fout, 7 * PH * fin)


def weights_first(w):
    fout = w.shape[0]
    per_p = [jnp.pad(w[:, 0], ((0, 0), (0, 1), (p + 1, 8 - p))).reshape(fout, 8, 4, PH) for p in range(PH)]
    return jnp.transpose(jnp.stack(per_p), (0, 1, 3, 2, 4)).reshape(PH * fout, 4 * 8 * PH)


def phase_select():
    block = LANE_BLOCK // 2
    seg = block // PH
    sel = np.zeros((block, block), np.float32)
    for p in range(PH):
        for u in range(seg):
            sel[PH * u + p, p * seg + u] = 1.0
    return jnp.asarray(sel, jnp.bfloat16)


def edge_mask(rows, groups, length, row0, time_of, block):
    t = lax.axis_index("tm")
    total_rows = lax.axis_size("chan") * C_DEV
    last = lax.axis_size("tm") - 1
    shape = (rows, groups, length)
    row = block * C_DEV + row0 + lax.broadcasted_iota(jnp.int32, shape, 0)
    tau, span = time_of(lax.broadcasted_iota(jnp.int32, shape, 1), lax.broadcasted_iota(jnp.int32, shape, 2))
    ok = (row >= 0) & (row < total_rows)
    ok = ok & ((t > 0) | (tau >= 0)) & ((t < last) | (tau < span))
    return ok.astype(jnp.float32)


def lower_layers(strain_wide, first_mask, first_weight, biases, second_weight, length):
    wide = C_DEV + 2 * REACH
    n_win, n_s = strain_wide.shape[0], strain_wide.shape[-1]
    n_f = n_s - 3
    first = first_layer(strain_wide, first_weight, biases, first_mask)
    return banded(
        first,
        second_weight,
        biases,
        64,
        None,
        groups=1,
        shifts=3,
        n_out=length,
        relu=False,
    )


def on_device(
    recorded,
    partners,
    offsets,
    first_weight,
    first_bias,
    second_weight,
    second_bias,
    loop_weight,
    third_weight,
    third_bias,
    fourth_weight,
    fourth_bias,
):
    blocks = lax.axis_size("chan")
    me = lax.axis_index("chan")
    mate = partners[me]
    times_here, nc = recorded.shape
    wide = C_DEV + 2 * REACH
    padded = jnp.pad(recorded, ((0, 0), (REACH, 3 * C_DEV - REACH)))
    windows = jnp.concatenate(
        [padded[:, k * C_DEV : k * C_DEV + nc].reshape(times_here, blocks, C_DEV) for k in range(3)], axis=2
    )[:, :, :wide]
    tag = jnp.zeros((times_here, blocks, 1), recorded.dtype).at[0].set(offsets[0].astype(recorded.dtype))
    both = jnp.concatenate([windows, jnp.take(windows, partners, axis=1, mode="clip"), tag], axis=2)
    outgoing = jnp.transpose(both, (1, 0, 2))
    arrived = lax.all_to_all(outgoing, "chan", split_axis=0, concat_axis=0, tiled=True)
    biases = jnp.concatenate([jnp.tile(first_bias, PH), second_bias, third_bias, fourth_bias]).reshape(-1, 1)
    prepared = (
        weights_first(first_weight),
        weights_stride4(second_weight, 3, 2),
        weights_stride1(third_weight),
        weights_stride4(fourth_weight, 2, 0),
        biases,
    )
    quarter = blocks * times_here // 4
    length = quarter + 2 * LEAD
    n_t = length - 6
    n_f = WL + blocks * times_here // PH + WR - 3
    first_time = lambda p, v: (PH * (v - (WL - 1)) + p, blocks * times_here)
    masks = (
        jnp.stack([edge_mask(wide - 6, PH, n_f, 3 - REACH, first_time, b) for b in (me, mate)]),
        edge_mask(C_DEV, 1, length, 0, lambda p, j: (j - LEAD, quarter), me),
        edge_mask(wide - 6, 1, n_t, 3 - REACH, lambda p, j: (j - (LEAD - 3), quarter), me),
    )
    prepared = settled(prepared)
    arrived, prepared, masks = lax.optimization_barrier((arrived, prepared, masks))
    first_weight, second_weight, third_weight, fourth_weight, biases = prepared
    first_mask, second_mask, third_mask = masks
    mate_offset = arrived[:, 0, 2 * wide].astype(jnp.int32)[mate]
    times = blocks * times_here
    tms = lax.axis_size("tm")
    up = [(i, i + 1) for i in range(tms - 1)]
    down = [(j, i) for i, j in up]
    before = lax.ppermute(arrived[blocks - 1], "tm", up)
    after = lax.ppermute(arrived[0, : PH * WR], "tm", down)
    strain_wide = strain_layout(arrived.reshape(times, -1), before, after, 2 * WIN_PAD)

    quarter = times // 4
    length = quarter + 2 * LEAD
    lower = lower_layers(
        strain_wide.reshape(2, WIN_PAD, -1), first_mask, first_weight, biases, second_weight, length
    )
    pre_second, mate_second = lower[0], lower[1]

    own_offset = offsets[0]
    crossing = lax.dynamic_slice(mate_second, (mate_offset - 3, 0, 0), (7, F2, length))
    flipped = crossing[::-1]
    coupling = jnp.einsum("kof,kft->kot", loop_weight, flipped, preferred_element_type=jnp.float32)
    extra = lax.dynamic_update_slice(
        jnp.zeros((C_DEV, F2, length), jnp.float32), coupling, (own_offset - 3, 0, 0)
    )
    second = (jnp.maximum(pre_second.astype(jnp.float32) + extra, 0.0) * second_mask).astype(jnp.bfloat16)

    ring_up = [(i, i + 1) for i in range(blocks - 1)]
    ring_down = [(j, i) for i, j in ring_up]
    above = lax.ppermute(second[C_DEV - REACH :], "chan", ring_up)
    below = lax.ppermute(second[:REACH], "chan", ring_down)
    second_wide = jnp.concatenate([above, second, below], axis=0)

    n_t = length - 6
    n_sel = quarter // 4 + 1
    third = banded(
        second_wide[None],
        third_weight,
        biases,
        96,
        third_mask[None],
        groups=1,
        shifts=7,
        n_out=n_t,
        relu=True,
        select=phase_select(),
        n_sel=n_sel,
    )
    features = banded(
        third,
        fourth_weight,
        biases,
        128,
        None,
        groups=1,
        shifts=2,
        n_out=quarter // 4,
        relu=True,
        rows_inner=True,
    )
    return features[0]


def solution(mesh):
    return jax.shard_map(
        on_device,
        mesh=mesh,
        in_specs=(
            P(("tm", "chan"), None),
            P(),
            P("chan"),
            P(),
            P(),
            P(),
            P(),
            P(),
            P(),
            P(),
            P(),
            P(),
        ),
        out_specs=P(None, "chan", "tm"),
        check_vma=False,
    )
```

```python
import numpy as np
import jax
import jax.numpy as jnp
from jax import lax
from jax.experimental import pallas as pl
from jax.sharding import PartitionSpec as P

F2 = 32
C_DEV = 8
REACH = 6
PH = 4
WL = 7
WR = 8
LEAD = 5
LANE_BLOCK = 256
WIN_ROWS = (C_DEV + 2 * REACH) * PH
WIN_PAD = 96


def banded(x, w_all, bias, b_row, mask, *, groups, shifts, n_out, relu, select=None, n_sel=0, rows_inner=False):
    windows = x.shape[0]
    flat = x.ndim == 3
    k_all = w_all.shape[1]
    row_step = k_all // 7
    r_out = (x.shape[1] // row_step if flat else x.shape[1]) - 6
    n_in = x.shape[-1]
    fout = w_all.shape[0] // (groups * shifts)
    if rows_inner:
        out_shape = (windows, groups * fout, r_out, n_out)
    elif select is None:
        out_shape = (windows, r_out, groups * fout, n_out)
    else:
        out_shape = (windows, r_out, PH * fout, n_sel)

    def kernel(x_ref, w_ref, b_ref, *rest):
        if mask is None:
            m_ref, rest = None, rest
        else:
            m_ref, rest = rest[0], rest[1:]
        if select is None:
            (o_ref,) = rest
        else:
            s_ref, o_ref = rest
        b_val = b_ref[b_row : b_row + fout, :]

        def row(r, carry):
            if flat:
                xs = x_ref[r * row_step : r * row_step + k_all, :]
            else:
                xs = x_ref[r : r + 7, :, :].reshape(k_all, n_in)
            z = jnp.dot(w_ref[...], xs, preferred_element_type=jnp.float32)
            m_row = None if m_ref is None else m_ref[r]
            for g in range(groups):
                base = g * shifts * fout
                acc = z[base : base + fout, 0:n_out]
                for s in range(1, shifts):
                    acc = acc + z[base + s * fout : base + (s + 1) * fout, s : s + n_out]
                acc = acc + b_val
                if relu:
                    acc = jnp.maximum(acc, 0.0)
                if m_row is not None:
                    acc = acc * m_row[g : g + 1, :]
                acc = acc.astype(jnp.bfloat16)
                if rows_inner:
                    o_ref[g * fout : (g + 1) * fout, r : r + 1, :] = acc[:, None, :]
                    continue
                if select is None:
                    o_ref[r, g * fout : (g + 1) * fout, :] = acc
                    continue
                for k in range(pl.cdiv(n_out, LANE_BLOCK // 2)):
                    lo = k * (LANE_BLOCK // 2)
                    width = min(LANE_BLOCK // 2, n_out - lo)
                    n_u = pl.cdiv(width, PH)
                    y = jnp.dot(acc[:, lo : lo + width], s_ref[0:width, :], preferred_element_type=jnp.float32)
                    seg = LANE_BLOCK // 2 // PH
                    for p in range(PH):
                        o_ref[r, p * fout : (p + 1) * fout, lo // PH : lo // PH + n_u] = y[
                            :, p * seg : p * seg + n_u
                        ].astype(jnp.bfloat16)
            return carry

        for r in range(r_out):
            row(r, 0)

    def per_window(a):
        return pl.BlockSpec((None,) + a.shape[1:], lambda w, n=a.ndim - 1: (w,) + (0,) * n)

    def whole(a):
        return pl.BlockSpec(a.shape, lambda w, n=a.ndim: (0,) * n)

    args = [x, w_all, bias]
    specs = [per_window(x), whole(w_all), whole(bias)]
    if mask is not None:
        args.append(mask)
        specs.append(per_window(mask))
    if select is not None:
        args.append(select)
        specs.append(whole(select))
    return pl.pallas_call(
        kernel,
        grid=(windows,),
        in_specs=specs,
        out_specs=pl.BlockSpec((None,) + out_shape[1:], lambda w: (w, 0, 0, 0)),
        out_shape=jax.ShapeDtypeStruct(out_shape, jnp.bfloat16),
    )(*args)


def strain_layout(raw, left, right, rows):
    channels = raw.shape[1]
    cols = raw.shape[0] // PH
    n_out = WL + cols + WR

    def kernel(raw_ref, l_ref, r_ref, o_ref):
        ci = lax.broadcasted_iota(jnp.int32, (rows, channels), 1)
        ri = lax.broadcasted_iota(jnp.int32, (rows, channels), 0)
        nt = (((1,), (1,)), ((), ()))
        pieces = ((l_ref, 0, left.shape[0] // PH, left.shape[0] // PH - WL), (raw_ref, WL, cols, 0), (r_ref, WL + cols, WR, 0))
        for src, lo, n, skip in pieces:
            acc = None
            for q in range(PH):
                e = (ri == ci * PH + q + (rows // 2 - WIN_ROWS) * (ci // (WIN_ROWS // PH))).astype(jnp.float32)
                piece = src[pl.ds(q, n, stride=PH), :].astype(jnp.float32)
                y = lax.dot_general(e, piece, nt, preferred_element_type=jnp.float32)
                acc = y if acc is None else acc + y
            o_ref[:, lo : lo + n - skip] = acc[:, skip:].astype(o_ref.dtype)

    return pl.pallas_call(kernel, out_shape=jax.ShapeDtypeStruct((rows, n_out), jnp.bfloat16))(raw, left, right)


def settled(arrays):
    n = len(arrays)

    def kernel(*refs):
        for src_ref, dst_ref in zip(refs[:n], refs[n:]):
            dst_ref[...] = src_ref[...]

    return pl.pallas_call(kernel, out_shape=tuple(jax.ShapeDtypeStruct(a.shape, a.dtype) for a in arrays))(*arrays)


def first_layer(x, w_all, bias, mask):
    windows, rows_in, n_in = x.shape
    n_out = n_in - 3
    r_out = WIN_ROWS // PH - 6
    fout = w_all.shape[0] // PH

    def kernel(x_ref, w_ref, b_ref, m_ref, o_ref):
        b_val = b_ref[0 : PH * fout, :]
        for r in range(r_out):
            base = x_ref[PH * r : PH * r + 8 * PH, :]
            xs = jnp.concatenate([base[:, d : d + n_out] for d in range(4)], axis=0)
            acc = jnp.dot(w_ref[...], xs, preferred_element_type=jnp.float32) + b_val
            acc = jnp.maximum(acc, 0.0)
            m_row = m_ref[r]
            for p in range(PH):
                o_ref[r, p * fout : (p + 1) * fout, :] = (acc[p * fout : (p + 1) * fout] * m_row[p : p + 1, :]).astype(
                    jnp.bfloat16
                )

    return pl.pallas_call(
        kernel,
        grid=(windows,),
        in_specs=[
            pl.BlockSpec((None, rows_in, n_in), lambda w: (w, 0, 0)),
            pl.BlockSpec(w_all.shape, lambda w: (0, 0)),
            pl.BlockSpec(bias.shape, lambda w: (0, 0)),
            pl.BlockSpec((None,) + mask.shape[1:], lambda w: (w, 0, 0, 0)),
        ],
        out_specs=pl.BlockSpec((None, r_out, PH * fout, n_out), lambda w: (w, 0, 0, 0)),
        out_shape=jax.ShapeDtypeStruct((windows, r_out, PH * fout, n_out), jnp.bfloat16),
    )(x, w_all, bias, mask)


def weights_stride1(w):
    fout, fin = w.shape[:2]
    return jnp.transpose(w, (3, 0, 2, 1)).reshape(7 * fout, 7 * fin)


def weights_stride4(w, shifts, lag):
    fout, fin = w.shape[:2]
    taps = jnp.pad(w, ((0, 0), (0, 0), (0, 0), (lag, shifts * PH - 7 - lag))).reshape(fout, fin, 7, shifts, PH)
    return jnp.transpose(taps, (3, 0, 2, 4, 1)).reshape(shifts * fout, 7 * PH * fin)


def weights_first(w):
    fout = w.shape[0]
    per_p = [jnp.pad(w[:, 0], ((0, 0), (0, 1), (p + 1, 8 - p))).reshape(fout, 8, 4, PH) for p in range(PH)]
    return jnp.transpose(jnp.stack(per_p), (0, 1, 3, 2, 4)).reshape(PH * fout, 4 * 8 * PH)


def phase_select():
    block = LANE_BLOCK // 2
    seg = block // PH
    sel = np.zeros((block, block), np.float32)
    for p in range(PH):
        for u in range(seg):
            sel[PH * u + p, p * seg + u] = 1.0
    return jnp.asarray(sel, jnp.bfloat16)


def edge_mask(rows, groups, length, row0, time_of, block):
    t = lax.axis_index("tm")
    total_rows = lax.axis_size("chan") * C_DEV
    last = lax.axis_size("tm") - 1
    shape = (rows, groups, length)
    row = block * C_DEV + row0 + lax.broadcasted_iota(jnp.int32, shape, 0)
    tau, span = time_of(lax.broadcasted_iota(jnp.int32, shape, 1), lax.broadcasted_iota(jnp.int32, shape, 2))
    ok = (row >= 0) & (row < total_rows)
    ok = ok & ((t > 0) | (tau >= 0)) & ((t < last) | (tau < span))
    return ok.astype(jnp.float32)


def lower_layers(strain_wide, first_mask, first_weight, biases, second_weight, length):
    wide = C_DEV + 2 * REACH
    n_win, n_s = strain_wide.shape[0], strain_wide.shape[-1]
    n_f = n_s - 3
    first = first_layer(strain_wide, first_weight, biases, first_mask)
    return banded(
        first,
        second_weight,
        biases,
        64,
        None,
        groups=1,
        shifts=3,
        n_out=length,
        relu=False,
    )


def on_device(
    recorded,
    partners,
    offsets,
    first_weight,
    first_bias,
    second_weight,
    second_bias,
    loop_weight,
    third_weight,
    third_bias,
    fourth_weight,
    fourth_bias,
):
    blocks = lax.axis_size("chan")
    me = lax.axis_index("chan")
    mate = partners[me]
    times_here, nc = recorded.shape
    wide = C_DEV + 2 * REACH
    padded = jnp.pad(recorded, ((0, 0), (REACH, 3 * C_DEV - REACH)))
    windows = jnp.concatenate(
        [padded[:, k * C_DEV : k * C_DEV + nc].reshape(times_here, blocks, C_DEV) for k in range(3)], axis=2
    )[:, :, :wide]
    tag = jnp.zeros((times_here, blocks, 1), recorded.dtype).at[0].set(offsets[0].astype(recorded.dtype))
    both = jnp.concatenate([windows, jnp.take(windows, partners, axis=1, mode="clip"), tag], axis=2)
    outgoing = jnp.transpose(both, (1, 0, 2))
    arrived = lax.all_to_all(outgoing, "chan", split_axis=0, concat_axis=0, tiled=True)
    biases = jnp.concatenate([jnp.tile(first_bias, PH), second_bias, third_bias, fourth_bias]).reshape(-1, 1)
    prepared = (
        weights_first(first_weight),
        weights_stride4(second_weight, 3, 2),
        weights_stride1(third_weight),
        weights_stride4(fourth_weight, 2, 0),
        biases,
    )
    quarter = blocks * times_here // 4
    length = quarter + 2 * LEAD
    n_t = length - 6
    n_f = WL + blocks * times_here // PH + WR - 3
    first_time = lambda p, v: (PH * (v - (WL - 1)) + p, blocks * times_here)
    masks = (
        jnp.stack([edge_mask(wide - 6, PH, n_f, 3 - REACH, first_time, b) for b in (me, mate)]),
        edge_mask(C_DEV, 1, length, 0, lambda p, j: (j - LEAD, quarter), me),
        edge_mask(wide - 6, 1, n_t, 3 - REACH, lambda p, j: (j - (LEAD - 3), quarter), me),
    )
    prepared = settled(prepared)
    arrived, prepared, masks = lax.optimization_barrier((arrived, prepared, masks))
    first_weight, second_weight, third_weight, fourth_weight, biases = prepared
    first_mask, second_mask, third_mask = masks
    mate_offset = arrived[:, 0, 2 * wide].astype(jnp.int32)[mate]
    times = blocks * times_here
    tms = lax.axis_size("tm")
    up = [(i, i + 1) for i in range(tms - 1)]
    down = [(j, i) for i, j in up]
    after = lax.ppermute(arrived[0, : PH * WR], "tm", down)
    before = lax.ppermute(arrived[blocks - 1], "tm", up)
    strain_wide = strain_layout(arrived.reshape(times, -1), before, after, 2 * WIN_PAD)

    quarter = times // 4
    length = quarter + 2 * LEAD
    lower = lower_layers(
        strain_wide.reshape(2, WIN_PAD, -1), first_mask, first_weight, biases, second_weight, length
    )
    pre_second, mate_second = lower[0], lower[1]

    own_offset = offsets[0]
    crossing = lax.dynamic_slice(mate_second, (mate_offset - 3, 0, 0), (7, F2, length))
    flipped = crossing[::-1]
    coupling = jnp.einsum("kof,kft->kot", loop_weight, flipped, preferred_element_type=jnp.float32)
    extra = lax.dynamic_update_slice(
        jnp.zeros((C_DEV, F2, length), jnp.float32), coupling, (own_offset - 3, 0, 0)
    )
    second = (jnp.maximum(pre_second.astype(jnp.float32) + extra, 0.0) * second_mask).astype(jnp.bfloat16)

    ring_up = [(i, i + 1) for i in range(blocks - 1)]
    ring_down = [(j, i) for i, j in ring_up]
    above = lax.ppermute(second[C_DEV - REACH :], "chan", ring_up)
    below = lax.ppermute(second[:REACH], "chan", ring_down)
    second_wide = jnp.concatenate([above, second, below], axis=0)

    n_t = length - 6
    n_sel = quarter // 4 + 1
    third = banded(
        second_wide[None],
        third_weight,
        biases,
        96,
        third_mask[None],
        groups=1,
        shifts=7,
        n_out=n_t,
        relu=True,
        select=phase_select(),
        n_sel=n_sel,
    )
    features = banded(
        third,
        fourth_weight,
        biases,
        128,
        None,
        groups=1,
        shifts=2,
        n_out=quarter // 4,
        relu=True,
        rows_inner=True,
    )
    return features[0]


def solution(mesh):
    return jax.shard_map(
        on_device,
        mesh=mesh,
        in_specs=(
            P(("tm", "chan"), None),
            P(),
            P("chan"),
            P(),
            P(),
            P(),
            P(),
            P(),
            P(),
            P(),
            P(),
            P(),
        ),
        out_specs=P(None, "chan", "tm"),
        check_vma=False,
    )
```
